128 devices in a mesh: serve: 8 (over x, core), store: 16 (over z, y).
Axes of the slice: x: 4, y: 4, z: 4, core: 2. Of those that a mesh axis runs over, the one named last changes fastest.
Arguments:
- normalized_hidden_states: bfloat16 [65536, 2048], P(('serve', 'store')), may hold values from -20 to 20
- query_weight_matrix: bfloat16 [2048, 2048], replicated, may hold values from -0.125 to 0.125
- key_weight_matrix: bfloat16 [2048, 512], replicated, may hold values from -0.125 to 0.125
- value_weight_matrix: bfloat16 [2048, 512], replicated, may hold values from -0.125 to 0.125
- adapter_down_weight: bfloat16 [512, 32, 2048], P('store', None, 'serve'), may hold values from -0.125 to 0.125
- adapter_up_query_weight: bfloat16 [512, 16, 2048], P('store', None, 'serve'), may hold values from -1.5 to 1.5
- adapter_up_value_weight: bfloat16 [512, 16, 512], P('store', None, 'serve'), may hold values from -1.5 to 1.5
- adapter_panel_slot: int32 [512], replicated, may hold values from 0 to 511, as said below
- adapter_per_request: int32 [128, 16], P(('serve', 'store')), may hold values from 0 to 511, as said below
- request_token_length: int32 [128, 16], P(('serve', 'store')), may hold values from 1 to 64, 512 in all within a row
Outputs:
- attended: bfloat16 [65536, 2048], P(('serve', 'store'))
The draws below stay inside these ranges and needn't reach their ends.
Inputs may be any that keep to these rules, and one draw needn't show every extreme that they name: Each number appears once; adapter a's panels are entry adapter_panel_slot[a] of the three panel arrays, whose owner is index adapter_panel_slot[a] // 32 of store. `adapter_per_request`: the 16 requests of one device use adapters of 16 different owners. `request_token_length`: each row sums to 512; the longest request of each device has exactly 64 tokens.
All inputs are finite; a program needn't handle non-finite values.
Results may differ from the reference program's by a relative error of at most 0.012.
Values may be sent and summed in bfloat16 or wider, within the bound.
No kernel may reach another device: no remote copies, remote signals or barrier semaphores. Data moves between devices by JAX's collectives and lax.ppermute only.
A program may use at most 128 MiB of HBM per device.

```python
import math
import jax
import jax.numpy as jnp
import numpy as np
from jax import lax

MODEL_WIDTH = 2048
HEADS = 32
KV_HEADS = 8
HEAD_DIM = 64
ADAPTER_RANK = 16
ADP_DEV = 32
TOK_DEV = 512
KEY_VALUE_WIDTH = 512
LEN_MAX = 64
REQ_DEV = 16
ADAPTER_TOTAL = 512
TOKENS = 65536
N_SERVE = 8
N_STORE = 16


def shared_layout(key):
    return jax.random.permutation(jax.random.fold_in(key, 7), ADAPTER_TOTAL).astype(jnp.int32)


def draw_adapter_panel_slot(key, part):
    return shared_layout(key)


def draw_adapter_per_request(key, part):
    shuffled = shared_layout(key)
    inverse = jnp.argsort(shuffled, stable=True).astype(jnp.int32)
    row_count = N_SERVE * N_STORE
    scores = jax.random.randint(jax.random.fold_in(key, 13), (row_count, REQ_DEV), 0, 1 << 20) * REQ_DEV + jnp.arange(REQ_DEV, dtype=jnp.int32)[None, :]
    owners = jnp.argsort(scores, axis=1, stable=True).astype(jnp.int32)
    first_pick = jax.random.randint(jax.random.fold_in(key, 17), (row_count, REQ_DEV), 0, ADP_DEV)
    second_pick = jax.random.randint(jax.random.fold_in(key, 19), (row_count, REQ_DEV), 0, ADP_DEV)
    popular = jnp.minimum(first_pick, second_pick)
    slot_index_list = owners * ADP_DEV + popular
    return inverse[slot_index_list].astype(jnp.int32)


def draw_normalized_hidden_states(key, part):
    values = jnp.clip(jax.random.normal(jax.random.fold_in(key, 3), (TOKENS, MODEL_WIDTH)), -4.0, 4.0)
    return values.astype(jnp.float32).astype(jnp.bfloat16)


def steps_of(rng, shape, cuts, low, largest):
    def one(position, blocks):
        steps = jax.random.uniform(jax.random.fold_in(jax.random.fold_in(rng, 6), position), (blocks,), jnp.float32, low / len(cuts), largest / len(cuts))
        return jnp.repeat(jnp.exp(steps), shape[position] // blocks).reshape((-1,) + (1,) * (len(shape) - position - 1))

    factor_of = one(*cuts[0])
    for cut in cuts[1:]:
        factor_of = factor_of * one(*cut)
    return factor_of


def split_up(number_of, total, limit, slope):
    loads = [(1 << 20) // math.isqrt(rank ** slope) + 1 for rank in range(2, number_of + 1)]
    surplus, counts = total - limit - (number_of - 1), [1] * (number_of - 1)
    while surplus > 0:
        movable = [i for i in range(number_of - 1) if counts[i] < limit]
        pool, left = sum([loads[i] for i in movable]), surplus
        for i in movable:
            addition = min(limit - counts[i], max(1, left * loads[i] // pool), surplus)
            counts[i] = counts[i] + addition
            surplus = surplus - addition
    return np.array([limit] + counts)


def uneven(own_key, number_of, total, limit, slope):
    if number_of == 2:
        one = jax.random.randint(own_key, (), max(1, total - limit), min(limit, total - 1) + 1)
        return jnp.stack([one, total - one])
    tallies = jnp.asarray(split_up(number_of, total, limit, slope), jnp.int32)
    twos = (number_of - 1) // 2
    source_of, taker = tallies[1:1 + 2 * twos:2], tallies[2:2 + 2 * twos:2]
    room = jnp.minimum(source_of - 1, limit - taker)
    passed = jax.random.randint(jax.random.fold_in(own_key, 1), (twos,), 0, 1 << 20) % (room + 1)
    tallies = tallies.at[1:1 + 2 * twos:2].set(source_of - passed).at[2:2 + 2 * twos:2].set(taker + passed)
    return tallies[jax.random.permutation(jax.random.fold_in(own_key, 2), number_of)]


def noise(key, extent, spread, bound, cuts=(), held_as=jnp.bfloat16):
    entries = spread * jax.random.normal(key, extent, jnp.float32)
    if cuts:
        entries = entries * steps_of(key, extent, cuts, -0.22, 0.18)
    return jnp.clip(entries, -bound, bound).astype(held_as)


def setup_inputs(seed: int = 0) -> dict:
    key_of = jax.random.split(jax.random.key(seed), 11)
    normalized_hidden_states = draw_normalized_hidden_states(jax.random.fold_in(key_of[10], 71), 0)
    query_weight_matrix = noise(key_of[1], (MODEL_WIDTH, MODEL_WIDTH), MODEL_WIDTH ** -0.5, 0.125)
    key_weight_matrix = noise(key_of[2], (MODEL_WIDTH, KEY_VALUE_WIDTH), MODEL_WIDTH ** -0.5, 0.125)
    value_weight_matrix = noise(key_of[3], (MODEL_WIDTH, KEY_VALUE_WIDTH), MODEL_WIDTH ** -0.5, 0.125)
    adapter_down_weight = noise(key_of[4], (ADAPTER_TOTAL, 2 * ADAPTER_RANK, MODEL_WIDTH), MODEL_WIDTH ** -0.5, 0.125, ((0, 16), (2, 8)))
    adapter_up_query_weight = noise(key_of[5], (ADAPTER_TOTAL, ADAPTER_RANK, MODEL_WIDTH), ADAPTER_RANK ** -0.5, 1.5, ((0, 16), (2, 8)))
    adapter_up_value_weight = noise(key_of[6], (ADAPTER_TOTAL, ADAPTER_RANK, KEY_VALUE_WIDTH), ADAPTER_RANK ** -0.5, 1.5, ((0, 16), (2, 8)))
    adapter_panel_slot = draw_adapter_panel_slot(jax.random.fold_in(key_of[10], 71), 0)
    adapter_per_request = draw_adapter_per_request(jax.random.fold_in(key_of[10], 71), 0)
    request_token_length = jax.vmap(lambda own: uneven(own, REQ_DEV, TOK_DEV, LEN_MAX, 2))(jax.random.split(key_of[9], (N_SERVE * N_STORE))).reshape((N_SERVE * N_STORE, REQ_DEV)).astype(jnp.int32)
    return dict(normalized_hidden_states=normalized_hidden_states, query_weight_matrix=query_weight_matrix, key_weight_matrix=key_weight_matrix, value_weight_matrix=value_weight_matrix, adapter_down_weight=adapter_down_weight, adapter_up_query_weight=adapter_up_query_weight, adapter_up_value_weight=adapter_up_value_weight, adapter_panel_slot=adapter_panel_slot, adapter_per_request=adapter_per_request, request_token_length=request_token_length)


def rotary(heads_in, positions):
    half_dim = HEAD_DIM // 2
    frequency = 500000.0 ** (-(jnp.arange(half_dim).astype(jnp.float32) * 2.0 / HEAD_DIM))
    angles = positions.astype(jnp.float32)[:, None] * frequency[None, :]
    cosine_table = jnp.cos(angles)[:, None, :]
    sine_table = jnp.sin(angles)[:, None, :]
    first_half = heads_in[..., :half_dim]
    second_half = heads_in[..., half_dim:]
    return jnp.concatenate([first_half * cosine_table - second_half * sine_table,
                            second_half * cosine_table + first_half * sine_table], axis=-1)


def reduced_rank_products(block_list, down_panels, up_query, up_value):
    low = jnp.einsum('jkd,jrd->jkr', block_list.astype(jnp.float32), down_panels.astype(jnp.float32)).astype(jnp.bfloat16)
    query_update = jnp.einsum('jkr,jrd->jkd', low[..., :ADAPTER_RANK].astype(jnp.float32), up_query.astype(jnp.float32)).astype(jnp.bfloat16)
    value_update = jnp.einsum('jkr,jrd->jkd', low[..., ADAPTER_RANK:].astype(jnp.float32), up_value.astype(jnp.float32)).astype(jnp.bfloat16)
    return query_update, value_update


def attention(query_rot, key_rot, value_rows, request_ids):
    tok_rows = query_rot.shape[0]
    per_group = HEADS // KV_HEADS
    token_order = jnp.arange(tok_rows)
    allowed = (request_ids[:, None] == request_ids[None, :]) & (token_order[None, :] <= token_order[:, None])
    pieces = []
    for group_index in range(KV_HEADS):
        query_part = query_rot[:, group_index * per_group:(group_index + 1) * per_group, :].astype(jnp.float32)
        key_part = key_rot[:, group_index, :].astype(jnp.float32)
        value_part = value_rows[:, group_index, :].astype(jnp.float32)
        scores = jnp.einsum('qhd,kd->hqk', query_part, key_part) * (HEAD_DIM ** -0.5)
        scores = jnp.where(allowed[None], scores, -jnp.inf)
        row_max = jnp.max(scores, axis=-1, keepdims=True)
        raised = jnp.exp(scores - row_max)
        row_total = jnp.sum(raised, axis=-1)
        weights = raised.astype(jnp.bfloat16)
        mixed_heads = jnp.einsum('hqk,kd->qhd', weights.astype(jnp.float32), value_part) / jnp.transpose(row_total)[:, :, None]
        pieces.append(mixed_heads)
    return jnp.concatenate(pieces, axis=1).reshape(tok_rows, HEADS * HEAD_DIM).astype(jnp.bfloat16)


def reference(normalized_hidden_states, query_weight_matrix, key_weight_matrix, value_weight_matrix, adapter_down_weight, adapter_up_query_weight, adapter_up_value_weight, adapter_panel_slot, adapter_per_request, request_token_length):
    device_count = request_token_length.shape[0]
    tok_dev = normalized_hidden_states.shape[0] // device_count
    states = normalized_hidden_states.reshape(device_count, tok_dev, MODEL_WIDTH)

    def one_device(operands):
        states_dev, lengths, adapters = operands
        request_ends = jnp.cumsum(lengths).astype(jnp.int32)
        starts = (request_ends - lengths).astype(jnp.int32)
        token_order = jnp.arange(tok_dev, dtype=jnp.int32)
        request_ids = jnp.sum((token_order[:, None] >= request_ends[None, :]).astype(jnp.int32), axis=1).astype(jnp.int32)
        positions = (token_order - starts[request_ids]).astype(jnp.int32)
        offsets = jnp.arange(LEN_MAX, dtype=jnp.int32)
        valid_rows = offsets[None, :] < lengths[:, None]
        row_index = jnp.where(valid_rows, starts[:, None] + offsets[None, :], 0).astype(jnp.int32)
        block_list = jnp.where(valid_rows[..., None], states_dev[row_index], jnp.zeros((), jnp.bfloat16))
        slot_index_list = adapter_panel_slot[adapters]
        query_update, value_update = reduced_rank_products(block_list, adapter_down_weight[slot_index_list], adapter_up_query_weight[slot_index_list], adapter_up_value_weight[slot_index_list])
        delta_query = query_update[request_ids, positions]
        delta_value = value_update[request_ids, positions]
        base_query = jnp.dot(states_dev, query_weight_matrix, preferred_element_type=jnp.float32) + delta_query.astype(jnp.float32)
        query_rot = rotary(base_query.reshape(tok_dev, HEADS, HEAD_DIM), positions).astype(jnp.bfloat16)
        base_key = jnp.dot(states_dev, key_weight_matrix, preferred_element_type=jnp.float32)
        key_rot = rotary(base_key.reshape(tok_dev, KV_HEADS, HEAD_DIM), positions).astype(jnp.bfloat16)
        value_rows = (jnp.dot(states_dev, value_weight_matrix, preferred_element_type=jnp.float32) + delta_value.astype(jnp.float32)).astype(jnp.bfloat16)
        value_rows = value_rows.reshape(tok_dev, KV_HEADS, HEAD_DIM)
        return attention(query_rot, key_rot, value_rows, request_ids)

    result = lax.map(one_device, (states, request_token_length, adapter_per_request))
    return result.reshape(device_count * tok_dev, MODEL_WIDTH)
```

```python
import jax
import jax.numpy as jnp
from jax import lax
from jax.sharding import PartitionSpec as P

HEADS = 32
KV_HEADS = 8
HEAD_DIM = 64
ADAPTER_RANK = 16
ADP_DEV = 32
LEN_MAX = 64


def rotary(heads_in, positions):
    half_dim = HEAD_DIM // 2
    frequency = 500000.0 ** (-(jnp.arange(half_dim).astype(jnp.float32) * 2.0 / HEAD_DIM))
    angles = positions.astype(jnp.float32)[:, None] * frequency[None, :]
    cosine_table = jnp.cos(angles)[:, None, :]
    sine_table = jnp.sin(angles)[:, None, :]
    first_half = heads_in[..., :half_dim]
    second_half = heads_in[..., half_dim:]
    return jnp.concatenate(
        [
            first_half * cosine_table - second_half * sine_table,
            second_half * cosine_table + first_half * sine_table,
        ],
        axis=-1,
    )


def table_lookup(table, wanted):
    entries = jnp.arange(table.shape[0], dtype=jnp.int32)
    return jnp.sum(jnp.where(wanted[..., None] == entries, table, 0), axis=-1)


def reduced_rank_products(block_list, down_panels, up_query, up_value):
    low = jnp.einsum(
        "jkd,jrd->jkr", block_list, down_panels, preferred_element_type=jnp.float32
    ).astype(jnp.bfloat16)
    query_update = jnp.einsum(
        "jkr,jrd->jkd", low[..., :ADAPTER_RANK], up_query, preferred_element_type=jnp.float32
    ).astype(jnp.bfloat16)
    value_update = jnp.einsum(
        "jkr,jrd->jkd", low[..., ADAPTER_RANK:], up_value, preferred_element_type=jnp.float32
    ).astype(jnp.bfloat16)
    return (query_update, value_update)


def local_choice(panel_set, lists, adapter_panel_slot, my_store):
    source_slots = table_lookup(adapter_panel_slot, lists)
    mine_mask = source_slots // ADP_DEV == my_store
    local_source = jnp.sum(jnp.where(mine_mask, source_slots % ADP_DEV, 0), axis=1)
    return tuple((jnp.take(panel, local_source, axis=0) for panel in panel_set))


def attention(query_rot, key_rot, value_rows, request_ids):
    tok_rows = query_rot.shape[0]
    per_group = HEADS // KV_HEADS
    block_rows = min(128, tok_rows)
    reach = LEN_MAX
    key_pad = jnp.concatenate(
        [jnp.zeros((reach,) + key_rot.shape[1:], key_rot.dtype), key_rot], axis=0
    )
    value_pad = jnp.concatenate(
        [jnp.zeros((reach,) + value_rows.shape[1:], value_rows.dtype), value_rows], axis=0
    )
    ids_pad = jnp.concatenate([jnp.full((reach,), -1, jnp.int32), request_ids], axis=0)
    token_order = jnp.arange(tok_rows, dtype=jnp.int32)
    order_pad = jnp.concatenate([jnp.full((reach,), -1, jnp.int32), token_order], axis=0)
    outputs = []
    for block_index in range(tok_rows // block_rows):
        first = block_index * block_rows
        query_block = query_rot[first : first + block_rows]
        query_ids = request_ids[first : first + block_rows]
        query_order = token_order[first : first + block_rows]
        key_block = key_pad[first : first + reach + block_rows]
        value_block = value_pad[first : first + reach + block_rows]
        key_ids = ids_pad[first : first + reach + block_rows]
        key_order = order_pad[first : first + reach + block_rows]
        allowed = (query_ids[:, None] == key_ids[None, :]) & (
            key_order[None, :] <= query_order[:, None]
        )
        pieces = []
        for group_index in range(KV_HEADS):
            query_part = query_block[:, group_index * per_group : (group_index + 1) * per_group, :]
            key_part = key_block[:, group_index, :]
            value_part = value_block[:, group_index, :]
            scores = jnp.einsum(
                "qhd,kd->hqk", query_part, key_part, preferred_element_type=jnp.float32
            ) * HEAD_DIM ** (-0.5)
            scores = jnp.where(allowed[None], scores, -jnp.inf)
            row_max = jnp.max(scores, axis=-1, keepdims=True)
            raised = jnp.exp(scores - row_max)
            row_total = jnp.sum(raised, axis=-1)
            weights = raised.astype(jnp.bfloat16)
            mixed_heads = (
                jnp.einsum("hqk,kd->qhd", weights, value_part, preferred_element_type=jnp.float32)
                / jnp.transpose(row_total)[:, :, None]
            )
            pieces.append(mixed_heads)
        outputs.append(
            jnp.concatenate(pieces, axis=1)
            .reshape(block_rows, HEADS * HEAD_DIM)
            .astype(jnp.bfloat16)
        )
    return jnp.concatenate(outputs, axis=0)


def local(
    normalized_hidden_states,
    query_weight_matrix,
    key_weight_matrix,
    value_weight_matrix,
    adapter_down_weight,
    adapter_up_query_weight,
    adapter_up_value_weight,
    adapter_panel_slot,
    adapter_per_request,
    request_token_length,
):
    axes = ("serve", "store")
    serve_count = lax.axis_size("serve")
    store_count = lax.axis_size("store")
    my_store = lax.axis_index("store")
    tok_rows, width = normalized_hidden_states.shape
    request_count = request_token_length.shape[1]
    adp_dev, rank2, cols = adapter_down_weight.shape
    vcols = adapter_up_value_weight.shape[2]
    all_lists = lax.all_gather(adapter_per_request, axes, axis=0, tiled=True)
    all_slots = table_lookup(adapter_panel_slot, all_lists)
    mine = all_slots // ADP_DEV == my_store
    local_pick = jnp.sum(jnp.where(mine, all_slots % ADP_DEV, 0), axis=1)
    send = jnp.concatenate(
        [
            jnp.take(adapter_down_weight, local_pick, axis=0).reshape(local_pick.shape[0], -1),
            jnp.take(adapter_up_query_weight, local_pick, axis=0).reshape(local_pick.shape[0], -1),
            jnp.take(adapter_up_value_weight, local_pick, axis=0).reshape(local_pick.shape[0], -1),
        ],
        axis=1,
    )
    got = lax.all_to_all(send, axes, split_axis=0, concat_axis=0, tiled=True)
    got = got.reshape(serve_count, store_count, -1)
    n_down = rank2 * cols
    n_upq = ADAPTER_RANK * cols
    down = got[:, :, :n_down].reshape(serve_count, store_count, rank2, cols)
    upq = got[:, :, n_down : n_down + n_upq].reshape(serve_count, store_count, ADAPTER_RANK, cols)
    upv = got[:, :, n_down + n_upq :].reshape(serve_count, store_count, ADAPTER_RANK, vcols)

    lengths = request_token_length[0]
    adapters = adapter_per_request[0]
    request_ends = jnp.cumsum(lengths)
    starts = request_ends - lengths
    token_order = jnp.arange(tok_rows, dtype=jnp.int32)
    request_ids = jnp.sum((token_order[:, None] >= request_ends[None, :]).astype(jnp.int32), axis=1)
    member = request_ids[:, None] == jnp.arange(request_count, dtype=jnp.int32)[None, :]
    positions = token_order - jnp.sum(jnp.where(member, starts[None, :], 0), axis=1)
    owners = table_lookup(adapter_panel_slot, adapters) // ADP_DEV
    owner_token = jnp.sum(jnp.where(member, owners[None, :], 0), axis=1)

    states3 = normalized_hidden_states.reshape(tok_rows, serve_count, cols)
    low = jnp.einsum(
        "tsf,sorf->tor", states3, down, preferred_element_type=jnp.float32
    ).astype(jnp.bfloat16)
    owner_mask = owner_token[:, None, None] == jnp.arange(store_count, dtype=jnp.int32)[None, :, None]
    low = jnp.where(owner_mask, low, jnp.zeros((), jnp.bfloat16))
    delta_query = jnp.einsum(
        "tor,sorf->tsf", low[..., :ADAPTER_RANK], upq, preferred_element_type=jnp.float32
    ).astype(jnp.bfloat16).reshape(tok_rows, serve_count * cols)
    delta_value = jnp.einsum(
        "tor,sorf->tsf", low[..., ADAPTER_RANK:], upv, preferred_element_type=jnp.float32
    ).astype(jnp.bfloat16).reshape(tok_rows, serve_count * vcols)

    base_query = jnp.dot(
        normalized_hidden_states, query_weight_matrix, preferred_element_type=jnp.float32
    ) + delta_query.astype(jnp.float32)
    query_rot = rotary(base_query.reshape(tok_rows, HEADS, HEAD_DIM), positions).astype(
        jnp.bfloat16
    )
    base_key = jnp.dot(
        normalized_hidden_states, key_weight_matrix, preferred_element_type=jnp.float32
    )
    key_rot = rotary(base_key.reshape(tok_rows, KV_HEADS, HEAD_DIM), positions).astype(jnp.bfloat16)
    value_rows = (
        jnp.dot(normalized_hidden_states, value_weight_matrix, preferred_element_type=jnp.float32)
        + delta_value.astype(jnp.float32)
    ).astype(jnp.bfloat16)
    value_rows = value_rows.reshape(tok_rows, KV_HEADS, HEAD_DIM)
    return attention(query_rot, key_rot, value_rows, request_ids)


def solution(mesh):
    return jax.shard_map(
        local,
        mesh=mesh,
        in_specs=(
            P(("serve", "store"), None),
            P(),
            P(),
            P(),
            P("store", None, "serve"),
            P("store", None, "serve"),
            P("store", None, "serve"),
            P(),
            P(("serve", "store"), None),
            P(("serve", "store"), None),
        ),
        out_specs=P(("serve", "store"), None),
        check_vma=False,
    )
```

```python
import jax
import jax.numpy as jnp
from jax import lax
from jax.sharding import PartitionSpec as P

HEADS = 32
KV_HEADS = 8
HEAD_DIM = 64
ADAPTER_RANK = 16
ADP_DEV = 32
LEN_MAX = 64


def rotary(heads_in, positions):
    half_dim = HEAD_DIM // 2
    frequency = 500000.0 ** (-(jnp.arange(half_dim).astype(jnp.float32) * 2.0 / HEAD_DIM))
    angles = positions.astype(jnp.float32)[:, None] * frequency[None, :]
    cosine_table = jnp.cos(angles)[:, None, :]
    sine_table = jnp.sin(angles)[:, None, :]
    first_half = heads_in[..., :half_dim]
    second_half = heads_in[..., half_dim:]
    return jnp.concatenate(
        [
            first_half * cosine_table - second_half * sine_table,
            second_half * cosine_table + first_half * sine_table,
        ],
        axis=-1,
    )


def table_lookup(table, wanted):
    entries = jnp.arange(table.shape[0], dtype=jnp.int32)
    return jnp.sum(jnp.where(wanted[..., None] == entries, table, 0), axis=-1)


def reduced_rank_products(block_list, down_panels, up_query, up_value):
    low = jnp.einsum(
        "jkd,jrd->jkr", block_list, down_panels, preferred_element_type=jnp.float32
    ).astype(jnp.bfloat16)
    query_update = jnp.einsum(
        "jkr,jrd->jkd", low[..., :ADAPTER_RANK], up_query, preferred_element_type=jnp.float32
    ).astype(jnp.bfloat16)
    value_update = jnp.einsum(
        "jkr,jrd->jkd", low[..., ADAPTER_RANK:], up_value, preferred_element_type=jnp.float32
    ).astype(jnp.bfloat16)
    return (query_update, value_update)


def local_choice(panel_set, lists, adapter_panel_slot, my_store):
    source_slots = table_lookup(adapter_panel_slot, lists)
    mine_mask = source_slots // ADP_DEV == my_store
    local_source = jnp.sum(jnp.where(mine_mask, source_slots % ADP_DEV, 0), axis=1)
    return tuple((jnp.take(panel, local_source, axis=0) for panel in panel_set))


def attention(query_rot, key_rot, value_rows, request_ids):
    tok_rows = query_rot.shape[0]
    per_group = HEADS // KV_HEADS
    block_rows = min(128, tok_rows)
    reach = LEN_MAX
    key_pad = jnp.concatenate(
        [jnp.zeros((reach,) + key_rot.shape[1:], key_rot.dtype), key_rot], axis=0
    )
    value_pad = jnp.concatenate(
        [jnp.zeros((reach,) + value_rows.shape[1:], value_rows.dtype), value_rows], axis=0
    )
    ids_pad = jnp.concatenate([jnp.full((reach,), -1, jnp.int32), request_ids], axis=0)
    token_order = jnp.arange(tok_rows, dtype=jnp.int32)
    order_pad = jnp.concatenate([jnp.full((reach,), -1, jnp.int32), token_order], axis=0)
    outputs = []
    for block_index in range(tok_rows // block_rows):
        first = block_index * block_rows
        query_block = query_rot[first : first + block_rows]
        query_ids = request_ids[first : first + block_rows]
        query_order = token_order[first : first + block_rows]
        key_block = key_pad[first : first + reach + block_rows]
        value_block = value_pad[first : first + reach + block_rows]
        key_ids = ids_pad[first : first + reach + block_rows]
        key_order = order_pad[first : first + reach + block_rows]
        allowed = (query_ids[:, None] == key_ids[None, :]) & (
            key_order[None, :] <= query_order[:, None]
        )
        pieces = []
        for group_index in range(KV_HEADS):
            query_part = query_block[:, group_index * per_group : (group_index + 1) * per_group, :]
            key_part = key_block[:, group_index, :]
            value_part = value_block[:, group_index, :]
            scores = jnp.einsum(
                "qhd,kd->hqk", query_part, key_part, preferred_element_type=jnp.float32
            ) * HEAD_DIM ** (-0.5)
            scores = jnp.where(allowed[None], scores, -jnp.inf)
            row_max = jnp.max(scores, axis=-1, keepdims=True)
            raised = jnp.exp(scores - row_max)
            row_total = jnp.sum(raised, axis=-1)
            weights = raised.astype(jnp.bfloat16)
            mixed_heads = (
                jnp.einsum("hqk,kd->qhd", weights, value_part, preferred_element_type=jnp.float32)
                / jnp.transpose(row_total)[:, :, None]
            )
            pieces.append(mixed_heads)
        outputs.append(
            jnp.concatenate(pieces, axis=1)
            .reshape(block_rows, HEADS * HEAD_DIM)
            .astype(jnp.bfloat16)
        )
    return jnp.concatenate(outputs, axis=0)


def local(
    normalized_hidden_states,
    query_weight_matrix,
    key_weight_matrix,
    value_weight_matrix,
    adapter_down_weight,
    adapter_up_query_weight,
    adapter_up_value_weight,
    adapter_panel_slot,
    adapter_per_request,
    request_token_length,
):
    axes = ("serve", "store")
    serve_count = lax.axis_size("serve")
    store_count = lax.axis_size("store")
    my_store = lax.axis_index("store")
    tok_rows, width = normalized_hidden_states.shape
    request_count = request_token_length.shape[1]
    adp_dev, rank2, cols = adapter_down_weight.shape
    vcols = adapter_up_value_weight.shape[2]
    device_total = serve_count * store_count
    all_lists = lax.all_to_all(
        jnp.broadcast_to(adapter_per_request, (device_total, request_count)), axes, 0, 0, tiled=True
    )
    all_slots = table_lookup(adapter_panel_slot, all_lists)
    mine = all_slots // ADP_DEV == my_store
    local_pick = jnp.sum(jnp.where(mine, all_slots % ADP_DEV, 0), axis=1)
    down = lax.all_to_all(
        jnp.take(adapter_down_weight, local_pick, axis=0), axes, 0, 0, tiled=True
    ).reshape(serve_count, store_count, rank2, cols)
    upq = lax.all_to_all(
        jnp.take(adapter_up_query_weight, local_pick, axis=0), axes, 0, 0, tiled=True
    ).reshape(serve_count, store_count, ADAPTER_RANK, cols)
    upv = lax.all_to_all(
        jnp.take(adapter_up_value_weight, local_pick, axis=0), axes, 0, 0, tiled=True
    ).reshape(serve_count, store_count, ADAPTER_RANK, vcols)

    lengths = request_token_length[0]
    adapters = adapter_per_request[0]
    request_ends = jnp.cumsum(lengths)
    starts = request_ends - lengths
    token_order = jnp.arange(tok_rows, dtype=jnp.int32)
    request_ids = jnp.sum((token_order[:, None] >= request_ends[None, :]).astype(jnp.int32), axis=1)
    member = request_ids[:, None] == jnp.arange(request_count, dtype=jnp.int32)[None, :]
    positions = token_order - jnp.sum(jnp.where(member, starts[None, :], 0), axis=1)
    owners = table_lookup(adapter_panel_slot, adapters) // ADP_DEV
    owner_token = jnp.sum(jnp.where(member, owners[None, :], 0), axis=1)

    states3 = normalized_hidden_states.reshape(tok_rows, serve_count, cols)
    low = jnp.einsum(
        "tsf,sorf->tor", states3, down, preferred_element_type=jnp.float32
    ).astype(jnp.bfloat16)
    owner_mask = owner_token[:, None, None] == jnp.arange(store_count, dtype=jnp.int32)[None, :, None]
    low = jnp.where(owner_mask, low, jnp.zeros((), jnp.bfloat16))
    delta_query = jnp.einsum(
        "tor,sorf->tsf", low[..., :ADAPTER_RANK], upq, preferred_element_type=jnp.float32
    ).astype(jnp.bfloat16).reshape(tok_rows, serve_count * cols)
    delta_value = jnp.einsum(
        "tor,sorf->tsf", low[..., ADAPTER_RANK:], upv, preferred_element_type=jnp.float32
    ).astype(jnp.bfloat16).reshape(tok_rows, serve_count * vcols)

    base_query = jnp.dot(
        normalized_hidden_states, query_weight_matrix, preferred_element_type=jnp.float32
    ) + delta_query.astype(jnp.float32)
    query_rot = rotary(base_query.reshape(tok_rows, HEADS, HEAD_DIM), positions).astype(
        jnp.bfloat16
    )
    base_key = jnp.dot(
        normalized_hidden_states, key_weight_matrix, preferred_element_type=jnp.float32
    )
    key_rot = rotary(base_key.reshape(tok_rows, KV_HEADS, HEAD_DIM), positions).astype(jnp.bfloat16)
    value_rows = (
        jnp.dot(normalized_hidden_states, value_weight_matrix, preferred_element_type=jnp.float32)
        + delta_value.astype(jnp.float32)
    ).astype(jnp.bfloat16)
    value_rows = value_rows.reshape(tok_rows, KV_HEADS, HEAD_DIM)
    return attention(query_rot, key_rot, value_rows, request_ids)


def solution(mesh):
    return jax.shard_map(
        local,
        mesh=mesh,
        in_specs=(
            P(("serve", "store"), None),
            P(),
            P(),
            P(),
            P("store", None, "serve"),
            P("store", None, "serve"),
            P("store", None, "serve"),
            P(),
            P(("serve", "store"), None),
            P(("serve", "store"), None),
        ),
        out_specs=P(("serve", "store"), None),
        check_vma=False,
    )
```

```python
import jax
import jax.numpy as jnp
from jax import lax
from jax.experimental import pallas as pl
from jax.experimental.pallas import tpu as pltpu
from jax.sharding import PartitionSpec as P

HEADS = 32
KV_HEADS = 8
HEAD_DIM = 64
ADAPTER_RANK = 16
ADP_DEV = 32
LEN_MAX = 64


def rotary(heads_in, positions):
    half_dim = HEAD_DIM // 2
    frequency = 500000.0 ** (-(jnp.arange(half_dim).astype(jnp.float32) * 2.0 / HEAD_DIM))
    angles = positions.astype(jnp.float32)[:, None] * frequency[None, :]
    cosine_table = jnp.cos(angles)[:, None, :]
    sine_table = jnp.sin(angles)[:, None, :]
    first_half = heads_in[..., :half_dim]
    second_half = heads_in[..., half_dim:]
    return jnp.concatenate(
        [
            first_half * cosine_table - second_half * sine_table,
            second_half * cosine_table + first_half * sine_table,
        ],
        axis=-1,
    )


def table_lookup(table, wanted):
    entries = jnp.arange(table.shape[0], dtype=jnp.int32)
    return jnp.sum(jnp.where(wanted[..., None] == entries, table, 0), axis=-1)


def reduced_rank_products(block_list, down_panels, up_query, up_value):
    low = jnp.einsum(
        "jkd,jrd->jkr", block_list, down_panels, preferred_element_type=jnp.float32
    ).astype(jnp.bfloat16)
    query_update = jnp.einsum(
        "jkr,jrd->jkd", low[..., :ADAPTER_RANK], up_query, preferred_element_type=jnp.float32
    ).astype(jnp.bfloat16)
    value_update = jnp.einsum(
        "jkr,jrd->jkd", low[..., ADAPTER_RANK:], up_value, preferred_element_type=jnp.float32
    ).astype(jnp.bfloat16)
    return (query_update, value_update)


def local_choice(panel_set, lists, adapter_panel_slot, my_store):
    source_slots = table_lookup(adapter_panel_slot, lists)
    mine_mask = source_slots // ADP_DEV == my_store
    local_source = jnp.sum(jnp.where(mine_mask, source_slots % ADP_DEV, 0), axis=1)
    return tuple((jnp.take(panel, local_source, axis=0) for panel in panel_set))


def attention(query_rot, key_rot, value_rows, request_ids):
    tok_rows = query_rot.shape[0]
    per_group = HEADS // KV_HEADS
    block_rows = min(128, tok_rows)
    reach = LEN_MAX
    key_pad = jnp.concatenate(
        [jnp.zeros((reach,) + key_rot.shape[1:], key_rot.dtype), key_rot], axis=0
    )
    value_pad = jnp.concatenate(
        [jnp.zeros((reach,) + value_rows.shape[1:], value_rows.dtype), value_rows], axis=0
    )
    ids_pad = jnp.concatenate([jnp.full((reach,), -1, jnp.int32), request_ids], axis=0)
    token_order = jnp.arange(tok_rows, dtype=jnp.int32)
    order_pad = jnp.concatenate([jnp.full((reach,), -1, jnp.int32), token_order], axis=0)
    outputs = []
    for block_index in range(tok_rows // block_rows):
        first = block_index * block_rows
        query_block = query_rot[first : first + block_rows]
        query_ids = request_ids[first : first + block_rows]
        query_order = token_order[first : first + block_rows]
        key_block = key_pad[first : first + reach + block_rows]
        value_block = value_pad[first : first + reach + block_rows]
        key_ids = ids_pad[first : first + reach + block_rows]
        key_order = order_pad[first : first + reach + block_rows]
        allowed = (query_ids[:, None] == key_ids[None, :]) & (
            key_order[None, :] <= query_order[:, None]
        )
        pieces = []
        for group_index in range(KV_HEADS):
            query_part = query_block[:, group_index * per_group : (group_index + 1) * per_group, :]
            key_part = key_block[:, group_index, :]
            value_part = value_block[:, group_index, :]
            scores = jnp.einsum(
                "qhd,kd->hqk", query_part, key_part, preferred_element_type=jnp.float32
            ) * HEAD_DIM ** (-0.5)
            scores = jnp.where(allowed[None], scores, -jnp.inf)
            row_max = jnp.max(scores, axis=-1, keepdims=True)
            raised = jnp.exp(scores - row_max)
            row_total = jnp.sum(raised, axis=-1)
            weights = raised.astype(jnp.bfloat16)
            mixed_heads = (
                jnp.einsum("hqk,kd->qhd", weights, value_part, preferred_element_type=jnp.float32)
                / jnp.transpose(row_total)[:, :, None]
            )
            pieces.append(mixed_heads)
        outputs.append(
            jnp.concatenate(pieces, axis=1)
            .reshape(block_rows, HEADS * HEAD_DIM)
            .astype(jnp.bfloat16)
        )
    return jnp.concatenate(outputs, axis=0)


def local(
    normalized_hidden_states,
    query_weight_matrix,
    key_weight_matrix,
    value_weight_matrix,
    adapter_down_weight,
    adapter_up_query_weight,
    adapter_up_value_weight,
    adapter_panel_slot,
    adapter_per_request,
    request_token_length,
):
    axes = ("serve", "store")
    serve_count = lax.axis_size("serve")
    store_count = lax.axis_size("store")
    my_store = lax.axis_index("store")
    tok_rows, width = normalized_hidden_states.shape
    request_count = request_token_length.shape[1]
    adp_dev, rank2, cols = adapter_down_weight.shape
    vcols = adapter_up_value_weight.shape[2]
    device_total = serve_count * store_count
    all_lists = lax.all_to_all(
        jnp.broadcast_to(adapter_per_request, (device_total, request_count)), axes, 0, 0, tiled=True
    )
    all_slots = table_lookup(adapter_panel_slot, all_lists)
    mine = all_slots // ADP_DEV == my_store
    local_pick = jnp.sum(jnp.where(mine, all_slots % ADP_DEV, 0), axis=1)
    down = lax.all_to_all(
        jnp.take(adapter_down_weight, local_pick, axis=0), axes, 0, 0, tiled=True
    ).reshape(serve_count, store_count, rank2, cols)
    upq = lax.all_to_all(
        jnp.take(adapter_up_query_weight, local_pick, axis=0), axes, 0, 0, tiled=True
    ).reshape(serve_count, store_count, ADAPTER_RANK, cols)
    upv = lax.all_to_all(
        jnp.take(adapter_up_value_weight, local_pick, axis=0), axes, 0, 0, tiled=True
    ).reshape(serve_count, store_count, ADAPTER_RANK, vcols)

    lengths = request_token_length[0]
    adapters = adapter_per_request[0]
    request_ends = jnp.cumsum(lengths)
    starts = request_ends - lengths
    token_order = jnp.arange(tok_rows, dtype=jnp.int32)
    request_ids = jnp.sum((token_order[:, None] >= request_ends[None, :]).astype(jnp.int32), axis=1)
    member = request_ids[:, None] == jnp.arange(request_count, dtype=jnp.int32)[None, :]
    positions = token_order - jnp.sum(jnp.where(member, starts[None, :], 0), axis=1)
    owners = table_lookup(adapter_panel_slot, adapters) // ADP_DEV
    owner_token = jnp.sum(jnp.where(member, owners[None, :], 0), axis=1)

    states3 = normalized_hidden_states.reshape(tok_rows, serve_count, cols)
    low = jnp.einsum(
        "tsf,sorf->tor", states3, down, preferred_element_type=jnp.float32
    ).astype(jnp.bfloat16)
    owner_mask = owner_token[:, None, None] == jnp.arange(store_count, dtype=jnp.int32)[None, :, None]
    low = jnp.where(owner_mask, low, jnp.zeros((), jnp.bfloat16))
    delta_query = jnp.einsum(
        "tor,sorf->tsf", low[..., :ADAPTER_RANK], upq, preferred_element_type=jnp.float32
    ).astype(jnp.bfloat16).reshape(tok_rows, serve_count * cols)
    delta_value = jnp.einsum(
        "tor,sorf->tsf", low[..., ADAPTER_RANK:], upv, preferred_element_type=jnp.float32
    ).astype(jnp.bfloat16).reshape(tok_rows, serve_count * vcols)

    q_base = jnp.dot(
        normalized_hidden_states, query_weight_matrix, preferred_element_type=jnp.float32
    )
    k_base = jnp.dot(
        normalized_hidden_states, key_weight_matrix, preferred_element_type=jnp.float32
    )
    v_base = jnp.dot(
        normalized_hidden_states, value_weight_matrix, preferred_element_type=jnp.float32
    )
    return fused_attention(q_base, delta_query, k_base, v_base, delta_value, positions)


def _swap_halves(x):
    return jnp.concatenate([x[:, 32:64], x[:, 0:32], x[:, 96:128], x[:, 64:96]], axis=1)


def _attend_kernel(qb_ref, dq_ref, kb_ref, vb_ref, dv_ref, cos_ref, sin_ref, pos_ref, out_ref,
                   q_s, kd_s, vd_s):
    rows = qb_ref.shape[0]
    blk = 128
    n_blk = rows // blk
    q_chunks = qb_ref.shape[1] // 128
    k_chunks = kb_ref.shape[1] // 128
    lane = lax.broadcasted_iota(jnp.int32, (1, 128), 1)

    def rope_rows(r, carry):
        r0 = pl.multiple_of(r * blk, blk)
        cos = cos_ref[pl.ds(r0, blk), :]
        sin = sin_ref[pl.ds(r0, blk), :]

        def q_col(c, carry2):
            c0 = pl.multiple_of(c * 128, 128)
            x = qb_ref[pl.ds(r0, blk), pl.ds(c0, 128)] + dq_ref[pl.ds(r0, blk), pl.ds(c0, 128)].astype(jnp.float32)
            q_s[pl.ds(r0, blk), pl.ds(c0, 128)] = (x * cos + _swap_halves(x) * sin).astype(jnp.bfloat16)
            return carry2

        lax.fori_loop(0, q_chunks, q_col, 0)
        for c in range(k_chunks):
            x = kb_ref[pl.ds(r0, blk), c * 128:(c + 1) * 128]
            k = (x * cos + _swap_halves(x) * sin).astype(jnp.bfloat16).astype(jnp.float32)
            v = (vb_ref[pl.ds(r0, blk), c * 128:(c + 1) * 128]
                 + dv_ref[pl.ds(r0, blk), c * 128:(c + 1) * 128].astype(jnp.float32))
            v = v.astype(jnp.bfloat16).astype(jnp.float32)
            zeros = jnp.zeros((blk, 64), jnp.float32)
            for half in range(2):
                g = 2 * c + half
                kg = k[:, half * 64:(half + 1) * 64]
                vg = v[:, half * 64:(half + 1) * 64]
                kd_s[g, pl.ds(r0, blk), :] = jnp.concatenate([kg, kg], axis=1).astype(jnp.bfloat16)
                vd_s[g, pl.ds(r0, blk), 0:128] = jnp.concatenate([vg, zeros], axis=1).astype(jnp.bfloat16)
                vd_s[g, pl.ds(r0, blk), 128:256] = jnp.concatenate([zeros, vg], axis=1).astype(jnp.bfloat16)
        return carry

    lax.fori_loop(0, n_blk, rope_rows, 0)

    window = 2 * blk
    per_group = HEADS // KV_HEADS

    def query_block(b, carry):
        q0 = pl.multiple_of(b * blk, blk)
        ws = pl.multiple_of(jnp.clip(b * blk - blk, 0, rows - window), blk)
        qpos = pos_ref[pl.ds(q0, blk), :]
        qidx = q0 + lax.broadcasted_iota(jnp.int32, (blk, 1), 0)
        kidx = ws + lax.broadcasted_iota(jnp.int32, (1, window), 1)
        allowed = (kidx >= qidx - qpos) & (kidx <= qidx)

        def head_pair(j, carry2):
            g = j // (per_group // 2)
            c0 = pl.multiple_of(j * 128, 128)
            qc = q_s[pl.ds(q0, blk), pl.ds(c0, 128)]
            kd = kd_s[g, pl.ds(ws, window), :]
            vd = vd_s[g, pl.ds(ws, window), :]
            zero = jnp.zeros_like(qc)
            probs, totals = [], []
            for half in range(2):
                keep = (lane < 64) if half == 0 else (lane >= 64)
                qh = jnp.where(keep, qc, zero)
                s = lax.dot_general(qh, kd, (((1,), (1,)), ((), ())),
                                    preferred_element_type=jnp.float32) * (HEAD_DIM ** -0.5)
                s = jnp.where(allowed, s, -jnp.inf)
                m = jnp.max(s, axis=1, keepdims=True)
                p = jnp.exp(s - m)
                totals.append(jnp.sum(p, axis=1, keepdims=True))
                probs.append(p.astype(jnp.bfloat16))
            o = (jnp.dot(probs[0], vd[:, 0:128], preferred_element_type=jnp.float32)
                 + jnp.dot(probs[1], vd[:, 128:256], preferred_element_type=jnp.float32))
            o = jnp.where(lane < 64, o / totals[0], o / totals[1])
            out_ref[pl.ds(q0, blk), pl.ds(c0, 128)] = o.astype(out_ref.dtype)
            return carry2

        lax.fori_loop(0, HEADS // 2, head_pair, 0)
        return carry

    lax.fori_loop(0, n_blk, query_block, 0)


def rope_tables(positions):
    half_dim = HEAD_DIM // 2
    frequency = 500000.0 ** (-(jnp.arange(half_dim).astype(jnp.float32) * 2.0 / HEAD_DIM))
    angles = positions.astype(jnp.float32)[:, None] * frequency[None, :]
    cos = jnp.cos(angles)
    sin = jnp.sin(angles)
    cos_t = jnp.concatenate([cos, cos, cos, cos], axis=1)
    sin_t = jnp.concatenate([-sin, sin, -sin, sin], axis=1)
    return cos_t, sin_t


def fused_attention(q_base, delta_q, k_base, v_base, delta_v, positions):
    rows = q_base.shape[0]
    cos_t, sin_t = rope_tables(positions)
    pos_col = positions.astype(jnp.int32).reshape(rows, 1)
    vmem = pl.BlockSpec(memory_space=pltpu.VMEM)
    flops = 2 * rows * 256 * 64 * 2 * HEADS * 2
    return pl.pallas_call(
        _attend_kernel,
        out_shape=jax.ShapeDtypeStruct((rows, HEADS * HEAD_DIM), jnp.bfloat16),
        in_specs=[vmem] * 8,
        out_specs=vmem,
        scratch_shapes=[
            pltpu.VMEM((rows, HEADS * HEAD_DIM), jnp.bfloat16),
            pltpu.VMEM((KV_HEADS, rows, 128), jnp.bfloat16),
            pltpu.VMEM((KV_HEADS, rows, 256), jnp.bfloat16),
        ],
        compiler_params=pltpu.CompilerParams(vmem_limit_bytes=48 * 1024 * 1024),
        cost_estimate=pl.CostEstimate(flops=flops, transcendentals=rows * 256 * HEADS,
                                      bytes_accessed=rows * (2048 * 6 + 512 * 12 + 256 * 4)),
    )(q_base, delta_q, k_base, v_base, delta_v, cos_t, sin_t, pos_col)


def solution(mesh):
    return jax.shard_map(
        local,
        mesh=mesh,
        in_specs=(
            P(("serve", "store"), None),
            P(),
            P(),
            P(),
            P("store", None, "serve"),
            P("store", None, "serve"),
            P("store", None, "serve"),
            P(),
            P(("serve", "store"), None),
            P(("serve", "store"), None),
        ),
        out_specs=P(("serve", "store"), None),
        check_vma=False,
    )
```

```python
import jax
import jax.numpy as jnp
from jax import lax
from jax.experimental import pallas as pl
from jax.experimental.pallas import tpu as pltpu
from jax.sharding import PartitionSpec as P

HEADS = 32
KV_HEADS = 8
HEAD_DIM = 64
ADAPTER_RANK = 16
ADP_DEV = 32
LEN_MAX = 64


def rotary(heads_in, positions):
    half_dim = HEAD_DIM // 2
    frequency = 500000.0 ** (-(jnp.arange(half_dim).astype(jnp.float32) * 2.0 / HEAD_DIM))
    angles = positions.astype(jnp.float32)[:, None] * frequency[None, :]
    cosine_table = jnp.cos(angles)[:, None, :]
    sine_table = jnp.sin(angles)[:, None, :]
    first_half = heads_in[..., :half_dim]
    second_half = heads_in[..., half_dim:]
    return jnp.concatenate(
        [
            first_half * cosine_table - second_half * sine_table,
            second_half * cosine_table + first_half * sine_table,
        ],
        axis=-1,
    )


def table_lookup(table, wanted):
    entries = jnp.arange(table.shape[0], dtype=jnp.int32)
    return jnp.sum(jnp.where(wanted[..., None] == entries, table, 0), axis=-1)


def reduced_rank_products(block_list, down_panels, up_query, up_value):
    low = jnp.einsum(
        "jkd,jrd->jkr", block_list, down_panels, preferred_element_type=jnp.float32
    ).astype(jnp.bfloat16)
    query_update = jnp.einsum(
        "jkr,jrd->jkd", low[..., :ADAPTER_RANK], up_query, preferred_element_type=jnp.float32
    ).astype(jnp.bfloat16)
    value_update = jnp.einsum(
        "jkr,jrd->jkd", low[..., ADAPTER_RANK:], up_value, preferred_element_type=jnp.float32
    ).astype(jnp.bfloat16)
    return (query_update, value_update)


def local_choice(panel_set, lists, adapter_panel_slot, my_store):
    source_slots = table_lookup(adapter_panel_slot, lists)
    mine_mask = source_slots // ADP_DEV == my_store
    local_source = jnp.sum(jnp.where(mine_mask, source_slots % ADP_DEV, 0), axis=1)
    return tuple((jnp.take(panel, local_source, axis=0) for panel in panel_set))


def attention(query_rot, key_rot, value_rows, request_ids):
    tok_rows = query_rot.shape[0]
    per_group = HEADS // KV_HEADS
    block_rows = min(128, tok_rows)
    reach = LEN_MAX
    key_pad = jnp.concatenate(
        [jnp.zeros((reach,) + key_rot.shape[1:], key_rot.dtype), key_rot], axis=0
    )
    value_pad = jnp.concatenate(
        [jnp.zeros((reach,) + value_rows.shape[1:], value_rows.dtype), value_rows], axis=0
    )
    ids_pad = jnp.concatenate([jnp.full((reach,), -1, jnp.int32), request_ids], axis=0)
    token_order = jnp.arange(tok_rows, dtype=jnp.int32)
    order_pad = jnp.concatenate([jnp.full((reach,), -1, jnp.int32), token_order], axis=0)
    outputs = []
    for block_index in range(tok_rows // block_rows):
        first = block_index * block_rows
        query_block = query_rot[first : first + block_rows]
        query_ids = request_ids[first : first + block_rows]
        query_order = token_order[first : first + block_rows]
        key_block = key_pad[first : first + reach + block_rows]
        value_block = value_pad[first : first + reach + block_rows]
        key_ids = ids_pad[first : first + reach + block_rows]
        key_order = order_pad[first : first + reach + block_rows]
        allowed = (query_ids[:, None] == key_ids[None, :]) & (
            key_order[None, :] <= query_order[:, None]
        )
        pieces = []
        for group_index in range(KV_HEADS):
            query_part = query_block[:, group_index * per_group : (group_index + 1) * per_group, :]
            key_part = key_block[:, group_index, :]
            value_part = value_block[:, group_index, :]
            scores = jnp.einsum(
                "qhd,kd->hqk", query_part, key_part, preferred_element_type=jnp.float32
            ) * HEAD_DIM ** (-0.5)
            scores = jnp.where(allowed[None], scores, -jnp.inf)
            row_max = jnp.max(scores, axis=-1, keepdims=True)
            raised = jnp.exp(scores - row_max)
            row_total = jnp.sum(raised, axis=-1)
            weights = raised.astype(jnp.bfloat16)
            mixed_heads = (
                jnp.einsum("hqk,kd->qhd", weights, value_part, preferred_element_type=jnp.float32)
                / jnp.transpose(row_total)[:, :, None]
            )
            pieces.append(mixed_heads)
        outputs.append(
            jnp.concatenate(pieces, axis=1)
            .reshape(block_rows, HEADS * HEAD_DIM)
            .astype(jnp.bfloat16)
        )
    return jnp.concatenate(outputs, axis=0)


def local(
    normalized_hidden_states,
    query_weight_matrix,
    key_weight_matrix,
    value_weight_matrix,
    adapter_down_weight,
    adapter_up_query_weight,
    adapter_up_value_weight,
    adapter_panel_slot,
    adapter_per_request,
    request_token_length,
):
    axes = ("serve", "store")
    serve_count = lax.axis_size("serve")
    store_count = lax.axis_size("store")
    my_store = lax.axis_index("store")
    tok_rows, width = normalized_hidden_states.shape
    request_count = request_token_length.shape[1]
    adp_dev, rank2, cols = adapter_down_weight.shape
    vcols = adapter_up_value_weight.shape[2]
    device_total = serve_count * store_count
    all_lists = lax.all_to_all(
        jnp.broadcast_to(adapter_per_request, (device_total, request_count)), axes, 0, 0, tiled=True
    )
    all_slots = table_lookup(adapter_panel_slot, all_lists)
    mine = all_slots // ADP_DEV == my_store
    local_pick = jnp.sum(jnp.where(mine, all_slots % ADP_DEV, 0), axis=1)
    down = lax.all_to_all(
        jnp.take(adapter_down_weight, local_pick, axis=0), axes, 0, 0, tiled=True
    ).reshape(serve_count, store_count, rank2, cols)
    upq = lax.all_to_all(
        jnp.take(adapter_up_query_weight, local_pick, axis=0), axes, 0, 0, tiled=True
    ).reshape(serve_count, store_count, ADAPTER_RANK, cols)
    upv = lax.all_to_all(
        jnp.take(adapter_up_value_weight, local_pick, axis=0), axes, 0, 0, tiled=True
    ).reshape(serve_count, store_count, ADAPTER_RANK, vcols)

    lengths = request_token_length[0]
    adapters = adapter_per_request[0]
    request_ends = jnp.cumsum(lengths)
    starts = request_ends - lengths
    token_order = jnp.arange(tok_rows, dtype=jnp.int32)
    request_ids = jnp.sum((token_order[:, None] >= request_ends[None, :]).astype(jnp.int32), axis=1)
    member = request_ids[:, None] == jnp.arange(request_count, dtype=jnp.int32)[None, :]
    positions = token_order - jnp.sum(jnp.where(member, starts[None, :], 0), axis=1)
    owners = table_lookup(adapter_panel_slot, adapters) // ADP_DEV
    owner_token = jnp.sum(jnp.where(member, owners[None, :], 0), axis=1)

    states3 = normalized_hidden_states.reshape(tok_rows, serve_count, cols)
    low = jnp.einsum(
        "tsf,sorf->tor", states3, down, preferred_element_type=jnp.float32
    ).astype(jnp.bfloat16)
    owner_mask = owner_token[:, None, None] == jnp.arange(store_count, dtype=jnp.int32)[None, :, None]
    low = jnp.where(owner_mask, low, jnp.zeros((), jnp.bfloat16))
    delta_query = jnp.einsum(
        "tor,sorf->tsf", low[..., :ADAPTER_RANK], upq, preferred_element_type=jnp.float32
    ).astype(jnp.bfloat16).reshape(tok_rows, serve_count * cols)
    delta_value = jnp.einsum(
        "tor,sorf->tsf", low[..., ADAPTER_RANK:], upv, preferred_element_type=jnp.float32
    ).astype(jnp.bfloat16).reshape(tok_rows, serve_count * vcols)

    q_base = jnp.dot(
        normalized_hidden_states, query_weight_matrix, preferred_element_type=jnp.float32
    )
    k_base = jnp.dot(
        normalized_hidden_states, key_weight_matrix, preferred_element_type=jnp.float32
    )
    v_base = jnp.dot(
        normalized_hidden_states, value_weight_matrix, preferred_element_type=jnp.float32
    )
    return fused_attention(q_base, delta_query, k_base, v_base, delta_value, positions)


def _swap_halves(x):
    return jnp.concatenate([x[:, 32:64], x[:, 0:32], x[:, 96:128], x[:, 64:96]], axis=1)


def _attend_kernel(qb_ref, dq_ref, kb_ref, vb_ref, dv_ref, cos_ref, sin_ref, pos_ref, out_ref,
                   q_s, kd_s, vd_s):
    rows = qb_ref.shape[0]
    blk = 128
    n_blk = rows // blk
    q_chunks = qb_ref.shape[1] // 128
    k_chunks = kb_ref.shape[1] // 128
    lane = lax.broadcasted_iota(jnp.int32, (1, 128), 1)

    def rope_rows(r, carry):
        r0 = pl.multiple_of(r * blk, blk)
        cos = cos_ref[pl.ds(r0, blk), :]
        sin = sin_ref[pl.ds(r0, blk), :]

        def q_col(c, carry2):
            c0 = pl.multiple_of(c * 128, 128)
            x = qb_ref[pl.ds(r0, blk), pl.ds(c0, 128)] + dq_ref[pl.ds(r0, blk), pl.ds(c0, 128)].astype(jnp.float32)
            q_s[pl.ds(r0, blk), pl.ds(c0, 128)] = (x * cos + _swap_halves(x) * sin).astype(jnp.bfloat16)
            return carry2

        lax.fori_loop(0, q_chunks, q_col, 0, unroll=True)
        for c in range(k_chunks):
            x = kb_ref[pl.ds(r0, blk), c * 128:(c + 1) * 128]
            k = (x * cos + _swap_halves(x) * sin).astype(jnp.bfloat16).astype(jnp.float32)
            v = (vb_ref[pl.ds(r0, blk), c * 128:(c + 1) * 128]
                 + dv_ref[pl.ds(r0, blk), c * 128:(c + 1) * 128].astype(jnp.float32))
            v = v.astype(jnp.bfloat16).astype(jnp.float32)
            zeros = jnp.zeros((blk, 64), jnp.float32)
            for half in range(2):
                g = 2 * c + half
                kg = k[:, half * 64:(half + 1) * 64]
                vg = v[:, half * 64:(half + 1) * 64]
                kd_s[g, pl.ds(r0, blk), :] = jnp.concatenate([kg, kg], axis=1).astype(jnp.bfloat16)
                vd_s[g, pl.ds(r0, blk), 0:128] = jnp.concatenate([vg, zeros], axis=1).astype(jnp.bfloat16)
                vd_s[g, pl.ds(r0, blk), 128:256] = jnp.concatenate([zeros, vg], axis=1).astype(jnp.bfloat16)
        return carry

    lax.fori_loop(0, n_blk, rope_rows, 0)

    window = 2 * blk
    per_group = HEADS // KV_HEADS

    def query_block(b, carry):
        q0 = pl.multiple_of(b * blk, blk)
        ws = pl.multiple_of(jnp.clip(b * blk - blk, 0, rows - window), blk)
        qpos = pos_ref[pl.ds(q0, blk), :]
        qidx = q0 + lax.broadcasted_iota(jnp.int32, (blk, 1), 0)
        kidx = ws + lax.broadcasted_iota(jnp.int32, (1, window), 1)
        allowed = (kidx >= qidx - qpos) & (kidx <= qidx)

        def head_pair(j, carry2):
            g = j // (per_group // 2)
            c0 = pl.multiple_of(j * 128, 128)
            qc = q_s[pl.ds(q0, blk), pl.ds(c0, 128)]
            kd = kd_s[g, pl.ds(ws, window), :]
            vd = vd_s[g, pl.ds(ws, window), :]
            zero = jnp.zeros_like(qc)
            probs, totals = [], []
            for half in range(2):
                keep = (lane < 64) if half == 0 else (lane >= 64)
                qh = jnp.where(keep, qc, zero)
                s = lax.dot_general(qh, kd, (((1,), (1,)), ((), ())),
                                    preferred_element_type=jnp.float32) * (HEAD_DIM ** -0.5)
                s = jnp.where(allowed, s, -jnp.inf)
                m = jnp.max(s, axis=1, keepdims=True)
                p = jnp.exp(s - m)
                totals.append(jnp.sum(p, axis=1, keepdims=True))
                probs.append(p.astype(jnp.bfloat16))
            o = (jnp.dot(probs[0], vd[:, 0:128], preferred_element_type=jnp.float32)
                 + jnp.dot(probs[1], vd[:, 128:256], preferred_element_type=jnp.float32))
            o = jnp.where(lane < 64, o / totals[0], o / totals[1])
            out_ref[pl.ds(q0, blk), pl.ds(c0, 128)] = o.astype(out_ref.dtype)
            return carry2

        lax.fori_loop(0, HEADS // 2, head_pair, 0, unroll=True)
        return carry

    lax.fori_loop(0, n_blk, query_block, 0)


def rope_tables(positions):
    half_dim = HEAD_DIM // 2
    frequency = 500000.0 ** (-(jnp.arange(half_dim).astype(jnp.float32) * 2.0 / HEAD_DIM))
    angles = positions.astype(jnp.float32)[:, None] * frequency[None, :]
    cos = jnp.cos(angles)
    sin = jnp.sin(angles)
    cos_t = jnp.concatenate([cos, cos, cos, cos], axis=1)
    sin_t = jnp.concatenate([-sin, sin, -sin, sin], axis=1)
    return cos_t, sin_t


def fused_attention(q_base, delta_q, k_base, v_base, delta_v, positions):
    rows = q_base.shape[0]
    cos_t, sin_t = rope_tables(positions)
    pos_col = positions.astype(jnp.int32).reshape(rows, 1)
    vmem = pl.BlockSpec(memory_space=pltpu.VMEM)
    flops = 2 * rows * 256 * 64 * 2 * HEADS * 2
    return pl.pallas_call(
        _attend_kernel,
        out_shape=jax.ShapeDtypeStruct((rows, HEADS * HEAD_DIM), jnp.bfloat16),
        in_specs=[vmem] * 8,
        out_specs=vmem,
        scratch_shapes=[
            pltpu.VMEM((rows, HEADS * HEAD_DIM), jnp.bfloat16),
            pltpu.VMEM((KV_HEADS, rows, 128), jnp.bfloat16),
            pltpu.VMEM((KV_HEADS, rows, 256), jnp.bfloat16),
        ],
        compiler_params=pltpu.CompilerParams(vmem_limit_bytes=48 * 1024 * 1024),
        cost_estimate=pl.CostEstimate(flops=flops, transcendentals=rows * 256 * HEADS,
                                      bytes_accessed=rows * (2048 * 6 + 512 * 12 + 256 * 4)),
    )(q_base, delta_q, k_base, v_base, delta_v, cos_t, sin_t, pos_col)


def solution(mesh):
    return jax.shard_map(
        local,
        mesh=mesh,
        in_specs=(
            P(("serve", "store"), None),
            P(),
            P(),
            P(),
            P("store", None, "serve"),
            P("store", None, "serve"),
            P("store", None, "serve"),
            P(),
            P(("serve", "store"), None),
            P(("serve", "store"), None),
        ),
        out_specs=P(("serve", "store"), None),
        check_vma=False,
    )
```

```python
import jax
import jax.numpy as jnp
from jax import lax
from jax.experimental import pallas as pl
from jax.experimental.pallas import tpu as pltpu
from jax.sharding import PartitionSpec as P

HEADS = 32
KV_HEADS = 8
HEAD_DIM = 64
ADAPTER_RANK = 16
ADP_DEV = 32
LEN_MAX = 64


def rotary(heads_in, positions):
    half_dim = HEAD_DIM // 2
    frequency = 500000.0 ** (-(jnp.arange(half_dim).astype(jnp.float32) * 2.0 / HEAD_DIM))
    angles = positions.astype(jnp.float32)[:, None] * frequency[None, :]
    cosine_table = jnp.cos(angles)[:, None, :]
    sine_table = jnp.sin(angles)[:, None, :]
    first_half = heads_in[..., :half_dim]
    second_half = heads_in[..., half_dim:]
    return jnp.concatenate(
        [
            first_half * cosine_table - second_half * sine_table,
            second_half * cosine_table + first_half * sine_table,
        ],
        axis=-1,
    )


def table_lookup(table, wanted):
    entries = jnp.arange(table.shape[0], dtype=jnp.int32)
    return jnp.sum(jnp.where(wanted[..., None] == entries, table, 0), axis=-1)


def reduced_rank_products(block_list, down_panels, up_query, up_value):
    low = jnp.einsum(
        "jkd,jrd->jkr", block_list, down_panels, preferred_element_type=jnp.float32
    ).astype(jnp.bfloat16)
    query_update = jnp.einsum(
        "jkr,jrd->jkd", low[..., :ADAPTER_RANK], up_query, preferred_element_type=jnp.float32
    ).astype(jnp.bfloat16)
    value_update = jnp.einsum(
        "jkr,jrd->jkd", low[..., ADAPTER_RANK:], up_value, preferred_element_type=jnp.float32
    ).astype(jnp.bfloat16)
    return (query_update, value_update)


def local_choice(panel_set, lists, adapter_panel_slot, my_store):
    source_slots = table_lookup(adapter_panel_slot, lists)
    mine_mask = source_slots // ADP_DEV == my_store
    local_source = jnp.sum(jnp.where(mine_mask, source_slots % ADP_DEV, 0), axis=1)
    return tuple((jnp.take(panel, local_source, axis=0) for panel in panel_set))


def attention(query_rot, key_rot, value_rows, request_ids):
    tok_rows = query_rot.shape[0]
    per_group = HEADS // KV_HEADS
    block_rows = min(128, tok_rows)
    reach = LEN_MAX
    key_pad = jnp.concatenate(
        [jnp.zeros((reach,) + key_rot.shape[1:], key_rot.dtype), key_rot], axis=0
    )
    value_pad = jnp.concatenate(
        [jnp.zeros((reach,) + value_rows.shape[1:], value_rows.dtype), value_rows], axis=0
    )
    ids_pad = jnp.concatenate([jnp.full((reach,), -1, jnp.int32), request_ids], axis=0)
    token_order = jnp.arange(tok_rows, dtype=jnp.int32)
    order_pad = jnp.concatenate([jnp.full((reach,), -1, jnp.int32), token_order], axis=0)
    outputs = []
    for block_index in range(tok_rows // block_rows):
        first = block_index * block_rows
        query_block = query_rot[first : first + block_rows]
        query_ids = request_ids[first : first + block_rows]
        query_order = token_order[first : first + block_rows]
        key_block = key_pad[first : first + reach + block_rows]
        value_block = value_pad[first : first + reach + block_rows]
        key_ids = ids_pad[first : first + reach + block_rows]
        key_order = order_pad[first : first + reach + block_rows]
        allowed = (query_ids[:, None] == key_ids[None, :]) & (
            key_order[None, :] <= query_order[:, None]
        )
        pieces = []
        for group_index in range(KV_HEADS):
            query_part = query_block[:, group_index * per_group : (group_index + 1) * per_group, :]
            key_part = key_block[:, group_index, :]
            value_part = value_block[:, group_index, :]
            scores = jnp.einsum(
                "qhd,kd->hqk", query_part, key_part, preferred_element_type=jnp.float32
            ) * HEAD_DIM ** (-0.5)
            scores = jnp.where(allowed[None], scores, -jnp.inf)
            row_max = jnp.max(scores, axis=-1, keepdims=True)
            raised = jnp.exp(scores - row_max)
            row_total = jnp.sum(raised, axis=-1)
            weights = raised.astype(jnp.bfloat16)
            mixed_heads = (
                jnp.einsum("hqk,kd->qhd", weights, value_part, preferred_element_type=jnp.float32)
                / jnp.transpose(row_total)[:, :, None]
            )
            pieces.append(mixed_heads)
        outputs.append(
            jnp.concatenate(pieces, axis=1)
            .reshape(block_rows, HEADS * HEAD_DIM)
            .astype(jnp.bfloat16)
        )
    return jnp.concatenate(outputs, axis=0)


def local(
    normalized_hidden_states,
    query_weight_matrix,
    key_weight_matrix,
    value_weight_matrix,
    adapter_down_weight,
    adapter_up_query_weight,
    adapter_up_value_weight,
    adapter_panel_slot,
    adapter_per_request,
    request_token_length,
):
    axes = ("serve", "store")
    serve_count = lax.axis_size("serve")
    store_count = lax.axis_size("store")
    my_store = lax.axis_index("store")
    tok_rows, width = normalized_hidden_states.shape
    request_count = request_token_length.shape[1]
    adp_dev, rank2, cols = adapter_down_weight.shape
    vcols = adapter_up_value_weight.shape[2]
    device_total = serve_count * store_count
    all_lists = lax.all_to_all(
        jnp.broadcast_to(adapter_per_request, (device_total, request_count)), axes, 0, 0, tiled=True
    )
    all_slots = table_lookup(adapter_panel_slot, all_lists)
    mine = all_slots // ADP_DEV == my_store
    local_pick = jnp.sum(jnp.where(mine, all_slots % ADP_DEV, 0), axis=1)
    picked = [jnp.take(panel, local_pick, axis=0, mode="clip")
              for panel in (adapter_down_weight, adapter_up_query_weight, adapter_up_value_weight)]
    send = jnp.concatenate(
        [picked[0][:, :ADAPTER_RANK], picked[0][:, ADAPTER_RANK:], picked[1], picked[2]], axis=2
    )
    got = lax.all_to_all(send, axes, 0, 0, tiled=True).reshape(
        serve_count, store_count, ADAPTER_RANK, send.shape[2]
    )
    down_q = got[..., :cols]
    down_v = got[..., cols : 2 * cols]
    upq = got[..., 2 * cols : 3 * cols]
    upv = got[..., 3 * cols : 3 * cols + vcols]

    lengths = request_token_length[0]
    adapters = adapter_per_request[0]
    request_ends = jnp.cumsum(lengths)
    starts = request_ends - lengths
    token_order = jnp.arange(tok_rows, dtype=jnp.int32)
    request_ids = jnp.sum((token_order[:, None] >= request_ends[None, :]).astype(jnp.int32), axis=1)
    member = request_ids[:, None] == jnp.arange(request_count, dtype=jnp.int32)[None, :]
    positions = token_order - jnp.sum(jnp.where(member, starts[None, :], 0), axis=1)
    owners = table_lookup(adapter_panel_slot, adapters) // ADP_DEV
    owner_token = jnp.sum(jnp.where(member, owners[None, :], 0), axis=1)

    states3 = normalized_hidden_states.reshape(tok_rows, serve_count, cols)
    owner_mask = owner_token[:, None, None] == jnp.arange(store_count, dtype=jnp.int32)[None, :, None]

    def low_part(down_half):
        low = jnp.einsum(
            "tsf,sorf->tor", states3, down_half, preferred_element_type=jnp.float32
        ).astype(jnp.bfloat16)
        return jnp.where(owner_mask, low, jnp.zeros((), jnp.bfloat16))

    delta_query = jnp.einsum(
        "tor,sorf->tsf", low_part(down_q), upq, preferred_element_type=jnp.float32
    ).astype(jnp.bfloat16).reshape(tok_rows, serve_count * cols)
    delta_value = jnp.einsum(
        "tor,sorf->tsf", low_part(down_v), upv, preferred_element_type=jnp.float32
    ).astype(jnp.bfloat16).reshape(tok_rows, serve_count * vcols)

    q_base = jnp.dot(
        normalized_hidden_states, query_weight_matrix, preferred_element_type=jnp.float32
    )
    k_base = jnp.dot(
        normalized_hidden_states, key_weight_matrix, preferred_element_type=jnp.float32
    )
    v_base = jnp.dot(
        normalized_hidden_states, value_weight_matrix, preferred_element_type=jnp.float32
    )
    return fused_attention(q_base, delta_query, k_base, v_base, delta_value, positions)


def _swap_halves(x):
    return jnp.concatenate([x[:, 32:64], x[:, 0:32], x[:, 96:128], x[:, 64:96]], axis=1)


def _attend_kernel(qb_ref, dq_ref, kb_ref, vb_ref, dv_ref, cos_ref, sin_ref, pos_ref, out_ref,
                   q_s, kd_s, vd_s):
    rows = qb_ref.shape[0]
    blk = 128
    n_blk = rows // blk
    q_chunks = qb_ref.shape[1] // 128
    k_chunks = kb_ref.shape[1] // 128
    lane = lax.broadcasted_iota(jnp.int32, (1, 128), 1)

    def rope_rows(r, carry):
        r0 = pl.multiple_of(r * blk, blk)
        cos = cos_ref[pl.ds(r0, blk), :]
        sin = sin_ref[pl.ds(r0, blk), :]

        def q_col(c, carry2):
            c0 = pl.multiple_of(c * 128, 128)
            x = qb_ref[pl.ds(r0, blk), pl.ds(c0, 128)] + dq_ref[pl.ds(r0, blk), pl.ds(c0, 128)].astype(jnp.float32)
            q_s[pl.ds(r0, blk), pl.ds(c0, 128)] = (x * cos + _swap_halves(x) * sin).astype(jnp.bfloat16)
            return carry2

        lax.fori_loop(0, q_chunks, q_col, 0, unroll=True)
        for c in range(k_chunks):
            x = kb_ref[pl.ds(r0, blk), c * 128:(c + 1) * 128]
            k = (x * cos + _swap_halves(x) * sin).astype(jnp.bfloat16).astype(jnp.float32)
            v = (vb_ref[pl.ds(r0, blk), c * 128:(c + 1) * 128]
                 + dv_ref[pl.ds(r0, blk), c * 128:(c + 1) * 128].astype(jnp.float32))
            v = v.astype(jnp.bfloat16).astype(jnp.float32)
            zeros = jnp.zeros((blk, 64), jnp.float32)
            for half in range(2):
                g = 2 * c + half
                kg = k[:, half * 64:(half + 1) * 64]
                vg = v[:, half * 64:(half + 1) * 64]
                kd_s[g, pl.ds(r0, blk), :] = jnp.concatenate([kg, kg], axis=1).astype(jnp.bfloat16)
                vd_s[g, pl.ds(r0, blk), 0:128] = jnp.concatenate([vg, zeros], axis=1).astype(jnp.bfloat16)
                vd_s[g, pl.ds(r0, blk), 128:256] = jnp.concatenate([zeros, vg], axis=1).astype(jnp.bfloat16)
        return carry

    lax.fori_loop(0, n_blk, rope_rows, 0)

    window = 2 * blk
    per_group = HEADS // KV_HEADS

    def query_block(b, carry):
        q0 = pl.multiple_of(b * blk, blk)
        ws = pl.multiple_of(jnp.clip(b * blk - blk, 0, rows - window), blk)
        qpos = pos_ref[pl.ds(q0, blk), :]
        qidx = q0 + lax.broadcasted_iota(jnp.int32, (blk, 1), 0)
        kidx = ws + lax.broadcasted_iota(jnp.int32, (1, window), 1)
        allowed = (kidx >= qidx - qpos) & (kidx <= qidx)

        def head_pair(j, carry2):
            g = j // (per_group // 2)
            c0 = pl.multiple_of(j * 128, 128)
            qc = q_s[pl.ds(q0, blk), pl.ds(c0, 128)]
            kd = kd_s[g, pl.ds(ws, window), :]
            vd = vd_s[g, pl.ds(ws, window), :]
            zero = jnp.zeros_like(qc)
            probs, totals = [], []
            for half in range(2):
                keep = (lane < 64) if half == 0 else (lane >= 64)
                qh = jnp.where(keep, qc, zero)
                s = lax.dot_general(qh, kd, (((1,), (1,)), ((), ())),
                                    preferred_element_type=jnp.float32) * (HEAD_DIM ** -0.5)
                s = jnp.where(allowed, s, -jnp.inf)
                m = jnp.max(s, axis=1, keepdims=True)
                p = jnp.exp(s - m)
                totals.append(jnp.sum(p, axis=1, keepdims=True))
                probs.append(p.astype(jnp.bfloat16))
            o = (jnp.dot(probs[0], vd[:, 0:128], preferred_element_type=jnp.float32)
                 + jnp.dot(probs[1], vd[:, 128:256], preferred_element_type=jnp.float32))
            o = jnp.where(lane < 64, o / totals[0], o / totals[1])
            out_ref[pl.ds(q0, blk), pl.ds(c0, 128)] = o.astype(out_ref.dtype)
            return carry2

        lax.fori_loop(0, HEADS // 2, head_pair, 0, unroll=True)
        return carry

    lax.fori_loop(0, n_blk, query_block, 0)


def rope_tables(positions):
    half_dim = HEAD_DIM // 2
    frequency = 500000.0 ** (-(jnp.arange(half_dim).astype(jnp.float32) * 2.0 / HEAD_DIM))
    angles = positions.astype(jnp.float32)[:, None] * frequency[None, :]
    cos = jnp.cos(angles)
    sin = jnp.sin(angles)
    cos_t = jnp.concatenate([cos, cos, cos, cos], axis=1)
    sin_t = jnp.concatenate([-sin, sin, -sin, sin], axis=1)
    return cos_t, sin_t


def fused_attention(q_base, delta_q, k_base, v_base, delta_v, positions):
    rows = q_base.shape[0]
    cos_t, sin_t = rope_tables(positions)
    pos_col = positions.astype(jnp.int32).reshape(rows, 1)
    vmem = pl.BlockSpec(memory_space=pltpu.VMEM)
    flops = 2 * rows * 256 * 64 * 2 * HEADS * 2
    return pl.pallas_call(
        _attend_kernel,
        out_shape=jax.ShapeDtypeStruct((rows, HEADS * HEAD_DIM), jnp.bfloat16),
        in_specs=[vmem] * 8,
        out_specs=vmem,
        scratch_shapes=[
            pltpu.VMEM((rows, HEADS * HEAD_DIM), jnp.bfloat16),
            pltpu.VMEM((KV_HEADS, rows, 128), jnp.bfloat16),
            pltpu.VMEM((KV_HEADS, rows, 256), jnp.bfloat16),
        ],
        compiler_params=pltpu.CompilerParams(vmem_limit_bytes=48 * 1024 * 1024),
        cost_estimate=pl.CostEstimate(flops=flops, transcendentals=rows * 256 * HEADS,
                                      bytes_accessed=rows * (2048 * 6 + 512 * 12 + 256 * 4)),
    )(q_base, delta_q, k_base, v_base, delta_v, cos_t, sin_t, pos_col)


def solution(mesh):
    return jax.shard_map(
        local,
        mesh=mesh,
        in_specs=(
            P(("serve", "store"), None),
            P(),
            P(),
            P(),
            P("store", None, "serve"),
            P("store", None, "serve"),
            P("store", None, "serve"),
            P(),
            P(("serve", "store"), None),
            P(("serve", "store"), None),
        ),
        out_specs=P(("serve", "store"), None),
        check_vma=False,
    )
```

```python
import jax
import jax.numpy as jnp
from jax import lax
from jax.experimental import pallas as pl
from jax.experimental.pallas import tpu as pltpu
from jax.sharding import PartitionSpec as P

HEADS = 32
KV_HEADS = 8
HEAD_DIM = 64
ADAPTER_RANK = 16
ADP_DEV = 32
LEN_MAX = 64


def rotary(heads_in, positions):
    half_dim = HEAD_DIM // 2
    frequency = 500000.0 ** (-(jnp.arange(half_dim).astype(jnp.float32) * 2.0 / HEAD_DIM))
    angles = positions.astype(jnp.float32)[:, None] * frequency[None, :]
    cosine_table = jnp.cos(angles)[:, None, :]
    sine_table = jnp.sin(angles)[:, None, :]
    first_half = heads_in[..., :half_dim]
    second_half = heads_in[..., half_dim:]
    return jnp.concatenate(
        [
            first_half * cosine_table - second_half * sine_table,
            second_half * cosine_table + first_half * sine_table,
        ],
        axis=-1,
    )


def table_lookup(table, wanted):
    entries = jnp.arange(table.shape[0], dtype=jnp.int32)
    return jnp.sum(jnp.where(wanted[..., None] == entries, table, 0), axis=-1)


def reduced_rank_products(block_list, down_panels, up_query, up_value):
    low = jnp.einsum(
        "jkd,jrd->jkr", block_list, down_panels, preferred_element_type=jnp.float32
    ).astype(jnp.bfloat16)
    query_update = jnp.einsum(
        "jkr,jrd->jkd", low[..., :ADAPTER_RANK], up_query, preferred_element_type=jnp.float32
    ).astype(jnp.bfloat16)
    value_update = jnp.einsum(
        "jkr,jrd->jkd", low[..., ADAPTER_RANK:], up_value, preferred_element_type=jnp.float32
    ).astype(jnp.bfloat16)
    return (query_update, value_update)


def local_choice(panel_set, lists, adapter_panel_slot, my_store):
    source_slots = table_lookup(adapter_panel_slot, lists)
    mine_mask = source_slots // ADP_DEV == my_store
    local_source = jnp.sum(jnp.where(mine_mask, source_slots % ADP_DEV, 0), axis=1)
    return tuple((jnp.take(panel, local_source, axis=0) for panel in panel_set))


def attention(query_rot, key_rot, value_rows, request_ids):
    tok_rows = query_rot.shape[0]
    per_group = HEADS // KV_HEADS
    block_rows = min(128, tok_rows)
    reach = LEN_MAX
    key_pad = jnp.concatenate(
        [jnp.zeros((reach,) + key_rot.shape[1:], key_rot.dtype), key_rot], axis=0
    )
    value_pad = jnp.concatenate(
        [jnp.zeros((reach,) + value_rows.shape[1:], value_rows.dtype), value_rows], axis=0
    )
    ids_pad = jnp.concatenate([jnp.full((reach,), -1, jnp.int32), request_ids], axis=0)
    token_order = jnp.arange(tok_rows, dtype=jnp.int32)
    order_pad = jnp.concatenate([jnp.full((reach,), -1, jnp.int32), token_order], axis=0)
    outputs = []
    for block_index in range(tok_rows // block_rows):
        first = block_index * block_rows
        query_block = query_rot[first : first + block_rows]
        query_ids = request_ids[first : first + block_rows]
        query_order = token_order[first : first + block_rows]
        key_block = key_pad[first : first + reach + block_rows]
        value_block = value_pad[first : first + reach + block_rows]
        key_ids = ids_pad[first : first + reach + block_rows]
        key_order = order_pad[first : first + reach + block_rows]
        allowed = (query_ids[:, None] == key_ids[None, :]) & (
            key_order[None, :] <= query_order[:, None]
        )
        pieces = []
        for group_index in range(KV_HEADS):
            query_part = query_block[:, group_index * per_group : (group_index + 1) * per_group, :]
            key_part = key_block[:, group_index, :]
            value_part = value_block[:, group_index, :]
            scores = jnp.einsum(
                "qhd,kd->hqk", query_part, key_part, preferred_element_type=jnp.float32
            ) * HEAD_DIM ** (-0.5)
            scores = jnp.where(allowed[None], scores, -jnp.inf)
            row_max = jnp.max(scores, axis=-1, keepdims=True)
            raised = jnp.exp(scores - row_max)
            row_total = jnp.sum(raised, axis=-1)
            weights = raised.astype(jnp.bfloat16)
            mixed_heads = (
                jnp.einsum("hqk,kd->qhd", weights, value_part, preferred_element_type=jnp.float32)
                / jnp.transpose(row_total)[:, :, None]
            )
            pieces.append(mixed_heads)
        outputs.append(
            jnp.concatenate(pieces, axis=1)
            .reshape(block_rows, HEADS * HEAD_DIM)
            .astype(jnp.bfloat16)
        )
    return jnp.concatenate(outputs, axis=0)


def local(
    normalized_hidden_states,
    query_weight_matrix,
    key_weight_matrix,
    value_weight_matrix,
    adapter_down_weight,
    adapter_up_query_weight,
    adapter_up_value_weight,
    adapter_panel_slot,
    adapter_per_request,
    request_token_length,
):
    axes = ("serve", "store")
    serve_count = lax.axis_size("serve")
    store_count = lax.axis_size("store")
    my_store = lax.axis_index("store")
    tok_rows, width = normalized_hidden_states.shape
    request_count = request_token_length.shape[1]
    adp_dev, rank2, cols = adapter_down_weight.shape
    vcols = adapter_up_value_weight.shape[2]
    device_total = serve_count * store_count
    all_lists = lax.all_to_all(
        jnp.broadcast_to(adapter_per_request, (device_total, request_count)), axes, 0, 0, tiled=True
    )
    all_slots = table_lookup(adapter_panel_slot, all_lists)
    mine = all_slots // ADP_DEV == my_store
    local_pick = jnp.sum(jnp.where(mine, all_slots % ADP_DEV, 0), axis=1)
    picked = [jnp.take(panel, local_pick, axis=0, mode="clip")
              for panel in (adapter_down_weight, adapter_up_query_weight, adapter_up_value_weight)]
    send = jnp.concatenate(
        [picked[0][:, :ADAPTER_RANK], picked[0][:, ADAPTER_RANK:], picked[1], picked[2]], axis=2
    )
    got = lax.all_to_all(send, axes, 0, 0, tiled=True)

    lengths = request_token_length[0]
    adapters = adapter_per_request[0]
    request_ends = jnp.cumsum(lengths)
    starts = request_ends - lengths
    token_order = jnp.arange(tok_rows, dtype=jnp.int32)
    request_ids = jnp.sum((token_order[:, None] >= request_ends[None, :]).astype(jnp.int32), axis=1)
    member = request_ids[:, None] == jnp.arange(request_count, dtype=jnp.int32)[None, :]
    positions = token_order - jnp.sum(jnp.where(member, starts[None, :], 0), axis=1)
    owners = table_lookup(adapter_panel_slot, adapters) // ADP_DEV
    owner_token = jnp.sum(jnp.where(member, owners[None, :], 0), axis=1)

    q_base = jnp.dot(
        normalized_hidden_states, query_weight_matrix, preferred_element_type=jnp.float32
    )
    k_base = jnp.dot(
        normalized_hidden_states, key_weight_matrix, preferred_element_type=jnp.float32
    )
    v_base = jnp.dot(
        normalized_hidden_states, value_weight_matrix, preferred_element_type=jnp.float32
    )
    return fused_attention(
        q_base, k_base, v_base, normalized_hidden_states,
        got.reshape(-1, got.shape[-1]), owner_token, positions,
    )


def _swap_halves(x):
    return jnp.concatenate([x[:, 32:64], x[:, 0:32], x[:, 96:128], x[:, 64:96]], axis=1)


def _attend_kernel(qb_ref, kb_ref, vb_ref, x_ref, got_ref, own_ref, cos_ref, sin_ref, pos_ref,
                   out_ref, q_s, kd_s, vd_s, dq_ref, dv_ref):
    rows = qb_ref.shape[0]
    blk = 128
    n_blk = rows // blk
    cols = 256
    slices = x_ref.shape[1] // cols
    owner_lane = lax.broadcasted_iota(jnp.int32, (1, cols), 1) // 16

    def low_rank_rows(r, carry):
        r0 = pl.multiple_of(r * blk, blk)
        low_q = jnp.zeros((blk, cols), jnp.float32)
        low_v = jnp.zeros((blk, cols), jnp.float32)
        for sl in range(slices):
            xs = x_ref[pl.ds(r0, blk), sl * cols:(sl + 1) * cols]
            panel = got_ref[sl * cols:(sl + 1) * cols, 0:2 * cols]
            nt = (((1,), (1,)), ((), ()))
            low_q += lax.dot_general(xs, panel[:, 0:cols], nt, preferred_element_type=jnp.float32)
            low_v += lax.dot_general(xs, panel[:, cols:2 * cols], nt, preferred_element_type=jnp.float32)
        mine = owner_lane == own_ref[pl.ds(r0, blk), :]
        low_q = jnp.where(mine, low_q.astype(jnp.bfloat16), jnp.zeros((), jnp.bfloat16))
        low_v = jnp.where(mine, low_v.astype(jnp.bfloat16), jnp.zeros((), jnp.bfloat16))
        pieces = []
        for sl in range(slices):
            upq = got_ref[sl * cols:(sl + 1) * cols, 2 * cols:3 * cols]
            dq_ref[pl.ds(r0, blk), sl * cols:(sl + 1) * cols] = jnp.dot(
                low_q, upq, preferred_element_type=jnp.float32).astype(jnp.bfloat16)
            upv = got_ref[sl * cols:(sl + 1) * cols, 3 * cols:3 * cols + 64]
            pieces.append(jnp.dot(low_v, upv, preferred_element_type=jnp.float32))
        for c in range(slices // 2):
            dv_ref[pl.ds(r0, blk), c * 128:(c + 1) * 128] = jnp.concatenate(
                [pieces[2 * c], pieces[2 * c + 1]], axis=1).astype(jnp.bfloat16)
        return carry

    lax.fori_loop(0, n_blk, low_rank_rows, 0)
    q_chunks = qb_ref.shape[1] // 128
    k_chunks = kb_ref.shape[1] // 128
    lane = lax.broadcasted_iota(jnp.int32, (1, 128), 1)

    def rope_rows(r, carry):
        r0 = pl.multiple_of(r * blk, blk)
        cos = cos_ref[pl.ds(r0, blk), :]
        sin = sin_ref[pl.ds(r0, blk), :]

        def q_col(c, carry2):
            c0 = pl.multiple_of(c * 128, 128)
            x = qb_ref[pl.ds(r0, blk), pl.ds(c0, 128)] + dq_ref[pl.ds(r0, blk), pl.ds(c0, 128)].astype(jnp.float32)
            q_s[pl.ds(r0, blk), pl.ds(c0, 128)] = (x * cos + _swap_halves(x) * sin).astype(jnp.bfloat16)
            return carry2

        lax.fori_loop(0, q_chunks, q_col, 0, unroll=True)
        for c in range(k_chunks):
            x = kb_ref[pl.ds(r0, blk), c * 128:(c + 1) * 128]
            k = (x * cos + _swap_halves(x) * sin).astype(jnp.bfloat16).astype(jnp.float32)
            v = (vb_ref[pl.ds(r0, blk), c * 128:(c + 1) * 128]
                 + dv_ref[pl.ds(r0, blk), c * 128:(c + 1) * 128].astype(jnp.float32))
            v = v.astype(jnp.bfloat16).astype(jnp.float32)
            zeros = jnp.zeros((blk, 64), jnp.float32)
            for half in range(2):
                g = 2 * c + half
                kg = k[:, half * 64:(half + 1) * 64]
                vg = v[:, half * 64:(half + 1) * 64]
                kd_s[g, pl.ds(r0, blk), :] = jnp.concatenate([kg, kg], axis=1).astype(jnp.bfloat16)
                vd_s[g, pl.ds(r0, blk), 0:128] = jnp.concatenate([vg, zeros], axis=1).astype(jnp.bfloat16)
                vd_s[g, pl.ds(r0, blk), 128:256] = jnp.concatenate([zeros, vg], axis=1).astype(jnp.bfloat16)
        return carry

    lax.fori_loop(0, n_blk, rope_rows, 0)

    window = 2 * blk
    per_group = HEADS // KV_HEADS

    def query_block(b, carry):
        q0 = pl.multiple_of(b * blk, blk)
        ws = pl.multiple_of(jnp.clip(b * blk - blk, 0, rows - window), blk)
        qpos = pos_ref[pl.ds(q0, blk), :]
        qidx = q0 + lax.broadcasted_iota(jnp.int32, (blk, 1), 0)
        kidx = ws + lax.broadcasted_iota(jnp.int32, (1, window), 1)
        allowed = (kidx >= qidx - qpos) & (kidx <= qidx)

        def head_pair(j, carry2):
            g = j // (per_group // 2)
            c0 = pl.multiple_of(j * 128, 128)
            qc = q_s[pl.ds(q0, blk), pl.ds(c0, 128)]
            kd = kd_s[g, pl.ds(ws, window), :]
            vd = vd_s[g, pl.ds(ws, window), :]
            zero = jnp.zeros_like(qc)
            probs, totals = [], []
            for half in range(2):
                keep = (lane < 64) if half == 0 else (lane >= 64)
                qh = jnp.where(keep, qc, zero)
                s = lax.dot_general(qh, kd, (((1,), (1,)), ((), ())),
                                    preferred_element_type=jnp.float32) * (HEAD_DIM ** -0.5)
                s = jnp.where(allowed, s, -jnp.inf)
                m = jnp.max(s, axis=1, keepdims=True)
                p = jnp.exp(s - m)
                totals.append(jnp.sum(p, axis=1, keepdims=True))
                probs.append(p.astype(jnp.bfloat16))
            o = (jnp.dot(probs[0], vd[:, 0:128], preferred_element_type=jnp.float32)
                 + jnp.dot(probs[1], vd[:, 128:256], preferred_element_type=jnp.float32))
            o = jnp.where(lane < 64, o / totals[0], o / totals[1])
            out_ref[pl.ds(q0, blk), pl.ds(c0, 128)] = o.astype(out_ref.dtype)
            return carry2

        lax.fori_loop(0, HEADS // 2, head_pair, 0, unroll=True)
        return carry

    lax.fori_loop(0, n_blk, query_block, 0)


def rope_tables(positions):
    half_dim = HEAD_DIM // 2
    frequency = 500000.0 ** (-(jnp.arange(half_dim).astype(jnp.float32) * 2.0 / HEAD_DIM))
    angles = positions.astype(jnp.float32)[:, None] * frequency[None, :]
    cos = jnp.cos(angles)
    sin = jnp.sin(angles)
    cos_t = jnp.concatenate([cos, cos, cos, cos], axis=1)
    sin_t = jnp.concatenate([-sin, sin, -sin, sin], axis=1)
    return cos_t, sin_t


def fused_attention(q_base, k_base, v_base, states, got, owner_token, positions):
    rows = q_base.shape[0]
    cos_t, sin_t = rope_tables(positions)
    pos_col = positions.astype(jnp.int32).reshape(rows, 1)
    own_col = owner_token.astype(jnp.int32).reshape(rows, 1)
    vmem = pl.BlockSpec(memory_space=pltpu.VMEM)
    flops = 2 * rows * 256 * 64 * 2 * HEADS * 2 + 2 * rows * 256 * (2 * 2048 + 2048 + 512)
    return pl.pallas_call(
        _attend_kernel,
        out_shape=jax.ShapeDtypeStruct((rows, HEADS * HEAD_DIM), jnp.bfloat16),
        in_specs=[vmem] * 9,
        out_specs=vmem,
        scratch_shapes=[
            pltpu.VMEM((rows, HEADS * HEAD_DIM), jnp.bfloat16),
            pltpu.VMEM((KV_HEADS, rows, 128), jnp.bfloat16),
            pltpu.VMEM((KV_HEADS, rows, 256), jnp.bfloat16),
            pltpu.VMEM((rows, HEADS * HEAD_DIM), jnp.bfloat16),
            pltpu.VMEM((rows, KV_HEADS * HEAD_DIM), jnp.bfloat16),
        ],
        compiler_params=pltpu.CompilerParams(vmem_limit_bytes=48 * 1024 * 1024),
        cost_estimate=pl.CostEstimate(flops=flops, transcendentals=rows * 256 * HEADS,
                                      bytes_accessed=rows * (2048 * 8 + 512 * 8 + 256 * 4) + got.size * 2),
    )(q_base, k_base, v_base, states, got, own_col, cos_t, sin_t, pos_col)


def solution(mesh):
    return jax.shard_map(
        local,
        mesh=mesh,
        in_specs=(
            P(("serve", "store"), None),
            P(),
            P(),
            P(),
            P("store", None, "serve"),
            P("store", None, "serve"),
            P("store", None, "serve"),
            P(),
            P(("serve", "store"), None),
            P(("serve", "store"), None),
        ),
        out_specs=P(("serve", "store"), None),
        check_vma=False,
    )
```

```python
import jax
import jax.numpy as jnp
from jax import lax
from jax.experimental import pallas as pl
from jax.experimental.pallas import tpu as pltpu
from jax.sharding import PartitionSpec as P

HEADS = 32
KV_HEADS = 8
HEAD_DIM = 64
ADAPTER_RANK = 16
ADP_DEV = 32
LEN_MAX = 64


def rotary(heads_in, positions):
    half_dim = HEAD_DIM // 2
    frequency = 500000.0 ** (-(jnp.arange(half_dim).astype(jnp.float32) * 2.0 / HEAD_DIM))
    angles = positions.astype(jnp.float32)[:, None] * frequency[None, :]
    cosine_table = jnp.cos(angles)[:, None, :]
    sine_table = jnp.sin(angles)[:, None, :]
    first_half = heads_in[..., :half_dim]
    second_half = heads_in[..., half_dim:]
    return jnp.concatenate(
        [
            first_half * cosine_table - second_half * sine_table,
            second_half * cosine_table + first_half * sine_table,
        ],
        axis=-1,
    )


def table_lookup(table, wanted):
    entries = jnp.arange(table.shape[0], dtype=jnp.int32)
    return jnp.sum(jnp.where(wanted[..., None] == entries, table, 0), axis=-1)


def reduced_rank_products(block_list, down_panels, up_query, up_value):
    low = jnp.einsum(
        "jkd,jrd->jkr", block_list, down_panels, preferred_element_type=jnp.float32
    ).astype(jnp.bfloat16)
    query_update = jnp.einsum(
        "jkr,jrd->jkd", low[..., :ADAPTER_RANK], up_query, preferred_element_type=jnp.float32
    ).astype(jnp.bfloat16)
    value_update = jnp.einsum(
        "jkr,jrd->jkd", low[..., ADAPTER_RANK:], up_value, preferred_element_type=jnp.float32
    ).astype(jnp.bfloat16)
    return (query_update, value_update)


def local_choice(panel_set, lists, adapter_panel_slot, my_store):
    source_slots = table_lookup(adapter_panel_slot, lists)
    mine_mask = source_slots // ADP_DEV == my_store
    local_source = jnp.sum(jnp.where(mine_mask, source_slots % ADP_DEV, 0), axis=1)
    return tuple((jnp.take(panel, local_source, axis=0) for panel in panel_set))


def attention(query_rot, key_rot, value_rows, request_ids):
    tok_rows = query_rot.shape[0]
    per_group = HEADS // KV_HEADS
    block_rows = min(128, tok_rows)
    reach = LEN_MAX
    key_pad = jnp.concatenate(
        [jnp.zeros((reach,) + key_rot.shape[1:], key_rot.dtype), key_rot], axis=0
    )
    value_pad = jnp.concatenate(
        [jnp.zeros((reach,) + value_rows.shape[1:], value_rows.dtype), value_rows], axis=0
    )
    ids_pad = jnp.concatenate([jnp.full((reach,), -1, jnp.int32), request_ids], axis=0)
    token_order = jnp.arange(tok_rows, dtype=jnp.int32)
    order_pad = jnp.concatenate([jnp.full((reach,), -1, jnp.int32), token_order], axis=0)
    outputs = []
    for block_index in range(tok_rows // block_rows):
        first = block_index * block_rows
        query_block = query_rot[first : first + block_rows]
        query_ids = request_ids[first : first + block_rows]
        query_order = token_order[first : first + block_rows]
        key_block = key_pad[first : first + reach + block_rows]
        value_block = value_pad[first : first + reach + block_rows]
        key_ids = ids_pad[first : first + reach + block_rows]
        key_order = order_pad[first : first + reach + block_rows]
        allowed = (query_ids[:, None] == key_ids[None, :]) & (
            key_order[None, :] <= query_order[:, None]
        )
        pieces = []
        for group_index in range(KV_HEADS):
            query_part = query_block[:, group_index * per_group : (group_index + 1) * per_group, :]
            key_part = key_block[:, group_index, :]
            value_part = value_block[:, group_index, :]
            scores = jnp.einsum(
                "qhd,kd->hqk", query_part, key_part, preferred_element_type=jnp.float32
            ) * HEAD_DIM ** (-0.5)
            scores = jnp.where(allowed[None], scores, -jnp.inf)
            row_max = jnp.max(scores, axis=-1, keepdims=True)
            raised = jnp.exp(scores - row_max)
            row_total = jnp.sum(raised, axis=-1)
            weights = raised.astype(jnp.bfloat16)
            mixed_heads = (
                jnp.einsum("hqk,kd->qhd", weights, value_part, preferred_element_type=jnp.float32)
                / jnp.transpose(row_total)[:, :, None]
            )
            pieces.append(mixed_heads)
        outputs.append(
            jnp.concatenate(pieces, axis=1)
            .reshape(block_rows, HEADS * HEAD_DIM)
            .astype(jnp.bfloat16)
        )
    return jnp.concatenate(outputs, axis=0)


def local(
    normalized_hidden_states,
    query_weight_matrix,
    key_weight_matrix,
    value_weight_matrix,
    adapter_down_weight,
    adapter_up_query_weight,
    adapter_up_value_weight,
    adapter_panel_slot,
    adapter_per_request,
    request_token_length,
):
    axes = ("serve", "store")
    serve_count = lax.axis_size("serve")
    store_count = lax.axis_size("store")
    my_store = lax.axis_index("store")
    tok_rows, width = normalized_hidden_states.shape
    request_count = request_token_length.shape[1]
    adp_dev, rank2, cols = adapter_down_weight.shape
    vcols = adapter_up_value_weight.shape[2]
    device_total = serve_count * store_count
    panel_table = jnp.concatenate(
        [
            adapter_down_weight[:, :ADAPTER_RANK],
            adapter_down_weight[:, ADAPTER_RANK:],
            adapter_up_query_weight,
            adapter_up_value_weight,
        ],
        axis=2,
    )
    all_lists = lax.all_to_all(
        jnp.broadcast_to(adapter_per_request, (device_total, request_count)), axes, 0, 0, tiled=True
    )
    all_slots = jnp.take(adapter_panel_slot, all_lists.reshape(-1), mode="clip").reshape(all_lists.shape)
    mine = all_slots // ADP_DEV == my_store
    local_pick = jnp.sum(jnp.where(mine, all_slots % ADP_DEV, 0), axis=1)
    send = jnp.take(panel_table, local_pick, axis=0, mode="clip")
    got = lax.all_to_all(send, axes, 0, 0, tiled=True)

    lengths = request_token_length[0]
    adapters = adapter_per_request[0]
    request_ends = jnp.cumsum(lengths)
    starts = request_ends - lengths
    token_order = jnp.arange(tok_rows, dtype=jnp.int32)
    request_ids = jnp.sum((token_order[:, None] >= request_ends[None, :]).astype(jnp.int32), axis=1)
    member = request_ids[:, None] == jnp.arange(request_count, dtype=jnp.int32)[None, :]
    positions = token_order - jnp.sum(jnp.where(member, starts[None, :], 0), axis=1)
    owners = table_lookup(adapter_panel_slot, adapters) // ADP_DEV
    owner_token = jnp.sum(jnp.where(member, owners[None, :], 0), axis=1)

    q_base = jnp.dot(
        normalized_hidden_states, query_weight_matrix, preferred_element_type=jnp.float32
    )
    k_base = jnp.dot(
        normalized_hidden_states, key_weight_matrix, preferred_element_type=jnp.float32
    )
    v_base = jnp.dot(
        normalized_hidden_states, value_weight_matrix, preferred_element_type=jnp.float32
    )
    return fused_attention(
        q_base, k_base, v_base, normalized_hidden_states,
        got.reshape(-1, got.shape[-1]), owner_token, positions,
    )


def _swap_halves(x):
    return jnp.concatenate([x[:, 32:64], x[:, 0:32], x[:, 96:128], x[:, 64:96]], axis=1)


def _attend_kernel(qb_ref, kb_ref, vb_ref, x_ref, got_ref, own_ref, cos_ref, sin_ref, pos_ref,
                   out_ref, q_s, kd_s, vd_s, dq_ref, dv_ref):
    rows = qb_ref.shape[0]
    blk = 128
    n_blk = rows // blk
    cols = 256
    slices = x_ref.shape[1] // cols
    owner_lane = lax.broadcasted_iota(jnp.int32, (1, cols), 1) // 16

    def low_rank_rows(r, carry):
        r0 = pl.multiple_of(r * blk, blk)
        low_q = jnp.zeros((blk, cols), jnp.float32)
        low_v = jnp.zeros((blk, cols), jnp.float32)
        for sl in range(slices):
            xs = x_ref[pl.ds(r0, blk), sl * cols:(sl + 1) * cols]
            panel = got_ref[sl * cols:(sl + 1) * cols, 0:2 * cols]
            nt = (((1,), (1,)), ((), ()))
            low_q += lax.dot_general(xs, panel[:, 0:cols], nt, preferred_element_type=jnp.float32)
            low_v += lax.dot_general(xs, panel[:, cols:2 * cols], nt, preferred_element_type=jnp.float32)
        mine = owner_lane == own_ref[pl.ds(r0, blk), :]
        low_q = jnp.where(mine, low_q.astype(jnp.bfloat16), jnp.zeros((), jnp.bfloat16))
        low_v = jnp.where(mine, low_v.astype(jnp.bfloat16), jnp.zeros((), jnp.bfloat16))
        pieces = []
        for sl in range(slices):
            upq = got_ref[sl * cols:(sl + 1) * cols, 2 * cols:3 * cols]
            dq_ref[pl.ds(r0, blk), sl * cols:(sl + 1) * cols] = jnp.dot(
                low_q, upq, preferred_element_type=jnp.float32).astype(jnp.bfloat16)
            upv = got_ref[sl * cols:(sl + 1) * cols, 3 * cols:3 * cols + 64]
            pieces.append(jnp.dot(low_v, upv, preferred_element_type=jnp.float32))
        for c in range(slices // 2):
            dv_ref[pl.ds(r0, blk), c * 128:(c + 1) * 128] = jnp.concatenate(
                [pieces[2 * c], pieces[2 * c + 1]], axis=1).astype(jnp.bfloat16)
        return carry

    lax.fori_loop(0, n_blk, low_rank_rows, 0)
    q_chunks = qb_ref.shape[1] // 128
    k_chunks = kb_ref.shape[1] // 128
    lane = lax.broadcasted_iota(jnp.int32, (1, 128), 1)

    def rope_rows(r, carry):
        r0 = pl.multiple_of(r * blk, blk)
        cos = cos_ref[pl.ds(r0, blk), :]
        sin = sin_ref[pl.ds(r0, blk), :]

        def q_col(c, carry2):
            c0 = pl.multiple_of(c * 128, 128)
            x = qb_ref[pl.ds(r0, blk), pl.ds(c0, 128)] + dq_ref[pl.ds(r0, blk), pl.ds(c0, 128)].astype(jnp.float32)
            q_s[pl.ds(r0, blk), pl.ds(c0, 128)] = (x * cos + _swap_halves(x) * sin).astype(jnp.bfloat16)
            return carry2

        lax.fori_loop(0, q_chunks, q_col, 0, unroll=True)
        for c in range(k_chunks):
            x = kb_ref[pl.ds(r0, blk), c * 128:(c + 1) * 128]
            k = (x * cos + _swap_halves(x) * sin).astype(jnp.bfloat16).astype(jnp.float32)
            v = (vb_ref[pl.ds(r0, blk), c * 128:(c + 1) * 128]
                 + dv_ref[pl.ds(r0, blk), c * 128:(c + 1) * 128].astype(jnp.float32))
            v = v.astype(jnp.bfloat16).astype(jnp.float32)
            zeros = jnp.zeros((blk, 64), jnp.float32)
            for half in range(2):
                g = 2 * c + half
                kg = k[:, half * 64:(half + 1) * 64]
                vg = v[:, half * 64:(half + 1) * 64]
                kd_s[g, pl.ds(r0, blk), :] = jnp.concatenate([kg, kg], axis=1).astype(jnp.bfloat16)
                vd_s[g, pl.ds(r0, blk), 0:128] = jnp.concatenate([vg, zeros], axis=1).astype(jnp.bfloat16)
                vd_s[g, pl.ds(r0, blk), 128:256] = jnp.concatenate([zeros, vg], axis=1).astype(jnp.bfloat16)
        return carry

    lax.fori_loop(0, n_blk, rope_rows, 0)

    window = 2 * blk
    per_group = HEADS // KV_HEADS

    def query_block(b, carry):
        q0 = pl.multiple_of(b * blk, blk)
        ws = pl.multiple_of(jnp.clip(b * blk - blk, 0, rows - window), blk)
        qpos = pos_ref[pl.ds(q0, blk), :]
        qidx = q0 + lax.broadcasted_iota(jnp.int32, (blk, 1), 0)
        kidx = ws + lax.broadcasted_iota(jnp.int32, (1, window), 1)
        allowed = (kidx >= qidx - qpos) & (kidx <= qidx)

        def head_pair(j, carry2):
            g = j // (per_group // 2)
            c0 = pl.multiple_of(j * 128, 128)
            qc = q_s[pl.ds(q0, blk), pl.ds(c0, 128)]
            kd = kd_s[g, pl.ds(ws, window), :]
            vd = vd_s[g, pl.ds(ws, window), :]
            zero = jnp.zeros_like(qc)
            probs, totals = [], []
            for half in range(2):
                keep = (lane < 64) if half == 0 else (lane >= 64)
                qh = jnp.where(keep, qc, zero)
                s = lax.dot_general(qh, kd, (((1,), (1,)), ((), ())),
                                    preferred_element_type=jnp.float32) * (HEAD_DIM ** -0.5)
                s = jnp.where(allowed, s, -jnp.inf)
                m = jnp.max(s, axis=1, keepdims=True)
                p = jnp.exp(s - m)
                totals.append(jnp.sum(p, axis=1, keepdims=True))
                probs.append(p.astype(jnp.bfloat16))
            o = (jnp.dot(probs[0], vd[:, 0:128], preferred_element_type=jnp.float32)
                 + jnp.dot(probs[1], vd[:, 128:256], preferred_element_type=jnp.float32))
            o = jnp.where(lane < 64, o / totals[0], o / totals[1])
            out_ref[pl.ds(q0, blk), pl.ds(c0, 128)] = o.astype(out_ref.dtype)
            return carry2

        lax.fori_loop(0, HEADS // 2, head_pair, 0, unroll=True)
        return carry

    lax.fori_loop(0, n_blk, query_block, 0)


def rope_tables(positions):
    half_dim = HEAD_DIM // 2
    frequency = 500000.0 ** (-(jnp.arange(half_dim).astype(jnp.float32) * 2.0 / HEAD_DIM))
    angles = positions.astype(jnp.float32)[:, None] * frequency[None, :]
    cos = jnp.cos(angles)
    sin = jnp.sin(angles)
    cos_t = jnp.concatenate([cos, cos, cos, cos], axis=1)
    sin_t = jnp.concatenate([-sin, sin, -sin, sin], axis=1)
    return cos_t, sin_t


def fused_attention(q_base, k_base, v_base, states, got, owner_token, positions):
    rows = q_base.shape[0]
    cos_t, sin_t = rope_tables(positions)
    pos_col = positions.astype(jnp.int32).reshape(rows, 1)
    own_col = owner_token.astype(jnp.int32).reshape(rows, 1)
    vmem = pl.BlockSpec(memory_space=pltpu.VMEM)
    flops = 2 * rows * 256 * 64 * 2 * HEADS * 2 + 2 * rows * 256 * (2 * 2048 + 2048 + 512)
    return pl.pallas_call(
        _attend_kernel,
        out_shape=jax.ShapeDtypeStruct((rows, HEADS * HEAD_DIM), jnp.bfloat16),
        in_specs=[vmem] * 9,
        out_specs=vmem,
        scratch_shapes=[
            pltpu.VMEM((rows, HEADS * HEAD_DIM), jnp.bfloat16),
            pltpu.VMEM((KV_HEADS, rows, 128), jnp.bfloat16),
            pltpu.VMEM((KV_HEADS, rows, 256), jnp.bfloat16),
            pltpu.VMEM((rows, HEADS * HEAD_DIM), jnp.bfloat16),
            pltpu.VMEM((rows, KV_HEADS * HEAD_DIM), jnp.bfloat16),
        ],
        compiler_params=pltpu.CompilerParams(vmem_limit_bytes=48 * 1024 * 1024),
        cost_estimate=pl.CostEstimate(flops=flops, transcendentals=rows * 256 * HEADS,
                                      bytes_accessed=rows * (2048 * 8 + 512 * 8 + 256 * 4) + got.size * 2),
    )(q_base, k_base, v_base, states, got, own_col, cos_t, sin_t, pos_col)


def solution(mesh):
    return jax.shard_map(
        local,
        mesh=mesh,
        in_specs=(
            P(("serve", "store"), None),
            P(),
            P(),
            P(),
            P("store", None, "serve"),
            P("store", None, "serve"),
            P("store", None, "serve"),
            P(),
            P(("serve", "store"), None),
            P(("serve", "store"), None),
        ),
        out_specs=P(("serve", "store"), None),
        check_vma=False,
    )
```

```python
import jax
import jax.numpy as jnp
from jax import lax
from jax.experimental import pallas as pl
from jax.experimental.pallas import tpu as pltpu
from jax.sharding import PartitionSpec as P

HEADS = 32
KV_HEADS = 8
HEAD_DIM = 64
ADAPTER_RANK = 16
ADP_DEV = 32
LEN_MAX = 64


def rotary(heads_in, positions):
    half_dim = HEAD_DIM // 2
    frequency = 500000.0 ** (-(jnp.arange(half_dim).astype(jnp.float32) * 2.0 / HEAD_DIM))
    angles = positions.astype(jnp.float32)[:, None] * frequency[None, :]
    cosine_table = jnp.cos(angles)[:, None, :]
    sine_table = jnp.sin(angles)[:, None, :]
    first_half = heads_in[..., :half_dim]
    second_half = heads_in[..., half_dim:]
    return jnp.concatenate(
        [
            first_half * cosine_table - second_half * sine_table,
            second_half * cosine_table + first_half * sine_table,
        ],
        axis=-1,
    )


def table_lookup(table, wanted):
    entries = jnp.arange(table.shape[0], dtype=jnp.int32)
    return jnp.sum(jnp.where(wanted[..., None] == entries, table, 0), axis=-1)


def reduced_rank_products(block_list, down_panels, up_query, up_value):
    low = jnp.einsum(
        "jkd,jrd->jkr", block_list, down_panels, preferred_element_type=jnp.float32
    ).astype(jnp.bfloat16)
    query_update = jnp.einsum(
        "jkr,jrd->jkd", low[..., :ADAPTER_RANK], up_query, preferred_element_type=jnp.float32
    ).astype(jnp.bfloat16)
    value_update = jnp.einsum(
        "jkr,jrd->jkd", low[..., ADAPTER_RANK:], up_value, preferred_element_type=jnp.float32
    ).astype(jnp.bfloat16)
    return (query_update, value_update)


def local_choice(panel_set, lists, adapter_panel_slot, my_store):
    source_slots = table_lookup(adapter_panel_slot, lists)
    mine_mask = source_slots // ADP_DEV == my_store
    local_source = jnp.sum(jnp.where(mine_mask, source_slots % ADP_DEV, 0), axis=1)
    return tuple((jnp.take(panel, local_source, axis=0) for panel in panel_set))


def attention(query_rot, key_rot, value_rows, request_ids):
    tok_rows = query_rot.shape[0]
    per_group = HEADS // KV_HEADS
    block_rows = min(128, tok_rows)
    reach = LEN_MAX
    key_pad = jnp.concatenate(
        [jnp.zeros((reach,) + key_rot.shape[1:], key_rot.dtype), key_rot], axis=0
    )
    value_pad = jnp.concatenate(
        [jnp.zeros((reach,) + value_rows.shape[1:], value_rows.dtype), value_rows], axis=0
    )
    ids_pad = jnp.concatenate([jnp.full((reach,), -1, jnp.int32), request_ids], axis=0)
    token_order = jnp.arange(tok_rows, dtype=jnp.int32)
    order_pad = jnp.concatenate([jnp.full((reach,), -1, jnp.int32), token_order], axis=0)
    outputs = []
    for block_index in range(tok_rows // block_rows):
        first = block_index * block_rows
        query_block = query_rot[first : first + block_rows]
        query_ids = request_ids[first : first + block_rows]
        query_order = token_order[first : first + block_rows]
        key_block = key_pad[first : first + reach + block_rows]
        value_block = value_pad[first : first + reach + block_rows]
        key_ids = ids_pad[first : first + reach + block_rows]
        key_order = order_pad[first : first + reach + block_rows]
        allowed = (query_ids[:, None] == key_ids[None, :]) & (
            key_order[None, :] <= query_order[:, None]
        )
        pieces = []
        for group_index in range(KV_HEADS):
            query_part = query_block[:, group_index * per_group : (group_index + 1) * per_group, :]
            key_part = key_block[:, group_index, :]
            value_part = value_block[:, group_index, :]
            scores = jnp.einsum(
                "qhd,kd->hqk", query_part, key_part, preferred_element_type=jnp.float32
            ) * HEAD_DIM ** (-0.5)
            scores = jnp.where(allowed[None], scores, -jnp.inf)
            row_max = jnp.max(scores, axis=-1, keepdims=True)
            raised = jnp.exp(scores - row_max)
            row_total = jnp.sum(raised, axis=-1)
            weights = raised.astype(jnp.bfloat16)
            mixed_heads = (
                jnp.einsum("hqk,kd->qhd", weights, value_part, preferred_element_type=jnp.float32)
                / jnp.transpose(row_total)[:, :, None]
            )
            pieces.append(mixed_heads)
        outputs.append(
            jnp.concatenate(pieces, axis=1)
            .reshape(block_rows, HEADS * HEAD_DIM)
            .astype(jnp.bfloat16)
        )
    return jnp.concatenate(outputs, axis=0)


def local(
    normalized_hidden_states,
    query_weight_matrix,
    key_weight_matrix,
    value_weight_matrix,
    adapter_down_weight,
    adapter_up_query_weight,
    adapter_up_value_weight,
    adapter_panel_slot,
    adapter_per_request,
    request_token_length,
):
    axes = ("serve", "store")
    serve_count = lax.axis_size("serve")
    store_count = lax.axis_size("store")
    my_store = lax.axis_index("store")
    tok_rows, width = normalized_hidden_states.shape
    request_count = request_token_length.shape[1]
    adp_dev, rank2, cols = adapter_down_weight.shape
    vcols = adapter_up_value_weight.shape[2]
    device_total = serve_count * store_count
    panel_table = jnp.concatenate(
        [
            adapter_down_weight[:, :ADAPTER_RANK],
            adapter_down_weight[:, ADAPTER_RANK:],
            adapter_up_query_weight,
            adapter_up_value_weight,
        ],
        axis=2,
    )
    all_lists = lax.all_to_all(
        jnp.broadcast_to(adapter_per_request, (device_total, request_count)), axes, 0, 0, tiled=True
    )
    all_slots = table_lookup(adapter_panel_slot, all_lists)
    mine = all_slots // ADP_DEV == my_store
    local_pick = jnp.sum(jnp.where(mine, all_slots % ADP_DEV, 0), axis=1)
    send = jnp.take(panel_table, local_pick, axis=0, mode="clip")
    got = lax.all_to_all(send, axes, 0, 0, tiled=True)

    lengths = request_token_length[0]
    adapters = adapter_per_request[0]
    request_ends = jnp.cumsum(lengths)
    starts = request_ends - lengths
    token_order = jnp.arange(tok_rows, dtype=jnp.int32)
    request_ids = jnp.sum((token_order[:, None] >= request_ends[None, :]).astype(jnp.int32), axis=1)
    member = request_ids[:, None] == jnp.arange(request_count, dtype=jnp.int32)[None, :]
    positions = token_order - jnp.sum(jnp.where(member, starts[None, :], 0), axis=1)
    owners = table_lookup(adapter_panel_slot, adapters) // ADP_DEV
    owner_token = jnp.sum(jnp.where(member, owners[None, :], 0), axis=1)

    q_base = jnp.dot(
        normalized_hidden_states, query_weight_matrix, preferred_element_type=jnp.float32
    )
    k_base = jnp.dot(
        normalized_hidden_states, key_weight_matrix, preferred_element_type=jnp.float32
    )
    v_base = jnp.dot(
        normalized_hidden_states, value_weight_matrix, preferred_element_type=jnp.float32
    )
    return fused_attention(
        q_base, k_base, v_base, normalized_hidden_states,
        got.reshape(-1, got.shape[-1]), owner_token, positions,
    )


def _swap_halves(x):
    return jnp.concatenate([x[:, 32:64], x[:, 0:32], x[:, 96:128], x[:, 64:96]], axis=1)


def _attend_kernel(qb_ref, kb_ref, vb_ref, x_ref, got_ref, own_ref, cos_ref, sin_ref, pos_ref,
                   out_ref, q_s, kd_s, vd_s, dq_ref, dv_ref):
    rows = qb_ref.shape[0]
    blk = 128
    n_blk = rows // blk
    cols = 256
    slices = x_ref.shape[1] // cols
    owner_lane = lax.broadcasted_iota(jnp.int32, (1, cols), 1) // 16

    def low_rank_rows(r, carry):
        r0 = pl.multiple_of(r * blk, blk)
        low_q = jnp.zeros((blk, cols), jnp.float32)
        low_v = jnp.zeros((blk, cols), jnp.float32)
        for sl in range(slices):
            xs = x_ref[pl.ds(r0, blk), sl * cols:(sl + 1) * cols]
            panel = got_ref[sl * cols:(sl + 1) * cols, 0:2 * cols]
            nt = (((1,), (1,)), ((), ()))
            low_q += lax.dot_general(xs, panel[:, 0:cols], nt, preferred_element_type=jnp.float32)
            low_v += lax.dot_general(xs, panel[:, cols:2 * cols], nt, preferred_element_type=jnp.float32)
        mine = owner_lane == own_ref[pl.ds(r0, blk), :]
        low_q = jnp.where(mine, low_q.astype(jnp.bfloat16), jnp.zeros((), jnp.bfloat16))
        low_v = jnp.where(mine, low_v.astype(jnp.bfloat16), jnp.zeros((), jnp.bfloat16))
        pieces = []
        for sl in range(slices):
            upq = got_ref[sl * cols:(sl + 1) * cols, 2 * cols:3 * cols]
            dq_ref[pl.ds(r0, blk), sl * cols:(sl + 1) * cols] = jnp.dot(
                low_q, upq, preferred_element_type=jnp.float32).astype(jnp.bfloat16)
            upv = got_ref[sl * cols:(sl + 1) * cols, 3 * cols:3 * cols + 64]
            pieces.append(jnp.dot(low_v, upv, preferred_element_type=jnp.float32))
        for c in range(slices // 2):
            dv_ref[pl.ds(r0, blk), c * 128:(c + 1) * 128] = jnp.concatenate(
                [pieces[2 * c], pieces[2 * c + 1]], axis=1).astype(jnp.bfloat16)
        return carry

    lax.fori_loop(0, n_blk, low_rank_rows, 0)
    q_chunks = qb_ref.shape[1] // 128
    k_chunks = kb_ref.shape[1] // 128
    lane = lax.broadcasted_iota(jnp.int32, (1, 128), 1)

    def rope_rows(r, carry):
        r0 = pl.multiple_of(r * blk, blk)
        cos = cos_ref[pl.ds(r0, blk), :]
        sin = sin_ref[pl.ds(r0, blk), :]

        def q_col(c, carry2):
            c0 = pl.multiple_of(c * 128, 128)
            x = qb_ref[pl.ds(r0, blk), pl.ds(c0, 128)] + dq_ref[pl.ds(r0, blk), pl.ds(c0, 128)].astype(jnp.float32)
            q_s[pl.ds(r0, blk), pl.ds(c0, 128)] = (x * cos + _swap_halves(x) * sin).astype(jnp.bfloat16)
            return carry2

        lax.fori_loop(0, q_chunks, q_col, 0, unroll=True)
        for c in range(k_chunks):
            x = kb_ref[pl.ds(r0, blk), c * 128:(c + 1) * 128]
            k = (x * cos + _swap_halves(x) * sin).astype(jnp.bfloat16).astype(jnp.float32)
            v = (vb_ref[pl.ds(r0, blk), c * 128:(c + 1) * 128]
                 + dv_ref[pl.ds(r0, blk), c * 128:(c + 1) * 128].astype(jnp.float32))
            v = v.astype(jnp.bfloat16).astype(jnp.float32)
            zeros = jnp.zeros((blk, 64), jnp.float32)
            for half in range(2):
                g = 2 * c + half
                kg = k[:, half * 64:(half + 1) * 64]
                vg = v[:, half * 64:(half + 1) * 64]
                kd_s[g, pl.ds(r0, blk), :] = jnp.concatenate([kg, kg], axis=1).astype(jnp.bfloat16)
                vd_s[g, pl.ds(r0, blk), 0:128] = jnp.concatenate([vg, zeros], axis=1).astype(jnp.bfloat16)
                vd_s[g, pl.ds(r0, blk), 128:256] = jnp.concatenate([zeros, vg], axis=1).astype(jnp.bfloat16)
        return carry

    lax.fori_loop(0, n_blk, rope_rows, 0)

    window = 2 * blk
    per_group = HEADS // KV_HEADS

    def query_block(b, carry):
        q0 = pl.multiple_of(b * blk, blk)
        ws = pl.multiple_of(jnp.clip(b * blk - blk, 0, rows - window), blk)
        qpos = pos_ref[pl.ds(q0, blk), :]
        qidx = q0 + lax.broadcasted_iota(jnp.int32, (blk, 1), 0)
        kidx = ws + lax.broadcasted_iota(jnp.int32, (1, window), 1)
        allowed = (kidx >= qidx - qpos) & (kidx <= qidx)

        def head_pair(j, carry2):
            g = j // (per_group // 2)
            c0 = pl.multiple_of(j * 128, 128)
            qc = q_s[pl.ds(q0, blk), pl.ds(c0, 128)]
            kd = kd_s[g, pl.ds(ws, window), :]
            vd = vd_s[g, pl.ds(ws, window), :]
            zero = jnp.zeros_like(qc)
            probs, totals = [], []
            for half in range(2):
                keep = (lane < 64) if half == 0 else (lane >= 64)
                qh = jnp.where(keep, qc, zero)
                s = lax.dot_general(qh, kd, (((1,), (1,)), ((), ())),
                                    preferred_element_type=jnp.float32) * (HEAD_DIM ** -0.5)
                s = jnp.where(allowed, s, -jnp.inf)
                m = jnp.max(s, axis=1, keepdims=True)
                p = jnp.exp(s - m)
                totals.append(jnp.sum(p, axis=1, keepdims=True))
                probs.append(p.astype(jnp.bfloat16))
            o = (jnp.dot(probs[0], vd[:, 0:128], preferred_element_type=jnp.float32)
                 + jnp.dot(probs[1], vd[:, 128:256], preferred_element_type=jnp.float32))
            o = jnp.where(lane < 64, o / totals[0], o / totals[1])
            out_ref[pl.ds(q0, blk), pl.ds(c0, 128)] = o.astype(out_ref.dtype)
            return carry2

        lax.fori_loop(0, HEADS // 2, head_pair, 0, unroll=True)
        return carry

    lax.fori_loop(0, n_blk, query_block, 0)


def rope_tables(positions):
    half_dim = HEAD_DIM // 2
    frequency = 500000.0 ** (-(jnp.arange(half_dim).astype(jnp.float32) * 2.0 / HEAD_DIM))
    angles = positions.astype(jnp.float32)[:, None] * frequency[None, :]
    cos = jnp.cos(angles)
    sin = jnp.sin(angles)
    cos_t = jnp.concatenate([cos, cos, cos, cos], axis=1)
    sin_t = jnp.concatenate([-sin, sin, -sin, sin], axis=1)
    return cos_t, sin_t


def fused_attention(q_base, k_base, v_base, states, got, owner_token, positions):
    rows = q_base.shape[0]
    cos_t, sin_t = rope_tables(positions)
    pos_col = positions.astype(jnp.int32).reshape(rows, 1)
    own_col = owner_token.astype(jnp.int32).reshape(rows, 1)
    vmem = pl.BlockSpec(memory_space=pltpu.VMEM)
    flops = 2 * rows * 256 * 64 * 2 * HEADS * 2 + 2 * rows * 256 * (2 * 2048 + 2048 + 512)
    return pl.pallas_call(
        _attend_kernel,
        out_shape=jax.ShapeDtypeStruct((rows, HEADS * HEAD_DIM), jnp.bfloat16),
        in_specs=[vmem] * 9,
        out_specs=vmem,
        scratch_shapes=[
            pltpu.VMEM((rows, HEADS * HEAD_DIM), jnp.bfloat16),
            pltpu.VMEM((KV_HEADS, rows, 128), jnp.bfloat16),
            pltpu.VMEM((KV_HEADS, rows, 256), jnp.bfloat16),
            pltpu.VMEM((rows, HEADS * HEAD_DIM), jnp.bfloat16),
            pltpu.VMEM((rows, KV_HEADS * HEAD_DIM), jnp.bfloat16),
        ],
        compiler_params=pltpu.CompilerParams(vmem_limit_bytes=48 * 1024 * 1024),
        cost_estimate=pl.CostEstimate(flops=flops, transcendentals=rows * 256 * HEADS,
                                      bytes_accessed=rows * (2048 * 8 + 512 * 8 + 256 * 4) + got.size * 2),
    )(q_base, k_base, v_base, states, got, own_col, cos_t, sin_t, pos_col)


def solution(mesh):
    return jax.shard_map(
        local,
        mesh=mesh,
        in_specs=(
            P(("serve", "store"), None),
            P(),
            P(),
            P(),
            P("store", None, "serve"),
            P("store", None, "serve"),
            P("store", None, "serve"),
            P(),
            P(("serve", "store"), None),
            P(("serve", "store"), None),
        ),
        out_specs=P(("serve", "store"), None),
        check_vma=False,
    )
```

```python
import jax
import jax.numpy as jnp
from jax import lax
from jax.experimental import pallas as pl
from jax.experimental.pallas import tpu as pltpu
from jax.sharding import PartitionSpec as P

HEADS = 32
KV_HEADS = 8
HEAD_DIM = 64
ADAPTER_RANK = 16
ADP_DEV = 32
LEN_MAX = 64


def rotary(heads_in, positions):
    half_dim = HEAD_DIM // 2
    frequency = 500000.0 ** (-(jnp.arange(half_dim).astype(jnp.float32) * 2.0 / HEAD_DIM))
    angles = positions.astype(jnp.float32)[:, None] * frequency[None, :]
    cosine_table = jnp.cos(angles)[:, None, :]
    sine_table = jnp.sin(angles)[:, None, :]
    first_half = heads_in[..., :half_dim]
    second_half = heads_in[..., half_dim:]
    return jnp.concatenate(
        [
            first_half * cosine_table - second_half * sine_table,
            second_half * cosine_table + first_half * sine_table,
        ],
        axis=-1,
    )


def table_lookup(table, wanted):
    entries = jnp.arange(table.shape[0], dtype=jnp.int32)
    return jnp.sum(jnp.where(wanted[..., None] == entries, table, 0), axis=-1)


def reduced_rank_products(block_list, down_panels, up_query, up_value):
    low = jnp.einsum(
        "jkd,jrd->jkr", block_list, down_panels, preferred_element_type=jnp.float32
    ).astype(jnp.bfloat16)
    query_update = jnp.einsum(
        "jkr,jrd->jkd", low[..., :ADAPTER_RANK], up_query, preferred_element_type=jnp.float32
    ).astype(jnp.bfloat16)
    value_update = jnp.einsum(
        "jkr,jrd->jkd", low[..., ADAPTER_RANK:], up_value, preferred_element_type=jnp.float32
    ).astype(jnp.bfloat16)
    return (query_update, value_update)


def local_choice(panel_set, lists, adapter_panel_slot, my_store):
    source_slots = table_lookup(adapter_panel_slot, lists)
    mine_mask = source_slots // ADP_DEV == my_store
    local_source = jnp.sum(jnp.where(mine_mask, source_slots % ADP_DEV, 0), axis=1)
    return tuple((jnp.take(panel, local_source, axis=0) for panel in panel_set))


def attention(query_rot, key_rot, value_rows, request_ids):
    tok_rows = query_rot.shape[0]
    per_group = HEADS // KV_HEADS
    block_rows = min(128, tok_rows)
    reach = LEN_MAX
    key_pad = jnp.concatenate(
        [jnp.zeros((reach,) + key_rot.shape[1:], key_rot.dtype), key_rot], axis=0
    )
    value_pad = jnp.concatenate(
        [jnp.zeros((reach,) + value_rows.shape[1:], value_rows.dtype), value_rows], axis=0
    )
    ids_pad = jnp.concatenate([jnp.full((reach,), -1, jnp.int32), request_ids], axis=0)
    token_order = jnp.arange(tok_rows, dtype=jnp.int32)
    order_pad = jnp.concatenate([jnp.full((reach,), -1, jnp.int32), token_order], axis=0)
    outputs = []
    for block_index in range(tok_rows // block_rows):
        first = block_index * block_rows
        query_block = query_rot[first : first + block_rows]
        query_ids = request_ids[first : first + block_rows]
        query_order = token_order[first : first + block_rows]
        key_block = key_pad[first : first + reach + block_rows]
        value_block = value_pad[first : first + reach + block_rows]
        key_ids = ids_pad[first : first + reach + block_rows]
        key_order = order_pad[first : first + reach + block_rows]
        allowed = (query_ids[:, None] == key_ids[None, :]) & (
            key_order[None, :] <= query_order[:, None]
        )
        pieces = []
        for group_index in range(KV_HEADS):
            query_part = query_block[:, group_index * per_group : (group_index + 1) * per_group, :]
            key_part = key_block[:, group_index, :]
            value_part = value_block[:, group_index, :]
            scores = jnp.einsum(
                "qhd,kd->hqk", query_part, key_part, preferred_element_type=jnp.float32
            ) * HEAD_DIM ** (-0.5)
            scores = jnp.where(allowed[None], scores, -jnp.inf)
            row_max = jnp.max(scores, axis=-1, keepdims=True)
            raised = jnp.exp(scores - row_max)
            row_total = jnp.sum(raised, axis=-1)
            weights = raised.astype(jnp.bfloat16)
            mixed_heads = (
                jnp.einsum("hqk,kd->qhd", weights, value_part, preferred_element_type=jnp.float32)
                / jnp.transpose(row_total)[:, :, None]
            )
            pieces.append(mixed_heads)
        outputs.append(
            jnp.concatenate(pieces, axis=1)
            .reshape(block_rows, HEADS * HEAD_DIM)
            .astype(jnp.bfloat16)
        )
    return jnp.concatenate(outputs, axis=0)


def local(
    normalized_hidden_states,
    query_weight_matrix,
    key_weight_matrix,
    value_weight_matrix,
    adapter_down_weight,
    adapter_up_query_weight,
    adapter_up_value_weight,
    adapter_panel_slot,
    adapter_per_request,
    request_token_length,
):
    axes = ("serve", "store")
    serve_count = lax.axis_size("serve")
    store_count = lax.axis_size("store")
    my_store = lax.axis_index("store")
    tok_rows, width = normalized_hidden_states.shape
    request_count = request_token_length.shape[1]
    adp_dev, rank2, cols = adapter_down_weight.shape
    vcols = adapter_up_value_weight.shape[2]
    device_total = serve_count * store_count
    panel_table = jnp.concatenate(
        [
            adapter_down_weight[:, :ADAPTER_RANK],
            adapter_down_weight[:, ADAPTER_RANK:],
            adapter_up_query_weight,
            adapter_up_value_weight,
        ],
        axis=2,
    )
    all_lists = lax.all_to_all(
        jnp.broadcast_to(adapter_per_request, (device_total, request_count)), axes, 0, 0, tiled=True
    )
    all_slots = table_lookup(adapter_panel_slot, all_lists)
    mine = all_slots // ADP_DEV == my_store
    local_pick = jnp.sum(jnp.where(mine, all_slots % ADP_DEV, 0), axis=1)
    send = jnp.take(panel_table, local_pick, axis=0, mode="clip")
    got = lax.all_to_all(send, axes, 0, 0, tiled=True)

    lengths = request_token_length[0]
    adapters = adapter_per_request[0]
    request_ends = jnp.cumsum(lengths)
    starts = request_ends - lengths
    token_order = jnp.arange(tok_rows, dtype=jnp.int32)
    request_ids = jnp.sum((token_order[:, None] >= request_ends[None, :]).astype(jnp.int32), axis=1)
    member = request_ids[:, None] == jnp.arange(request_count, dtype=jnp.int32)[None, :]
    positions = token_order - jnp.sum(jnp.where(member, starts[None, :], 0), axis=1)
    owners = table_lookup(adapter_panel_slot, adapters) // ADP_DEV
    owner_token = jnp.sum(jnp.where(member, owners[None, :], 0), axis=1)

    q_base = jnp.dot(
        normalized_hidden_states, query_weight_matrix, preferred_element_type=jnp.float32
    )
    k_base = jnp.dot(
        normalized_hidden_states, key_weight_matrix, preferred_element_type=jnp.float32
    )
    v_base = jnp.dot(
        normalized_hidden_states, value_weight_matrix, preferred_element_type=jnp.float32
    )
    return fused_attention(
        q_base, k_base, v_base, normalized_hidden_states,
        got.reshape(-1, got.shape[-1]), owner_token, positions,
    )


def _swap_halves(x):
    return jnp.concatenate([x[:, 32:64], x[:, 0:32], x[:, 96:128], x[:, 64:96]], axis=1)


def _attend_kernel(qb_ref, kb_ref, vb_ref, x_ref, got_ref, own_ref, cos_ref, sin_ref, pos_ref,
                   out_ref, q_s, kd_s, vd_s, dq_ref, dv_ref):
    blk = qb_ref.shape[0]
    rows = kd_s.shape[1]
    b = pl.program_id(0)
    g0 = pl.multiple_of(b * blk, blk)
    cols = 256
    slices = x_ref.shape[1] // cols
    q_chunks = qb_ref.shape[1] // 128
    k_chunks = kb_ref.shape[1] // 128
    lane = lax.broadcasted_iota(jnp.int32, (1, 128), 1)
    owner_lane = lax.broadcasted_iota(jnp.int32, (1, cols), 1) // 16

    @pl.when(b == 0)
    def _():
        kd_s[:, blk:2 * blk, :] = jnp.zeros((kd_s.shape[0], blk, kd_s.shape[2]), kd_s.dtype)
        vd_s[:, blk:2 * blk, :] = jnp.zeros((vd_s.shape[0], blk, vd_s.shape[2]), vd_s.dtype)

    low_q = jnp.zeros((blk, cols), jnp.float32)
    low_v = jnp.zeros((blk, cols), jnp.float32)
    nt = (((1,), (1,)), ((), ()))
    for sl in range(slices):
        xs = x_ref[:, sl * cols:(sl + 1) * cols]
        panel = got_ref[sl * cols:(sl + 1) * cols, 0:2 * cols]
        low_q += lax.dot_general(xs, panel[:, 0:cols], nt, preferred_element_type=jnp.float32)
        low_v += lax.dot_general(xs, panel[:, cols:2 * cols], nt, preferred_element_type=jnp.float32)
    mine = owner_lane == own_ref[...]
    low_q = jnp.where(mine, low_q.astype(jnp.bfloat16), jnp.zeros((), jnp.bfloat16))
    low_v = jnp.where(mine, low_v.astype(jnp.bfloat16), jnp.zeros((), jnp.bfloat16))
    pieces = []
    for sl in range(slices):
        upq = got_ref[sl * cols:(sl + 1) * cols, 2 * cols:3 * cols]
        dq_ref[:, sl * cols:(sl + 1) * cols] = jnp.dot(
            low_q, upq, preferred_element_type=jnp.float32).astype(jnp.bfloat16)
        upv = got_ref[sl * cols:(sl + 1) * cols, 3 * cols:3 * cols + 64]
        pieces.append(jnp.dot(low_v, upv, preferred_element_type=jnp.float32))
    for c in range(slices // 2):
        dv_ref[:, c * 128:(c + 1) * 128] = jnp.concatenate(
            [pieces[2 * c], pieces[2 * c + 1]], axis=1).astype(jnp.bfloat16)

    cos = cos_ref[...]
    sin = sin_ref[...]

    def q_col(c, carry2):
        c0 = pl.multiple_of(c * 128, 128)
        x = qb_ref[:, pl.ds(c0, 128)] + dq_ref[:, pl.ds(c0, 128)].astype(jnp.float32)
        q_s[:, pl.ds(c0, 128)] = (x * cos + _swap_halves(x) * sin).astype(jnp.bfloat16)
        return carry2

    lax.fori_loop(0, q_chunks, q_col, 0, unroll=True)
    zeros = jnp.zeros((blk, 64), jnp.float32)
    for c in range(k_chunks):
        x = kb_ref[:, c * 128:(c + 1) * 128]
        k = (x * cos + _swap_halves(x) * sin).astype(jnp.bfloat16).astype(jnp.float32)
        v = vb_ref[:, c * 128:(c + 1) * 128] + dv_ref[:, c * 128:(c + 1) * 128].astype(jnp.float32)
        v = v.astype(jnp.bfloat16).astype(jnp.float32)
        for half in range(2):
            g = 2 * c + half
            kg = k[:, half * 64:(half + 1) * 64]
            vg = v[:, half * 64:(half + 1) * 64]
            kd_s[g, pl.ds(g0, blk), :] = jnp.concatenate([kg, kg], axis=1).astype(jnp.bfloat16)
            vd_s[g, pl.ds(g0, blk), 0:128] = jnp.concatenate([vg, zeros], axis=1).astype(jnp.bfloat16)
            vd_s[g, pl.ds(g0, blk), 128:256] = jnp.concatenate([zeros, vg], axis=1).astype(jnp.bfloat16)

    window = 2 * blk
    per_group = HEADS // KV_HEADS
    ws = pl.multiple_of(jnp.clip(g0 - blk, 0, rows - window), blk)
    qpos = pos_ref[...]
    qidx = g0 + lax.broadcasted_iota(jnp.int32, (blk, 1), 0)
    kidx = ws + lax.broadcasted_iota(jnp.int32, (1, window), 1)
    allowed = (kidx >= qidx - qpos) & (kidx <= qidx)

    def head_pair(j, carry2):
        g = j // (per_group // 2)
        c0 = pl.multiple_of(j * 128, 128)
        qc = q_s[:, pl.ds(c0, 128)]
        kd = kd_s[g, pl.ds(ws, window), :]
        vd = vd_s[g, pl.ds(ws, window), :]
        zero = jnp.zeros_like(qc)
        probs, totals = [], []
        for half in range(2):
            keep = (lane < 64) if half == 0 else (lane >= 64)
            qh = jnp.where(keep, qc, zero)
            s = lax.dot_general(qh, kd, nt, preferred_element_type=jnp.float32) * (HEAD_DIM ** -0.5)
            s = jnp.where(allowed, s, -jnp.inf)
            m = jnp.max(s, axis=1, keepdims=True)
            p = jnp.exp(s - m)
            totals.append(jnp.sum(p, axis=1, keepdims=True))
            probs.append(p.astype(jnp.bfloat16))
        o = (jnp.dot(probs[0], vd[:, 0:128], preferred_element_type=jnp.float32)
             + jnp.dot(probs[1], vd[:, 128:256], preferred_element_type=jnp.float32))
        o = jnp.where(lane < 64, o / totals[0], o / totals[1])
        out_ref[:, pl.ds(c0, 128)] = o.astype(out_ref.dtype)
        return carry2

    lax.fori_loop(0, HEADS // 2, head_pair, 0, unroll=True)


def rope_tables(positions):
    half_dim = HEAD_DIM // 2
    frequency = 500000.0 ** (-(jnp.arange(half_dim).astype(jnp.float32) * 2.0 / HEAD_DIM))
    angles = positions.astype(jnp.float32)[:, None] * frequency[None, :]
    cos = jnp.cos(angles)
    sin = jnp.sin(angles)
    cos_t = jnp.concatenate([cos, cos, cos, cos], axis=1)
    sin_t = jnp.concatenate([-sin, sin, -sin, sin], axis=1)
    return cos_t, sin_t


def fused_attention(q_base, k_base, v_base, states, got, owner_token, positions):
    rows = q_base.shape[0]
    cos_t, sin_t = rope_tables(positions)
    pos_col = positions.astype(jnp.int32).reshape(rows, 1)
    own_col = owner_token.astype(jnp.int32).reshape(rows, 1)
    flops = 2 * rows * 256 * 64 * 2 * HEADS * 2 + 2 * rows * 256 * (2 * 2048 + 2048 + 512)
    blk = 128
    row_block = lambda width: pl.BlockSpec((blk, width), lambda b: (b, 0))
    return pl.pallas_call(
        _attend_kernel,
        out_shape=jax.ShapeDtypeStruct((rows, HEADS * HEAD_DIM), jnp.bfloat16),
        grid=(rows // blk,),
        in_specs=[
            row_block(q_base.shape[1]),
            row_block(k_base.shape[1]),
            row_block(v_base.shape[1]),
            row_block(states.shape[1]),
            pl.BlockSpec(got.shape, lambda b: (0, 0)),
            row_block(1),
            row_block(128),
            row_block(128),
            row_block(1),
        ],
        out_specs=row_block(HEADS * HEAD_DIM),
        scratch_shapes=[
            pltpu.VMEM((blk, HEADS * HEAD_DIM), jnp.bfloat16),
            pltpu.VMEM((KV_HEADS, rows, 128), jnp.bfloat16),
            pltpu.VMEM((KV_HEADS, rows, 256), jnp.bfloat16),
            pltpu.VMEM((blk, HEADS * HEAD_DIM), jnp.bfloat16),
            pltpu.VMEM((blk, KV_HEADS * HEAD_DIM), jnp.bfloat16),
        ],
        compiler_params=pltpu.CompilerParams(
            dimension_semantics=("arbitrary",), vmem_limit_bytes=48 * 1024 * 1024
        ),
        cost_estimate=pl.CostEstimate(flops=flops, transcendentals=rows * 256 * HEADS,
                                      bytes_accessed=rows * (2048 * 8 + 512 * 8 + 256 * 4) + got.size * 2),
    )(q_base, k_base, v_base, states, got, own_col, cos_t, sin_t, pos_col)


def solution(mesh):
    return jax.shard_map(
        local,
        mesh=mesh,
        in_specs=(
            P(("serve", "store"), None),
            P(),
            P(),
            P(),
            P("store", None, "serve"),
            P("store", None, "serve"),
            P("store", None, "serve"),
            P(),
            P(("serve", "store"), None),
            P(("serve", "store"), None),
        ),
        out_specs=P(("serve", "store"), None),
        check_vma=False,
    )
```

```python
import jax
import jax.numpy as jnp
from jax import lax
from jax.experimental import pallas as pl
from jax.experimental.pallas import tpu as pltpu
from jax.sharding import PartitionSpec as P

HEADS = 32
KV_HEADS = 8
HEAD_DIM = 64
ADAPTER_RANK = 16
ADP_DEV = 32
LEN_MAX = 64


def rotary(heads_in, positions):
    half_dim = HEAD_DIM // 2
    frequency = 500000.0 ** (-(jnp.arange(half_dim).astype(jnp.float32) * 2.0 / HEAD_DIM))
    angles = positions.astype(jnp.float32)[:, None] * frequency[None, :]
    cosine_table = jnp.cos(angles)[:, None, :]
    sine_table = jnp.sin(angles)[:, None, :]
    first_half = heads_in[..., :half_dim]
    second_half = heads_in[..., half_dim:]
    return jnp.concatenate(
        [
            first_half * cosine_table - second_half * sine_table,
            second_half * cosine_table + first_half * sine_table,
        ],
        axis=-1,
    )


def table_lookup(table, wanted):
    entries = jnp.arange(table.shape[0], dtype=jnp.int32)
    return jnp.sum(jnp.where(wanted[..., None] == entries, table, 0), axis=-1)


def reduced_rank_products(block_list, down_panels, up_query, up_value):
    low = jnp.einsum(
        "jkd,jrd->jkr", block_list, down_panels, preferred_element_type=jnp.float32
    ).astype(jnp.bfloat16)
    query_update = jnp.einsum(
        "jkr,jrd->jkd", low[..., :ADAPTER_RANK], up_query, preferred_element_type=jnp.float32
    ).astype(jnp.bfloat16)
    value_update = jnp.einsum(
        "jkr,jrd->jkd", low[..., ADAPTER_RANK:], up_value, preferred_element_type=jnp.float32
    ).astype(jnp.bfloat16)
    return (query_update, value_update)


def local_choice(panel_set, lists, adapter_panel_slot, my_store):
    source_slots = table_lookup(adapter_panel_slot, lists)
    mine_mask = source_slots // ADP_DEV == my_store
    local_source = jnp.sum(jnp.where(mine_mask, source_slots % ADP_DEV, 0), axis=1)
    return tuple((jnp.take(panel, local_source, axis=0) for panel in panel_set))


def attention(query_rot, key_rot, value_rows, request_ids):
    tok_rows = query_rot.shape[0]
    per_group = HEADS // KV_HEADS
    block_rows = min(128, tok_rows)
    reach = LEN_MAX
    key_pad = jnp.concatenate(
        [jnp.zeros((reach,) + key_rot.shape[1:], key_rot.dtype), key_rot], axis=0
    )
    value_pad = jnp.concatenate(
        [jnp.zeros((reach,) + value_rows.shape[1:], value_rows.dtype), value_rows], axis=0
    )
    ids_pad = jnp.concatenate([jnp.full((reach,), -1, jnp.int32), request_ids], axis=0)
    token_order = jnp.arange(tok_rows, dtype=jnp.int32)
    order_pad = jnp.concatenate([jnp.full((reach,), -1, jnp.int32), token_order], axis=0)
    outputs = []
    for block_index in range(tok_rows // block_rows):
        first = block_index * block_rows
        query_block = query_rot[first : first + block_rows]
        query_ids = request_ids[first : first + block_rows]
        query_order = token_order[first : first + block_rows]
        key_block = key_pad[first : first + reach + block_rows]
        value_block = value_pad[first : first + reach + block_rows]
        key_ids = ids_pad[first : first + reach + block_rows]
        key_order = order_pad[first : first + reach + block_rows]
        allowed = (query_ids[:, None] == key_ids[None, :]) & (
            key_order[None, :] <= query_order[:, None]
        )
        pieces = []
        for group_index in range(KV_HEADS):
            query_part = query_block[:, group_index * per_group : (group_index + 1) * per_group, :]
            key_part = key_block[:, group_index, :]
            value_part = value_block[:, group_index, :]
            scores = jnp.einsum(
                "qhd,kd->hqk", query_part, key_part, preferred_element_type=jnp.float32
            ) * HEAD_DIM ** (-0.5)
            scores = jnp.where(allowed[None], scores, -jnp.inf)
            row_max = jnp.max(scores, axis=-1, keepdims=True)
            raised = jnp.exp(scores - row_max)
            row_total = jnp.sum(raised, axis=-1)
            weights = raised.astype(jnp.bfloat16)
            mixed_heads = (
                jnp.einsum("hqk,kd->qhd", weights, value_part, preferred_element_type=jnp.float32)
                / jnp.transpose(row_total)[:, :, None]
            )
            pieces.append(mixed_heads)
        outputs.append(
            jnp.concatenate(pieces, axis=1)
            .reshape(block_rows, HEADS * HEAD_DIM)
            .astype(jnp.bfloat16)
        )
    return jnp.concatenate(outputs, axis=0)


def local(
    normalized_hidden_states,
    query_weight_matrix,
    key_weight_matrix,
    value_weight_matrix,
    adapter_down_weight,
    adapter_up_query_weight,
    adapter_up_value_weight,
    adapter_panel_slot,
    adapter_per_request,
    request_token_length,
):
    axes = ("serve", "store")
    serve_count = lax.axis_size("serve")
    store_count = lax.axis_size("store")
    my_store = lax.axis_index("store")
    tok_rows, width = normalized_hidden_states.shape
    request_count = request_token_length.shape[1]
    adp_dev, rank2, cols = adapter_down_weight.shape
    vcols = adapter_up_value_weight.shape[2]
    device_total = serve_count * store_count
    panel_table = jnp.concatenate(
        [
            adapter_down_weight[:, :ADAPTER_RANK],
            adapter_down_weight[:, ADAPTER_RANK:],
            adapter_up_query_weight,
            adapter_up_value_weight,
        ],
        axis=2,
    )
    all_lists = lax.all_to_all(
        jnp.broadcast_to(adapter_per_request, (device_total, request_count)), axes, 0, 0, tiled=True
    )
    all_slots = table_lookup(adapter_panel_slot, all_lists)
    mine = all_slots // ADP_DEV == my_store
    local_pick = jnp.sum(jnp.where(mine, all_slots % ADP_DEV, 0), axis=1)
    send = jnp.take(panel_table, local_pick, axis=0, mode="clip")
    got = lax.all_to_all(send, axes, 0, 0, tiled=True)

    lengths = request_token_length[0]
    adapters = adapter_per_request[0]
    request_ends = jnp.cumsum(lengths)
    starts = request_ends - lengths
    token_order = jnp.arange(tok_rows, dtype=jnp.int32)
    request_ids = jnp.sum((token_order[:, None] >= request_ends[None, :]).astype(jnp.int32), axis=1)
    member = request_ids[:, None] == jnp.arange(request_count, dtype=jnp.int32)[None, :]
    positions = token_order - jnp.sum(jnp.where(member, starts[None, :], 0), axis=1)
    owners = table_lookup(adapter_panel_slot, adapters) // ADP_DEV
    owner_token = jnp.sum(jnp.where(member, owners[None, :], 0), axis=1)

    q_base = jnp.dot(
        normalized_hidden_states, query_weight_matrix, preferred_element_type=jnp.float32
    )
    k_base = jnp.dot(
        normalized_hidden_states, key_weight_matrix, preferred_element_type=jnp.float32
    )
    v_base = jnp.dot(
        normalized_hidden_states, value_weight_matrix, preferred_element_type=jnp.float32
    )
    return fused_attention(
        q_base, k_base, v_base, normalized_hidden_states,
        got.reshape(-1, got.shape[-1]), owner_token, positions,
    )


def _swap_halves(x):
    return jnp.concatenate([x[:, 32:64], x[:, 0:32], x[:, 96:128], x[:, 64:96]], axis=1)


def _attend_kernel(qkv_ref, x_ref, got_ref, aux_ref, out_ref, q_s, kd_s, vd_s, dq_ref, dv_ref):
    q_width = dq_ref.shape[1]
    kv_width = dv_ref.shape[1]
    qb_ref = qkv_ref.at[:, 0:q_width]
    kb_ref = qkv_ref.at[:, q_width:q_width + kv_width]
    vb_ref = qkv_ref.at[:, q_width + kv_width:q_width + 2 * kv_width]
    blk = qb_ref.shape[0]
    rows = kd_s.shape[1]
    b = pl.program_id(0)
    g0 = pl.multiple_of(b * blk, blk)
    cols = 256
    slices = x_ref.shape[1] // cols
    q_chunks = qb_ref.shape[1] // 128
    k_chunks = kb_ref.shape[1] // 128
    lane = lax.broadcasted_iota(jnp.int32, (1, 128), 1)
    owner_lane = lax.broadcasted_iota(jnp.int32, (1, cols), 1) // 16

    @pl.when(b == 0)
    def _():
        kd_s[:, blk:2 * blk, :] = jnp.zeros((kd_s.shape[0], blk, kd_s.shape[2]), kd_s.dtype)
        vd_s[:, blk:2 * blk, :] = jnp.zeros((vd_s.shape[0], blk, vd_s.shape[2]), vd_s.dtype)

    low_q = jnp.zeros((blk, cols), jnp.float32)
    low_v = jnp.zeros((blk, cols), jnp.float32)
    nt = (((1,), (1,)), ((), ()))
    for sl in range(slices):
        xs = x_ref[:, sl * cols:(sl + 1) * cols]
        panel = got_ref[sl * cols:(sl + 1) * cols, 0:2 * cols]
        low_q += lax.dot_general(xs, panel[:, 0:cols], nt, preferred_element_type=jnp.float32)
        low_v += lax.dot_general(xs, panel[:, cols:2 * cols], nt, preferred_element_type=jnp.float32)
    mine = owner_lane == aux_ref[:, 257:258].astype(jnp.int32)
    low_q = jnp.where(mine, low_q.astype(jnp.bfloat16), jnp.zeros((), jnp.bfloat16))
    low_v = jnp.where(mine, low_v.astype(jnp.bfloat16), jnp.zeros((), jnp.bfloat16))
    pieces = []
    for sl in range(slices):
        upq = got_ref[sl * cols:(sl + 1) * cols, 2 * cols:3 * cols]
        dq_ref[:, sl * cols:(sl + 1) * cols] = jnp.dot(
            low_q, upq, preferred_element_type=jnp.float32).astype(jnp.bfloat16)
        upv = got_ref[sl * cols:(sl + 1) * cols, 3 * cols:3 * cols + 64]
        pieces.append(jnp.dot(low_v, upv, preferred_element_type=jnp.float32))
    for c in range(slices // 2):
        dv_ref[:, c * 128:(c + 1) * 128] = jnp.concatenate(
            [pieces[2 * c], pieces[2 * c + 1]], axis=1).astype(jnp.bfloat16)

    cos = aux_ref[:, 0:128]
    sin = aux_ref[:, 128:256]

    def q_col(c, carry2):
        c0 = pl.multiple_of(c * 128, 128)
        x = qb_ref[:, pl.ds(c0, 128)] + dq_ref[:, pl.ds(c0, 128)].astype(jnp.float32)
        q_s[:, pl.ds(c0, 128)] = (x * cos + _swap_halves(x) * sin).astype(jnp.bfloat16)
        return carry2

    lax.fori_loop(0, q_chunks, q_col, 0, unroll=True)
    zeros = jnp.zeros((blk, 64), jnp.float32)
    for c in range(k_chunks):
        x = kb_ref[:, c * 128:(c + 1) * 128]
        k = (x * cos + _swap_halves(x) * sin).astype(jnp.bfloat16).astype(jnp.float32)
        v = vb_ref[:, c * 128:(c + 1) * 128] + dv_ref[:, c * 128:(c + 1) * 128].astype(jnp.float32)
        v = v.astype(jnp.bfloat16).astype(jnp.float32)
        for half in range(2):
            g = 2 * c + half
            kg = k[:, half * 64:(half + 1) * 64]
            vg = v[:, half * 64:(half + 1) * 64]
            kd_s[g, pl.ds(g0, blk), :] = jnp.concatenate([kg, kg], axis=1).astype(jnp.bfloat16)
            vd_s[g, pl.ds(g0, blk), 0:128] = jnp.concatenate([vg, zeros], axis=1).astype(jnp.bfloat16)
            vd_s[g, pl.ds(g0, blk), 128:256] = jnp.concatenate([zeros, vg], axis=1).astype(jnp.bfloat16)

    window = 2 * blk
    per_group = HEADS // KV_HEADS
    ws = pl.multiple_of(jnp.clip(g0 - blk, 0, rows - window), blk)
    qpos = aux_ref[:, 256:257].astype(jnp.int32)
    qidx = g0 + lax.broadcasted_iota(jnp.int32, (blk, 1), 0)
    kidx = ws + lax.broadcasted_iota(jnp.int32, (1, window), 1)
    allowed = (kidx >= qidx - qpos) & (kidx <= qidx)

    def head_pair(j, carry2):
        g = j // (per_group // 2)
        c0 = pl.multiple_of(j * 128, 128)
        qc = q_s[:, pl.ds(c0, 128)]
        kd = kd_s[g, pl.ds(ws, window), :]
        vd = vd_s[g, pl.ds(ws, window), :]
        zero = jnp.zeros_like(qc)
        probs, totals = [], []
        for half in range(2):
            keep = (lane < 64) if half == 0 else (lane >= 64)
            qh = jnp.where(keep, qc, zero)
            s = lax.dot_general(qh, kd, nt, preferred_element_type=jnp.float32) * (HEAD_DIM ** -0.5)
            s = jnp.where(allowed, s, -jnp.inf)
            m = jnp.max(s, axis=1, keepdims=True)
            p = jnp.exp(s - m)
            totals.append(jnp.sum(p, axis=1, keepdims=True))
            probs.append(p.astype(jnp.bfloat16))
        o = (jnp.dot(probs[0], vd[:, 0:128], preferred_element_type=jnp.float32)
             + jnp.dot(probs[1], vd[:, 128:256], preferred_element_type=jnp.float32))
        o = jnp.where(lane < 64, o / totals[0], o / totals[1])
        out_ref[:, pl.ds(c0, 128)] = o.astype(out_ref.dtype)
        return carry2

    lax.fori_loop(0, HEADS // 2, head_pair, 0, unroll=True)


def rope_tables(positions):
    half_dim = HEAD_DIM // 2
    frequency = 500000.0 ** (-(jnp.arange(half_dim).astype(jnp.float32) * 2.0 / HEAD_DIM))
    angles = positions.astype(jnp.float32)[:, None] * frequency[None, :]
    cos = jnp.cos(angles)
    sin = jnp.sin(angles)
    cos_t = jnp.concatenate([cos, cos, cos, cos], axis=1)
    sin_t = jnp.concatenate([-sin, sin, -sin, sin], axis=1)
    return cos_t, sin_t


def fused_attention(q_base, k_base, v_base, states, got, owner_token, positions):
    rows = q_base.shape[0]
    cos_t, sin_t = rope_tables(positions)
    side = jnp.zeros((rows, 128), jnp.float32)
    side = side.at[:, 0].set(positions.astype(jnp.float32)).at[:, 1].set(owner_token.astype(jnp.float32))
    aux = jnp.concatenate([cos_t, sin_t, side], axis=1)
    qkv = jnp.concatenate([q_base, k_base, v_base], axis=1)
    flops = 2 * rows * 256 * 64 * 2 * HEADS * 2 + 2 * rows * 256 * (2 * 2048 + 2048 + 512)
    blk = 128
    row_block = lambda width: pl.BlockSpec((blk, width), lambda b: (b, 0))
    return pl.pallas_call(
        _attend_kernel,
        out_shape=jax.ShapeDtypeStruct((rows, HEADS * HEAD_DIM), jnp.bfloat16),
        grid=(rows // blk,),
        in_specs=[
            row_block(qkv.shape[1]),
            row_block(states.shape[1]),
            pl.BlockSpec(got.shape, lambda b: (0, 0)),
            row_block(aux.shape[1]),
        ],
        out_specs=row_block(HEADS * HEAD_DIM),
        scratch_shapes=[
            pltpu.VMEM((blk, HEADS * HEAD_DIM), jnp.bfloat16),
            pltpu.VMEM((KV_HEADS, rows, 128), jnp.bfloat16),
            pltpu.VMEM((KV_HEADS, rows, 256), jnp.bfloat16),
            pltpu.VMEM((blk, HEADS * HEAD_DIM), jnp.bfloat16),
            pltpu.VMEM((blk, KV_HEADS * HEAD_DIM), jnp.bfloat16),
        ],
        compiler_params=pltpu.CompilerParams(
            dimension_semantics=("arbitrary",), vmem_limit_bytes=48 * 1024 * 1024
        ),
        cost_estimate=pl.CostEstimate(flops=flops, transcendentals=rows * 256 * HEADS,
                                      bytes_accessed=rows * (2048 * 8 + 512 * 8 + 256 * 4) + got.size * 2),
    )(qkv, states, got, aux)


def solution(mesh):
    return jax.shard_map(
        local,
        mesh=mesh,
        in_specs=(
            P(("serve", "store"), None),
            P(),
            P(),
            P(),
            P("store", None, "serve"),
            P("store", None, "serve"),
            P("store", None, "serve"),
            P(),
            P(("serve", "store"), None),
            P(("serve", "store"), None),
        ),
        out_specs=P(("serve", "store"), None),
        check_vma=False,
    )
```

```python
import jax
import jax.numpy as jnp
from jax import lax
from jax.experimental import pallas as pl
from jax.experimental.pallas import tpu as pltpu
from jax.sharding import PartitionSpec as P

HEADS = 32
KV_HEADS = 8
HEAD_DIM = 64
ADAPTER_RANK = 16
ADP_DEV = 32
LEN_MAX = 64


def rotary(heads_in, positions):
    half_dim = HEAD_DIM // 2
    frequency = 500000.0 ** (-(jnp.arange(half_dim).astype(jnp.float32) * 2.0 / HEAD_DIM))
    angles = positions.astype(jnp.float32)[:, None] * frequency[None, :]
    cosine_table = jnp.cos(angles)[:, None, :]
    sine_table = jnp.sin(angles)[:, None, :]
    first_half = heads_in[..., :half_dim]
    second_half = heads_in[..., half_dim:]
    return jnp.concatenate(
        [
            first_half * cosine_table - second_half * sine_table,
            second_half * cosine_table + first_half * sine_table,
        ],
        axis=-1,
    )


def table_lookup(table, wanted):
    entries = jnp.arange(table.shape[0], dtype=jnp.int32)
    return jnp.sum(jnp.where(wanted[..., None] == entries, table, 0), axis=-1)


def reduced_rank_products(block_list, down_panels, up_query, up_value):
    low = jnp.einsum(
        "jkd,jrd->jkr", block_list, down_panels, preferred_element_type=jnp.float32
    ).astype(jnp.bfloat16)
    query_update = jnp.einsum(
        "jkr,jrd->jkd", low[..., :ADAPTER_RANK], up_query, preferred_element_type=jnp.float32
    ).astype(jnp.bfloat16)
    value_update = jnp.einsum(
        "jkr,jrd->jkd", low[..., ADAPTER_RANK:], up_value, preferred_element_type=jnp.float32
    ).astype(jnp.bfloat16)
    return (query_update, value_update)


def local_choice(panel_set, lists, adapter_panel_slot, my_store):
    source_slots = table_lookup(adapter_panel_slot, lists)
    mine_mask = source_slots // ADP_DEV == my_store
    local_source = jnp.sum(jnp.where(mine_mask, source_slots % ADP_DEV, 0), axis=1)
    return tuple((jnp.take(panel, local_source, axis=0) for panel in panel_set))


def attention(query_rot, key_rot, value_rows, request_ids):
    tok_rows = query_rot.shape[0]
    per_group = HEADS // KV_HEADS
    block_rows = min(128, tok_rows)
    reach = LEN_MAX
    key_pad = jnp.concatenate(
        [jnp.zeros((reach,) + key_rot.shape[1:], key_rot.dtype), key_rot], axis=0
    )
    value_pad = jnp.concatenate(
        [jnp.zeros((reach,) + value_rows.shape[1:], value_rows.dtype), value_rows], axis=0
    )
    ids_pad = jnp.concatenate([jnp.full((reach,), -1, jnp.int32), request_ids], axis=0)
    token_order = jnp.arange(tok_rows, dtype=jnp.int32)
    order_pad = jnp.concatenate([jnp.full((reach,), -1, jnp.int32), token_order], axis=0)
    outputs = []
    for block_index in range(tok_rows // block_rows):
        first = block_index * block_rows
        query_block = query_rot[first : first + block_rows]
        query_ids = request_ids[first : first + block_rows]
        query_order = token_order[first : first + block_rows]
        key_block = key_pad[first : first + reach + block_rows]
        value_block = value_pad[first : first + reach + block_rows]
        key_ids = ids_pad[first : first + reach + block_rows]
        key_order = order_pad[first : first + reach + block_rows]
        allowed = (query_ids[:, None] == key_ids[None, :]) & (
            key_order[None, :] <= query_order[:, None]
        )
        pieces = []
        for group_index in range(KV_HEADS):
            query_part = query_block[:, group_index * per_group : (group_index + 1) * per_group, :]
            key_part = key_block[:, group_index, :]
            value_part = value_block[:, group_index, :]
            scores = jnp.einsum(
                "qhd,kd->hqk", query_part, key_part, preferred_element_type=jnp.float32
            ) * HEAD_DIM ** (-0.5)
            scores = jnp.where(allowed[None], scores, -jnp.inf)
            row_max = jnp.max(scores, axis=-1, keepdims=True)
            raised = jnp.exp(scores - row_max)
            row_total = jnp.sum(raised, axis=-1)
            weights = raised.astype(jnp.bfloat16)
            mixed_heads = (
                jnp.einsum("hqk,kd->qhd", weights, value_part, preferred_element_type=jnp.float32)
                / jnp.transpose(row_total)[:, :, None]
            )
            pieces.append(mixed_heads)
        outputs.append(
            jnp.concatenate(pieces, axis=1)
            .reshape(block_rows, HEADS * HEAD_DIM)
            .astype(jnp.bfloat16)
        )
    return jnp.concatenate(outputs, axis=0)


def local(
    normalized_hidden_states,
    query_weight_matrix,
    key_weight_matrix,
    value_weight_matrix,
    adapter_down_weight,
    adapter_up_query_weight,
    adapter_up_value_weight,
    adapter_panel_slot,
    adapter_per_request,
    request_token_length,
):
    axes = ("serve", "store")
    serve_count = lax.axis_size("serve")
    store_count = lax.axis_size("store")
    my_store = lax.axis_index("store")
    tok_rows, width = normalized_hidden_states.shape
    request_count = request_token_length.shape[1]
    adp_dev, rank2, cols = adapter_down_weight.shape
    vcols = adapter_up_value_weight.shape[2]
    device_total = serve_count * store_count
    panel_table = jnp.concatenate(
        [
            adapter_down_weight[:, :ADAPTER_RANK],
            adapter_down_weight[:, ADAPTER_RANK:],
            adapter_up_query_weight,
            adapter_up_value_weight,
        ],
        axis=2,
    )
    all_lists = lax.all_to_all(
        jnp.broadcast_to(adapter_per_request, (device_total, request_count)), axes, 0, 0, tiled=True
    )
    all_slots = table_lookup(adapter_panel_slot, all_lists)
    mine = all_slots // ADP_DEV == my_store
    local_pick = jnp.sum(jnp.where(mine, all_slots % ADP_DEV, 0), axis=1)
    send = jnp.take(panel_table, local_pick, axis=0, mode="clip")
    got = lax.all_to_all(send, axes, 0, 0, tiled=True)

    lengths = request_token_length[0]
    adapters = adapter_per_request[0]
    request_ends = jnp.cumsum(lengths)
    starts = request_ends - lengths
    token_order = jnp.arange(tok_rows, dtype=jnp.int32)
    request_ids = jnp.sum((token_order[:, None] >= request_ends[None, :]).astype(jnp.int32), axis=1)
    member = request_ids[:, None] == jnp.arange(request_count, dtype=jnp.int32)[None, :]
    positions = token_order - jnp.sum(jnp.where(member, starts[None, :], 0), axis=1)
    owners = table_lookup(adapter_panel_slot, adapters) // ADP_DEV
    owner_token = jnp.sum(jnp.where(member, owners[None, :], 0), axis=1)

    q_base = jnp.dot(
        normalized_hidden_states, query_weight_matrix, preferred_element_type=jnp.float32
    )
    k_base = jnp.dot(
        normalized_hidden_states, key_weight_matrix, preferred_element_type=jnp.float32
    )
    v_base = jnp.dot(
        normalized_hidden_states, value_weight_matrix, preferred_element_type=jnp.float32
    )
    return fused_attention(
        q_base, k_base, v_base, normalized_hidden_states,
        got.reshape(-1, got.shape[-1]), owner_token, positions,
    )


def _swap_halves(x):
    return jnp.concatenate([x[:, 32:64], x[:, 0:32], x[:, 96:128], x[:, 64:96]], axis=1)


def _attend_kernel(qkv_ref, x_ref, got_ref, aux_ref, out_ref, q_s, kd_s, vd_s, dq_ref, dv_ref):
    q_width = dq_ref.shape[1]
    kv_width = dv_ref.shape[1]
    qb_ref = qkv_ref.at[:, 0:q_width]
    kb_ref = qkv_ref.at[:, q_width:q_width + kv_width]
    vb_ref = qkv_ref.at[:, q_width + kv_width:q_width + 2 * kv_width]
    blk = qb_ref.shape[0]
    rows = kd_s.shape[1]
    b = pl.program_id(0)
    g0 = pl.multiple_of(b * blk, blk)
    cols = 256
    slices = x_ref.shape[1] // cols
    q_chunks = qb_ref.shape[1] // 128
    k_chunks = kb_ref.shape[1] // 128
    lane = lax.broadcasted_iota(jnp.int32, (1, 128), 1)
    owner_lane = lax.broadcasted_iota(jnp.int32, (1, cols), 1) // 16

    @pl.when(b == 0)
    def _():
        kd_s[:, blk:2 * blk, :] = jnp.zeros((kd_s.shape[0], blk, kd_s.shape[2]), kd_s.dtype)
        vd_s[:, blk:2 * blk, :] = jnp.zeros((vd_s.shape[0], blk, vd_s.shape[2]), vd_s.dtype)

    low_q = jnp.zeros((blk, cols), jnp.float32)
    low_v = jnp.zeros((blk, cols), jnp.float32)
    nt = (((1,), (1,)), ((), ()))
    for sl in range(slices):
        xs = x_ref[:, sl * cols:(sl + 1) * cols]
        panel = got_ref[sl * cols:(sl + 1) * cols, 0:2 * cols]
        low_q += lax.dot_general(xs, panel[:, 0:cols], nt, preferred_element_type=jnp.float32)
        low_v += lax.dot_general(xs, panel[:, cols:2 * cols], nt, preferred_element_type=jnp.float32)
    mine = owner_lane == aux_ref[:, 257:258].astype(jnp.int32)
    low_q = jnp.where(mine, low_q.astype(jnp.bfloat16), jnp.zeros((), jnp.bfloat16))
    low_v = jnp.where(mine, low_v.astype(jnp.bfloat16), jnp.zeros((), jnp.bfloat16))
    pieces = []
    for sl in range(slices):
        upq = got_ref[sl * cols:(sl + 1) * cols, 2 * cols:3 * cols]
        dq_ref[:, sl * cols:(sl + 1) * cols] = jnp.dot(
            low_q, upq, preferred_element_type=jnp.float32).astype(jnp.bfloat16)
        upv = got_ref[sl * cols:(sl + 1) * cols, 3 * cols:3 * cols + 64]
        pieces.append(jnp.dot(low_v, upv, preferred_element_type=jnp.float32))
    for c in range(slices // 2):
        dv_ref[:, c * 128:(c + 1) * 128] = jnp.concatenate(
            [pieces[2 * c], pieces[2 * c + 1]], axis=1).astype(jnp.bfloat16)

    cos = aux_ref[:, 0:128]
    sin = aux_ref[:, 128:256]

    def q_col(c, carry2):
        c0 = pl.multiple_of(c * 128, 128)
        x = qb_ref[:, pl.ds(c0, 128)] + dq_ref[:, pl.ds(c0, 128)].astype(jnp.float32)
        q_s[:, pl.ds(c0, 128)] = (x * cos + _swap_halves(x) * sin).astype(jnp.bfloat16)
        return carry2

    lax.fori_loop(0, q_chunks, q_col, 0, unroll=True)
    zeros = jnp.zeros((blk, 64), jnp.float32)
    for c in range(k_chunks):
        x = kb_ref[:, c * 128:(c + 1) * 128]
        k = (x * cos + _swap_halves(x) * sin).astype(jnp.bfloat16).astype(jnp.float32)
        v = vb_ref[:, c * 128:(c + 1) * 128] + dv_ref[:, c * 128:(c + 1) * 128].astype(jnp.float32)
        v = v.astype(jnp.bfloat16).astype(jnp.float32)
        for half in range(2):
            g = 2 * c + half
            kg = k[:, half * 64:(half + 1) * 64]
            vg = v[:, half * 64:(half + 1) * 64]
            kd_s[g, pl.ds(g0, blk), :] = jnp.concatenate([kg, kg], axis=1).astype(jnp.bfloat16)
            vd_s[g, pl.ds(g0, blk), 0:128] = jnp.concatenate([vg, zeros], axis=1).astype(jnp.bfloat16)
            vd_s[g, pl.ds(g0, blk), 128:256] = jnp.concatenate([zeros, vg], axis=1).astype(jnp.bfloat16)

    window = 2 * blk
    per_group = HEADS // KV_HEADS
    ws = pl.multiple_of(jnp.clip(g0 - blk, 0, rows - window), blk)
    qpos = aux_ref[:, 256:257].astype(jnp.int32)
    qidx = g0 + lax.broadcasted_iota(jnp.int32, (blk, 1), 0)
    kidx = ws + lax.broadcasted_iota(jnp.int32, (1, window), 1)
    allowed = (kidx >= qidx - qpos) & (kidx <= qidx)

    def head_pair(j, carry2):
        g = j // (per_group // 2)
        c0 = pl.multiple_of(j * 128, 128)
        qc = q_s[:, pl.ds(c0, 128)]
        kd = kd_s[g, pl.ds(ws, window), :]
        vd = vd_s[g, pl.ds(ws, window), :]
        zero = jnp.zeros_like(qc)
        probs, totals = [], []
        for half in range(2):
            keep = (lane < 64) if half == 0 else (lane >= 64)
            qh = jnp.where(keep, qc, zero)
            s = lax.dot_general(qh, kd, nt, preferred_element_type=jnp.float32) * (HEAD_DIM ** -0.5)
            s = jnp.where(allowed, s, -jnp.inf)
            m = jnp.max(s, axis=1, keepdims=True)
            p = jnp.exp(s - m)
            totals.append(jnp.sum(p, axis=1, keepdims=True))
            probs.append(p.astype(jnp.bfloat16))
        o = (jnp.dot(probs[0], vd[:, 0:128], preferred_element_type=jnp.float32)
             + jnp.dot(probs[1], vd[:, 128:256], preferred_element_type=jnp.float32))
        o = o * jnp.where(lane < 64, 1.0 / totals[0], 1.0 / totals[1])
        out_ref[:, pl.ds(c0, 128)] = o.astype(out_ref.dtype)
        return carry2

    lax.fori_loop(0, HEADS // 2, head_pair, 0, unroll=True)


def rope_tables(positions):
    half_dim = HEAD_DIM // 2
    frequency = 500000.0 ** (-(jnp.arange(half_dim).astype(jnp.float32) * 2.0 / HEAD_DIM))
    angles = positions.astype(jnp.float32)[:, None] * frequency[None, :]
    cos = jnp.cos(angles)
    sin = jnp.sin(angles)
    cos_t = jnp.concatenate([cos, cos, cos, cos], axis=1)
    sin_t = jnp.concatenate([-sin, sin, -sin, sin], axis=1)
    return cos_t, sin_t


def fused_attention(q_base, k_base, v_base, states, got, owner_token, positions):
    rows = q_base.shape[0]
    cos_t, sin_t = rope_tables(positions)
    side = jnp.zeros((rows, 128), jnp.float32)
    side = side.at[:, 0].set(positions.astype(jnp.float32)).at[:, 1].set(owner_token.astype(jnp.float32))
    aux = jnp.concatenate([cos_t, sin_t, side], axis=1)
    qkv = jnp.concatenate([q_base, k_base, v_base], axis=1)
    flops = 2 * rows * 256 * 64 * 2 * HEADS * 2 + 2 * rows * 256 * (2 * 2048 + 2048 + 512)
    blk = 128
    row_block = lambda width: pl.BlockSpec((blk, width), lambda b: (b, 0))
    return pl.pallas_call(
        _attend_kernel,
        out_shape=jax.ShapeDtypeStruct((rows, HEADS * HEAD_DIM), jnp.bfloat16),
        grid=(rows // blk,),
        in_specs=[
            row_block(qkv.shape[1]),
            row_block(states.shape[1]),
            pl.BlockSpec(got.shape, lambda b: (0, 0)),
            row_block(aux.shape[1]),
        ],
        out_specs=row_block(HEADS * HEAD_DIM),
        scratch_shapes=[
            pltpu.VMEM((blk, HEADS * HEAD_DIM), jnp.bfloat16),
            pltpu.VMEM((KV_HEADS, rows, 128), jnp.bfloat16),
            pltpu.VMEM((KV_HEADS, rows, 256), jnp.bfloat16),
            pltpu.VMEM((blk, HEADS * HEAD_DIM), jnp.bfloat16),
            pltpu.VMEM((blk, KV_HEADS * HEAD_DIM), jnp.bfloat16),
        ],
        compiler_params=pltpu.CompilerParams(
            dimension_semantics=("arbitrary",), vmem_limit_bytes=48 * 1024 * 1024
        ),
        cost_estimate=pl.CostEstimate(flops=flops, transcendentals=rows * 256 * HEADS,
                                      bytes_accessed=rows * (2048 * 8 + 512 * 8 + 256 * 4) + got.size * 2),
    )(qkv, states, got, aux)


def solution(mesh):
    return jax.shard_map(
        local,
        mesh=mesh,
        in_specs=(
            P(("serve", "store"), None),
            P(),
            P(),
            P(),
            P("store", None, "serve"),
            P("store", None, "serve"),
            P("store", None, "serve"),
            P(),
            P(("serve", "store"), None),
            P(("serve", "store"), None),
        ),
        out_specs=P(("serve", "store"), None),
        check_vma=False,
    )
```

```python
import jax
import jax.numpy as jnp
from jax import lax
from jax.experimental import pallas as pl
from jax.experimental.pallas import tpu as pltpu
from jax.sharding import PartitionSpec as P

HEADS = 32
KV_HEADS = 8
HEAD_DIM = 64
ADAPTER_RANK = 16
ADP_DEV = 32
LEN_MAX = 64


def rotary(heads_in, positions):
    half_dim = HEAD_DIM // 2
    frequency = 500000.0 ** (-(jnp.arange(half_dim).astype(jnp.float32) * 2.0 / HEAD_DIM))
    angles = positions.astype(jnp.float32)[:, None] * frequency[None, :]
    cosine_table = jnp.cos(angles)[:, None, :]
    sine_table = jnp.sin(angles)[:, None, :]
    first_half = heads_in[..., :half_dim]
    second_half = heads_in[..., half_dim:]
    return jnp.concatenate(
        [
            first_half * cosine_table - second_half * sine_table,
            second_half * cosine_table + first_half * sine_table,
        ],
        axis=-1,
    )


def table_lookup(table, wanted):
    entries = jnp.arange(table.shape[0], dtype=jnp.int32)
    return jnp.sum(jnp.where(wanted[..., None] == entries, table, 0), axis=-1)


def reduced_rank_products(block_list, down_panels, up_query, up_value):
    low = jnp.einsum(
        "jkd,jrd->jkr", block_list, down_panels, preferred_element_type=jnp.float32
    ).astype(jnp.bfloat16)
    query_update = jnp.einsum(
        "jkr,jrd->jkd", low[..., :ADAPTER_RANK], up_query, preferred_element_type=jnp.float32
    ).astype(jnp.bfloat16)
    value_update = jnp.einsum(
        "jkr,jrd->jkd", low[..., ADAPTER_RANK:], up_value, preferred_element_type=jnp.float32
    ).astype(jnp.bfloat16)
    return (query_update, value_update)


def local_choice(panel_set, lists, adapter_panel_slot, my_store):
    source_slots = table_lookup(adapter_panel_slot, lists)
    mine_mask = source_slots // ADP_DEV == my_store
    local_source = jnp.sum(jnp.where(mine_mask, source_slots % ADP_DEV, 0), axis=1)
    return tuple((jnp.take(panel, local_source, axis=0) for panel in panel_set))


def attention(query_rot, key_rot, value_rows, request_ids):
    tok_rows = query_rot.shape[0]
    per_group = HEADS // KV_HEADS
    block_rows = min(128, tok_rows)
    reach = LEN_MAX
    key_pad = jnp.concatenate(
        [jnp.zeros((reach,) + key_rot.shape[1:], key_rot.dtype), key_rot], axis=0
    )
    value_pad = jnp.concatenate(
        [jnp.zeros((reach,) + value_rows.shape[1:], value_rows.dtype), value_rows], axis=0
    )
    ids_pad = jnp.concatenate([jnp.full((reach,), -1, jnp.int32), request_ids], axis=0)
    token_order = jnp.arange(tok_rows, dtype=jnp.int32)
    order_pad = jnp.concatenate([jnp.full((reach,), -1, jnp.int32), token_order], axis=0)
    outputs = []
    for block_index in range(tok_rows // block_rows):
        first = block_index * block_rows
        query_block = query_rot[first : first + block_rows]
        query_ids = request_ids[first : first + block_rows]
        query_order = token_order[first : first + block_rows]
        key_block = key_pad[first : first + reach + block_rows]
        value_block = value_pad[first : first + reach + block_rows]
        key_ids = ids_pad[first : first + reach + block_rows]
        key_order = order_pad[first : first + reach + block_rows]
        allowed = (query_ids[:, None] == key_ids[None, :]) & (
            key_order[None, :] <= query_order[:, None]
        )
        pieces = []
        for group_index in range(KV_HEADS):
            query_part = query_block[:, group_index * per_group : (group_index + 1) * per_group, :]
            key_part = key_block[:, group_index, :]
            value_part = value_block[:, group_index, :]
            scores = jnp.einsum(
                "qhd,kd->hqk", query_part, key_part, preferred_element_type=jnp.float32
            ) * HEAD_DIM ** (-0.5)
            scores = jnp.where(allowed[None], scores, -jnp.inf)
            row_max = jnp.max(scores, axis=-1, keepdims=True)
            raised = jnp.exp(scores - row_max)
            row_total = jnp.sum(raised, axis=-1)
            weights = raised.astype(jnp.bfloat16)
            mixed_heads = (
                jnp.einsum("hqk,kd->qhd", weights, value_part, preferred_element_type=jnp.float32)
                / jnp.transpose(row_total)[:, :, None]
            )
            pieces.append(mixed_heads)
        outputs.append(
            jnp.concatenate(pieces, axis=1)
            .reshape(block_rows, HEADS * HEAD_DIM)
            .astype(jnp.bfloat16)
        )
    return jnp.concatenate(outputs, axis=0)


def local(
    normalized_hidden_states,
    query_weight_matrix,
    key_weight_matrix,
    value_weight_matrix,
    adapter_down_weight,
    adapter_up_query_weight,
    adapter_up_value_weight,
    adapter_panel_slot,
    adapter_per_request,
    request_token_length,
):
    axes = ("serve", "store")
    serve_count = lax.axis_size("serve")
    store_count = lax.axis_size("store")
    my_store = lax.axis_index("store")
    tok_rows, width = normalized_hidden_states.shape
    request_count = request_token_length.shape[1]
    adp_dev, rank2, cols = adapter_down_weight.shape
    vcols = adapter_up_value_weight.shape[2]
    device_total = serve_count * store_count
    panel_table = jnp.concatenate(
        [
            adapter_down_weight[:, :ADAPTER_RANK],
            adapter_down_weight[:, ADAPTER_RANK:],
            adapter_up_query_weight,
            adapter_up_value_weight,
        ],
        axis=2,
    )
    all_lists = lax.all_to_all(
        jnp.broadcast_to(adapter_per_request, (device_total, request_count)), axes, 0, 0, tiled=True
    )
    all_slots = table_lookup(adapter_panel_slot, all_lists)
    mine = all_slots // ADP_DEV == my_store
    local_pick = jnp.sum(jnp.where(mine, all_slots % ADP_DEV, 0), axis=1)
    send = jnp.take(panel_table, local_pick, axis=0, mode="clip")
    got = lax.all_to_all(send, axes, 0, 0, tiled=True)

    lengths = request_token_length[0]
    adapters = adapter_per_request[0]
    request_ends = jnp.cumsum(lengths)
    starts = request_ends - lengths
    token_order = jnp.arange(tok_rows, dtype=jnp.int32)
    request_ids = jnp.sum((token_order[:, None] >= request_ends[None, :]).astype(jnp.int32), axis=1)
    member = request_ids[:, None] == jnp.arange(request_count, dtype=jnp.int32)[None, :]
    positions = token_order - jnp.sum(jnp.where(member, starts[None, :], 0), axis=1)
    owners = table_lookup(adapter_panel_slot, adapters) // ADP_DEV
    owner_token = jnp.sum(jnp.where(member, owners[None, :], 0), axis=1)

    q_base = jnp.dot(
        normalized_hidden_states, query_weight_matrix, preferred_element_type=jnp.float32
    )
    k_base = jnp.dot(
        normalized_hidden_states, key_weight_matrix, preferred_element_type=jnp.float32
    )
    v_base = jnp.dot(
        normalized_hidden_states, value_weight_matrix, preferred_element_type=jnp.float32
    )
    return fused_attention(
        q_base, k_base, v_base, normalized_hidden_states,
        got.reshape(-1, got.shape[-1]), owner_token, positions,
    )


def _swap_halves(x):
    return jnp.concatenate([x[:, 32:64], x[:, 0:32], x[:, 96:128], x[:, 64:96]], axis=1)


def _attend_kernel(qkv_ref, x_ref, got_ref, aux_ref, out_ref, q_s, kd_s, vd_s, dq_ref, dv_ref):
    q_width = dq_ref.shape[1]
    kv_width = dv_ref.shape[1]
    qb_ref = qkv_ref.at[:, 0:q_width]
    kb_ref = qkv_ref.at[:, q_width:q_width + kv_width]
    vb_ref = qkv_ref.at[:, q_width + kv_width:q_width + 2 * kv_width]
    blk = qb_ref.shape[0]
    rows = kd_s.shape[2]
    b = pl.program_id(0)
    g0 = pl.multiple_of(b * blk, blk)
    cols = 256
    slices = x_ref.shape[1] // cols
    q_chunks = qb_ref.shape[1] // 128
    k_chunks = kb_ref.shape[1] // 128
    lane = lax.broadcasted_iota(jnp.int32, (1, 128), 1)
    owner_lane = lax.broadcasted_iota(jnp.int32, (1, cols), 1) // 16

    @pl.when(b == 0)
    def _():
        kd_s[:, :, blk:2 * blk] = jnp.zeros((kd_s.shape[0], kd_s.shape[1], blk), kd_s.dtype)
        vd_s[:, blk:2 * blk, :] = jnp.zeros((vd_s.shape[0], blk, vd_s.shape[2]), vd_s.dtype)

    low_q = jnp.zeros((blk, cols), jnp.float32)
    low_v = jnp.zeros((blk, cols), jnp.float32)
    nt = (((1,), (1,)), ((), ()))
    for sl in range(slices):
        xs = x_ref[:, sl * cols:(sl + 1) * cols]
        panel = got_ref[sl * cols:(sl + 1) * cols, 0:2 * cols]
        low_q += lax.dot_general(xs, panel[:, 0:cols], nt, preferred_element_type=jnp.float32)
        low_v += lax.dot_general(xs, panel[:, cols:2 * cols], nt, preferred_element_type=jnp.float32)
    mine = owner_lane == aux_ref[:, 257:258].astype(jnp.int32)
    low_q = jnp.where(mine, low_q.astype(jnp.bfloat16), jnp.zeros((), jnp.bfloat16))
    low_v = jnp.where(mine, low_v.astype(jnp.bfloat16), jnp.zeros((), jnp.bfloat16))
    pieces = []
    for sl in range(slices):
        upq = got_ref[sl * cols:(sl + 1) * cols, 2 * cols:3 * cols]
        dq_ref[:, sl * cols:(sl + 1) * cols] = jnp.dot(
            low_q, upq, preferred_element_type=jnp.float32).astype(jnp.bfloat16)
        upv = got_ref[sl * cols:(sl + 1) * cols, 3 * cols:3 * cols + 64]
        pieces.append(jnp.dot(low_v, upv, preferred_element_type=jnp.float32))
    for c in range(slices // 2):
        dv_ref[:, c * 128:(c + 1) * 128] = jnp.concatenate(
            [pieces[2 * c], pieces[2 * c + 1]], axis=1).astype(jnp.bfloat16)

    cos = aux_ref[:, 0:128]
    sin = aux_ref[:, 128:256]

    def q_col(c, carry2):
        c0 = pl.multiple_of(c * 128, 128)
        x = qb_ref[:, pl.ds(c0, 128)] + dq_ref[:, pl.ds(c0, 128)].astype(jnp.float32)
        q_s[:, pl.ds(c0, 128)] = (x * cos + _swap_halves(x) * sin).astype(jnp.bfloat16)
        return carry2

    lax.fori_loop(0, q_chunks, q_col, 0, unroll=True)
    zeros = jnp.zeros((blk, 64), jnp.float32)
    for c in range(k_chunks):
        x = kb_ref[:, c * 128:(c + 1) * 128]
        k = (x * cos + _swap_halves(x) * sin).astype(jnp.bfloat16).astype(jnp.float32)
        v = vb_ref[:, c * 128:(c + 1) * 128] + dv_ref[:, c * 128:(c + 1) * 128].astype(jnp.float32)
        v = v.astype(jnp.bfloat16).astype(jnp.float32)
        for half in range(2):
            g = 2 * c + half
            kg = k[:, half * 64:(half + 1) * 64]
            vg = v[:, half * 64:(half + 1) * 64]
            kd_s[g, :, pl.ds(g0, blk)] = jnp.transpose(jnp.concatenate([kg, kg], axis=1)).astype(jnp.bfloat16)
            vd_s[g, pl.ds(g0, blk), 0:128] = jnp.concatenate([vg, zeros], axis=1).astype(jnp.bfloat16)
            vd_s[g, pl.ds(g0, blk), 128:256] = jnp.concatenate([zeros, vg], axis=1).astype(jnp.bfloat16)

    window = 2 * blk
    per_group = HEADS // KV_HEADS
    ws = pl.multiple_of(jnp.clip(g0 - blk, 0, rows - window), blk)
    qpos = aux_ref[:, 256:257].astype(jnp.int32)
    qidx = g0 + lax.broadcasted_iota(jnp.int32, (blk, 1), 0)
    kidx = ws + lax.broadcasted_iota(jnp.int32, (1, window), 1)
    allowed = (kidx >= qidx - qpos) & (kidx <= qidx)

    def head_pair(j, carry2):
        g = j // (per_group // 2)
        c0 = pl.multiple_of(j * 128, 128)
        qc = q_s[:, pl.ds(c0, 128)]
        kd = kd_s[g, :, pl.ds(ws, window)]
        vd = vd_s[g, pl.ds(ws, window), :]
        zero = jnp.zeros_like(qc)
        probs, totals = [], []
        for half in range(2):
            keep = (lane < 64) if half == 0 else (lane >= 64)
            qh = jnp.where(keep, qc, zero)
            s = jnp.dot(qh, kd, preferred_element_type=jnp.float32) * (HEAD_DIM ** -0.5)
            s = jnp.where(allowed, s, -jnp.inf)
            m = jnp.max(s, axis=1, keepdims=True)
            p = jnp.exp(s - m)
            totals.append(jnp.sum(p, axis=1, keepdims=True))
            probs.append(p.astype(jnp.bfloat16))
        o = (jnp.dot(probs[0], vd[:, 0:128], preferred_element_type=jnp.float32)
             + jnp.dot(probs[1], vd[:, 128:256], preferred_element_type=jnp.float32))
        o = o * jnp.where(lane < 64, 1.0 / totals[0], 1.0 / totals[1])
        out_ref[:, pl.ds(c0, 128)] = o.astype(out_ref.dtype)
        return carry2

    lax.fori_loop(0, HEADS // 2, head_pair, 0, unroll=True)


def rope_tables(positions):
    half_dim = HEAD_DIM // 2
    frequency = 500000.0 ** (-(jnp.arange(half_dim).astype(jnp.float32) * 2.0 / HEAD_DIM))
    angles = positions.astype(jnp.float32)[:, None] * frequency[None, :]
    cos = jnp.cos(angles)
    sin = jnp.sin(angles)
    cos_t = jnp.concatenate([cos, cos, cos, cos], axis=1)
    sin_t = jnp.concatenate([-sin, sin, -sin, sin], axis=1)
    return cos_t, sin_t


def fused_attention(q_base, k_base, v_base, states, got, owner_token, positions):
    rows = q_base.shape[0]
    cos_t, sin_t = rope_tables(positions)
    side = jnp.zeros((rows, 128), jnp.float32)
    side = side.at[:, 0].set(positions.astype(jnp.float32)).at[:, 1].set(owner_token.astype(jnp.float32))
    aux = jnp.concatenate([cos_t, sin_t, side], axis=1)
    qkv = jnp.concatenate([q_base, k_base, v_base], axis=1)
    flops = 2 * rows * 256 * 64 * 2 * HEADS * 2 + 2 * rows * 256 * (2 * 2048 + 2048 + 512)
    blk = 128
    row_block = lambda width: pl.BlockSpec((blk, width), lambda b: (b, 0))
    return pl.pallas_call(
        _attend_kernel,
        out_shape=jax.ShapeDtypeStruct((rows, HEADS * HEAD_DIM), jnp.bfloat16),
        grid=(rows // blk,),
        in_specs=[
            row_block(qkv.shape[1]),
            row_block(states.shape[1]),
            pl.BlockSpec(got.shape, lambda b: (0, 0)),
            row_block(aux.shape[1]),
        ],
        out_specs=row_block(HEADS * HEAD_DIM),
        scratch_shapes=[
            pltpu.VMEM((blk, HEADS * HEAD_DIM), jnp.bfloat16),
            pltpu.VMEM((KV_HEADS, 128, rows), jnp.bfloat16),
            pltpu.VMEM((KV_HEADS, rows, 256), jnp.bfloat16),
            pltpu.VMEM((blk, HEADS * HEAD_DIM), jnp.bfloat16),
            pltpu.VMEM((blk, KV_HEADS * HEAD_DIM), jnp.bfloat16),
        ],
        compiler_params=pltpu.CompilerParams(
            dimension_semantics=("arbitrary",), vmem_limit_bytes=48 * 1024 * 1024
        ),
        cost_estimate=pl.CostEstimate(flops=flops, transcendentals=rows * 256 * HEADS,
                                      bytes_accessed=rows * (2048 * 8 + 512 * 8 + 256 * 4) + got.size * 2),
    )(qkv, states, got, aux)


def solution(mesh):
    return jax.shard_map(
        local,
        mesh=mesh,
        in_specs=(
            P(("serve", "store"), None),
            P(),
            P(),
            P(),
            P("store", None, "serve"),
            P("store", None, "serve"),
            P("store", None, "serve"),
            P(),
            P(("serve", "store"), None),
            P(("serve", "store"), None),
        ),
        out_specs=P(("serve", "store"), None),
        check_vma=False,
    )
```

```python
import jax
import jax.numpy as jnp
from jax import lax
from jax.experimental import pallas as pl
from jax.experimental.pallas import tpu as pltpu
from jax.sharding import PartitionSpec as P

HEADS = 32
KV_HEADS = 8
HEAD_DIM = 64
ADAPTER_RANK = 16
ADP_DEV = 32
LEN_MAX = 64


def rotary(heads_in, positions):
    half_dim = HEAD_DIM // 2
    frequency = 500000.0 ** (-(jnp.arange(half_dim).astype(jnp.float32) * 2.0 / HEAD_DIM))
    angles = positions.astype(jnp.float32)[:, None] * frequency[None, :]
    cosine_table = jnp.cos(angles)[:, None, :]
    sine_table = jnp.sin(angles)[:, None, :]
    first_half = heads_in[..., :half_dim]
    second_half = heads_in[..., half_dim:]
    return jnp.concatenate(
        [
            first_half * cosine_table - second_half * sine_table,
            second_half * cosine_table + first_half * sine_table,
        ],
        axis=-1,
    )


def table_lookup(table, wanted):
    entries = jnp.arange(table.shape[0], dtype=jnp.int32)
    return jnp.sum(jnp.where(wanted[..., None] == entries, table, 0), axis=-1)


def reduced_rank_products(block_list, down_panels, up_query, up_value):
    low = jnp.einsum(
        "jkd,jrd->jkr", block_list, down_panels, preferred_element_type=jnp.float32
    ).astype(jnp.bfloat16)
    query_update = jnp.einsum(
        "jkr,jrd->jkd", low[..., :ADAPTER_RANK], up_query, preferred_element_type=jnp.float32
    ).astype(jnp.bfloat16)
    value_update = jnp.einsum(
        "jkr,jrd->jkd", low[..., ADAPTER_RANK:], up_value, preferred_element_type=jnp.float32
    ).astype(jnp.bfloat16)
    return (query_update, value_update)


def local_choice(panel_set, lists, adapter_panel_slot, my_store):
    source_slots = table_lookup(adapter_panel_slot, lists)
    mine_mask = source_slots // ADP_DEV == my_store
    local_source = jnp.sum(jnp.where(mine_mask, source_slots % ADP_DEV, 0), axis=1)
    return tuple((jnp.take(panel, local_source, axis=0) for panel in panel_set))


def attention(query_rot, key_rot, value_rows, request_ids):
    tok_rows = query_rot.shape[0]
    per_group = HEADS // KV_HEADS
    block_rows = min(128, tok_rows)
    reach = LEN_MAX
    key_pad = jnp.concatenate(
        [jnp.zeros((reach,) + key_rot.shape[1:], key_rot.dtype), key_rot], axis=0
    )
    value_pad = jnp.concatenate(
        [jnp.zeros((reach,) + value_rows.shape[1:], value_rows.dtype), value_rows], axis=0
    )
    ids_pad = jnp.concatenate([jnp.full((reach,), -1, jnp.int32), request_ids], axis=0)
    token_order = jnp.arange(tok_rows, dtype=jnp.int32)
    order_pad = jnp.concatenate([jnp.full((reach,), -1, jnp.int32), token_order], axis=0)
    outputs = []
    for block_index in range(tok_rows // block_rows):
        first = block_index * block_rows
        query_block = query_rot[first : first + block_rows]
        query_ids = request_ids[first : first + block_rows]
        query_order = token_order[first : first + block_rows]
        key_block = key_pad[first : first + reach + block_rows]
        value_block = value_pad[first : first + reach + block_rows]
        key_ids = ids_pad[first : first + reach + block_rows]
        key_order = order_pad[first : first + reach + block_rows]
        allowed = (query_ids[:, None] == key_ids[None, :]) & (
            key_order[None, :] <= query_order[:, None]
        )
        pieces = []
        for group_index in range(KV_HEADS):
            query_part = query_block[:, group_index * per_group : (group_index + 1) * per_group, :]
            key_part = key_block[:, group_index, :]
            value_part = value_block[:, group_index, :]
            scores = jnp.einsum(
                "qhd,kd->hqk", query_part, key_part, preferred_element_type=jnp.float32
            ) * HEAD_DIM ** (-0.5)
            scores = jnp.where(allowed[None], scores, -jnp.inf)
            row_max = jnp.max(scores, axis=-1, keepdims=True)
            raised = jnp.exp(scores - row_max)
            row_total = jnp.sum(raised, axis=-1)
            weights = raised.astype(jnp.bfloat16)
            mixed_heads = (
                jnp.einsum("hqk,kd->qhd", weights, value_part, preferred_element_type=jnp.float32)
                / jnp.transpose(row_total)[:, :, None]
            )
            pieces.append(mixed_heads)
        outputs.append(
            jnp.concatenate(pieces, axis=1)
            .reshape(block_rows, HEADS * HEAD_DIM)
            .astype(jnp.bfloat16)
        )
    return jnp.concatenate(outputs, axis=0)


def local(
    normalized_hidden_states,
    query_weight_matrix,
    key_weight_matrix,
    value_weight_matrix,
    adapter_down_weight,
    adapter_up_query_weight,
    adapter_up_value_weight,
    adapter_panel_slot,
    adapter_per_request,
    request_token_length,
):
    axes = ("serve", "store")
    serve_count = lax.axis_size("serve")
    store_count = lax.axis_size("store")
    my_store = lax.axis_index("store")
    tok_rows, width = normalized_hidden_states.shape
    request_count = request_token_length.shape[1]
    adp_dev, rank2, cols = adapter_down_weight.shape
    vcols = adapter_up_value_weight.shape[2]
    device_total = serve_count * store_count
    panel_table = jnp.concatenate(
        [
            adapter_down_weight[:, :ADAPTER_RANK],
            adapter_down_weight[:, ADAPTER_RANK:],
            adapter_up_query_weight,
            adapter_up_value_weight,
        ],
        axis=2,
    )
    my_slots = table_lookup(adapter_panel_slot, adapter_per_request[0])
    slot_for_owner = jnp.sum(
        jnp.where(
            my_slots[None, :] // ADP_DEV == jnp.arange(store_count, dtype=jnp.int32)[:, None],
            my_slots[None, :] % ADP_DEV,
            0,
        ),
        axis=1,
    )
    local_pick = lax.all_to_all(
        jnp.tile(slot_for_owner, serve_count).reshape(device_total, 1), axes, 0, 0, tiled=True
    ).reshape(device_total)
    send = jnp.take(panel_table, local_pick, axis=0, mode="clip")
    got = lax.all_to_all(send, axes, 0, 0, tiled=True)

    lengths = request_token_length[0]
    adapters = adapter_per_request[0]
    request_ends = jnp.cumsum(lengths)
    starts = request_ends - lengths
    token_order = jnp.arange(tok_rows, dtype=jnp.int32)
    request_ids = jnp.sum((token_order[:, None] >= request_ends[None, :]).astype(jnp.int32), axis=1)
    member = request_ids[:, None] == jnp.arange(request_count, dtype=jnp.int32)[None, :]
    positions = token_order - jnp.sum(jnp.where(member, starts[None, :], 0), axis=1)
    owners = table_lookup(adapter_panel_slot, adapters) // ADP_DEV
    owner_token = jnp.sum(jnp.where(member, owners[None, :], 0), axis=1)

    q_base = jnp.dot(
        normalized_hidden_states, query_weight_matrix, preferred_element_type=jnp.float32
    )
    k_base = jnp.dot(
        normalized_hidden_states, key_weight_matrix, preferred_element_type=jnp.float32
    )
    v_base = jnp.dot(
        normalized_hidden_states, value_weight_matrix, preferred_element_type=jnp.float32
    )
    return fused_attention(
        q_base, k_base, v_base, normalized_hidden_states,
        got.reshape(-1, got.shape[-1]), owner_token, positions,
    )


def _swap_halves(x):
    return jnp.concatenate([x[:, 32:64], x[:, 0:32], x[:, 96:128], x[:, 64:96]], axis=1)


def _attend_kernel(qkv_ref, x_ref, got_ref, aux_ref, out_ref, q_s, kd_s, vd_s, dq_ref, dv_ref):
    q_width = dq_ref.shape[1]
    kv_width = dv_ref.shape[1]
    qb_ref = qkv_ref.at[:, 0:q_width]
    kb_ref = qkv_ref.at[:, q_width:q_width + kv_width]
    vb_ref = qkv_ref.at[:, q_width + kv_width:q_width + 2 * kv_width]
    blk = qb_ref.shape[0]
    rows = kd_s.shape[2]
    b = pl.program_id(0)
    g0 = pl.multiple_of(b * blk, blk)
    cols = 256
    slices = x_ref.shape[1] // cols
    q_chunks = qb_ref.shape[1] // 128
    k_chunks = kb_ref.shape[1] // 128
    lane = lax.broadcasted_iota(jnp.int32, (1, 128), 1)
    owner_lane = lax.broadcasted_iota(jnp.int32, (1, cols), 1) // 16

    @pl.when(b == 0)
    def _():
        kd_s[:, :, blk:2 * blk] = jnp.zeros((kd_s.shape[0], kd_s.shape[1], blk), kd_s.dtype)
        vd_s[:, blk:2 * blk, :] = jnp.zeros((vd_s.shape[0], blk, vd_s.shape[2]), vd_s.dtype)

    low_q = jnp.zeros((blk, cols), jnp.float32)
    low_v = jnp.zeros((blk, cols), jnp.float32)
    nt = (((1,), (1,)), ((), ()))
    for sl in range(slices):
        xs = x_ref[:, sl * cols:(sl + 1) * cols]
        panel = got_ref[sl * cols:(sl + 1) * cols, 0:2 * cols]
        low_q += lax.dot_general(xs, panel[:, 0:cols], nt, preferred_element_type=jnp.float32)
        low_v += lax.dot_general(xs, panel[:, cols:2 * cols], nt, preferred_element_type=jnp.float32)
    mine = owner_lane == aux_ref[:, 257:258].astype(jnp.int32)
    low_q = jnp.where(mine, low_q.astype(jnp.bfloat16), jnp.zeros((), jnp.bfloat16))
    low_v = jnp.where(mine, low_v.astype(jnp.bfloat16), jnp.zeros((), jnp.bfloat16))
    pieces = []
    for sl in range(slices):
        upq = got_ref[sl * cols:(sl + 1) * cols, 2 * cols:3 * cols]
        dq_ref[:, sl * cols:(sl + 1) * cols] = jnp.dot(
            low_q, upq, preferred_element_type=jnp.float32).astype(jnp.bfloat16)
        upv = got_ref[sl * cols:(sl + 1) * cols, 3 * cols:3 * cols + 64]
        pieces.append(jnp.dot(low_v, upv, preferred_element_type=jnp.float32))
    for c in range(slices // 2):
        dv_ref[:, c * 128:(c + 1) * 128] = jnp.concatenate(
            [pieces[2 * c], pieces[2 * c + 1]], axis=1).astype(jnp.bfloat16)

    cos = aux_ref[:, 0:128]
    sin = aux_ref[:, 128:256]

    def q_col(c, carry2):
        c0 = pl.multiple_of(c * 128, 128)
        x = qb_ref[:, pl.ds(c0, 128)] + dq_ref[:, pl.ds(c0, 128)].astype(jnp.float32)
        q_s[:, pl.ds(c0, 128)] = (x * cos + _swap_halves(x) * sin).astype(jnp.bfloat16)
        return carry2

    lax.fori_loop(0, q_chunks, q_col, 0, unroll=True)
    zeros = jnp.zeros((blk, 64), jnp.float32)
    for c in range(k_chunks):
        x = kb_ref[:, c * 128:(c + 1) * 128]
        k = (x * cos + _swap_halves(x) * sin).astype(jnp.bfloat16).astype(jnp.float32)
        v = vb_ref[:, c * 128:(c + 1) * 128] + dv_ref[:, c * 128:(c + 1) * 128].astype(jnp.float32)
        v = v.astype(jnp.bfloat16).astype(jnp.float32)
        for half in range(2):
            g = 2 * c + half
            kg = k[:, half * 64:(half + 1) * 64]
            vg = v[:, half * 64:(half + 1) * 64]
            kd_s[g, :, pl.ds(g0, blk)] = jnp.transpose(jnp.concatenate([kg, kg], axis=1)).astype(jnp.bfloat16)
            vd_s[g, pl.ds(g0, blk), 0:128] = jnp.concatenate([vg, zeros], axis=1).astype(jnp.bfloat16)
            vd_s[g, pl.ds(g0, blk), 128:256] = jnp.concatenate([zeros, vg], axis=1).astype(jnp.bfloat16)

    window = 2 * blk
    per_group = HEADS // KV_HEADS
    ws = pl.multiple_of(jnp.clip(g0 - blk, 0, rows - window), blk)
    qpos = aux_ref[:, 256:257].astype(jnp.int32)
    qidx = g0 + lax.broadcasted_iota(jnp.int32, (blk, 1), 0)
    kidx = ws + lax.broadcasted_iota(jnp.int32, (1, window), 1)
    allowed = (kidx >= qidx - qpos) & (kidx <= qidx)

    def head_pair(j, carry2):
        g = j // (per_group // 2)
        c0 = pl.multiple_of(j * 128, 128)
        qc = q_s[:, pl.ds(c0, 128)]
        kd = kd_s[g, :, pl.ds(ws, window)]
        vd = vd_s[g, pl.ds(ws, window), :]
        zero = jnp.zeros_like(qc)
        probs, totals = [], []
        for half in range(2):
            keep = (lane < 64) if half == 0 else (lane >= 64)
            qh = jnp.where(keep, qc, zero)
            s = jnp.dot(qh, kd, preferred_element_type=jnp.float32) * (HEAD_DIM ** -0.5)
            s = jnp.where(allowed, s, -jnp.inf)
            m = jnp.max(s, axis=1, keepdims=True)
            p = jnp.exp(s - m)
            totals.append(jnp.sum(p, axis=1, keepdims=True))
            probs.append(p.astype(jnp.bfloat16))
        o = (jnp.dot(probs[0], vd[:, 0:128], preferred_element_type=jnp.float32)
             + jnp.dot(probs[1], vd[:, 128:256], preferred_element_type=jnp.float32))
        o = o * jnp.where(lane < 64, 1.0 / totals[0], 1.0 / totals[1])
        out_ref[:, pl.ds(c0, 128)] = o.astype(out_ref.dtype)
        return carry2

    lax.fori_loop(0, HEADS // 2, head_pair, 0, unroll=True)


def rope_tables(positions):
    half_dim = HEAD_DIM // 2
    frequency = 500000.0 ** (-(jnp.arange(half_dim).astype(jnp.float32) * 2.0 / HEAD_DIM))
    angles = positions.astype(jnp.float32)[:, None] * frequency[None, :]
    cos = jnp.cos(angles)
    sin = jnp.sin(angles)
    cos_t = jnp.concatenate([cos, cos, cos, cos], axis=1)
    sin_t = jnp.concatenate([-sin, sin, -sin, sin], axis=1)
    return cos_t, sin_t


def fused_attention(q_base, k_base, v_base, states, got, owner_token, positions):
    rows = q_base.shape[0]
    cos_t, sin_t = rope_tables(positions)
    side = jnp.zeros((rows, 128), jnp.float32)
    side = side.at[:, 0].set(positions.astype(jnp.float32)).at[:, 1].set(owner_token.astype(jnp.float32))
    aux = jnp.concatenate([cos_t, sin_t, side], axis=1)
    qkv = jnp.concatenate([q_base, k_base, v_base], axis=1)
    flops = 2 * rows * 256 * 64 * 2 * HEADS * 2 + 2 * rows * 256 * (2 * 2048 + 2048 + 512)
    blk = 128
    row_block = lambda width: pl.BlockSpec((blk, width), lambda b: (b, 0))
    return pl.pallas_call(
        _attend_kernel,
        out_shape=jax.ShapeDtypeStruct((rows, HEADS * HEAD_DIM), jnp.bfloat16),
        grid=(rows // blk,),
        in_specs=[
            row_block(qkv.shape[1]),
            row_block(states.shape[1]),
            pl.BlockSpec(got.shape, lambda b: (0, 0)),
            row_block(aux.shape[1]),
        ],
        out_specs=row_block(HEADS * HEAD_DIM),
        scratch_shapes=[
            pltpu.VMEM((blk, HEADS * HEAD_DIM), jnp.bfloat16),
            pltpu.VMEM((KV_HEADS, 128, rows), jnp.bfloat16),
            pltpu.VMEM((KV_HEADS, rows, 256), jnp.bfloat16),
            pltpu.VMEM((blk, HEADS * HEAD_DIM), jnp.bfloat16),
            pltpu.VMEM((blk, KV_HEADS * HEAD_DIM), jnp.bfloat16),
        ],
        compiler_params=pltpu.CompilerParams(
            dimension_semantics=("arbitrary",), vmem_limit_bytes=48 * 1024 * 1024
        ),
        cost_estimate=pl.CostEstimate(flops=flops, transcendentals=rows * 256 * HEADS,
                                      bytes_accessed=rows * (2048 * 8 + 512 * 8 + 256 * 4) + got.size * 2),
    )(qkv, states, got, aux)


def solution(mesh):
    return jax.shard_map(
        local,
        mesh=mesh,
        in_specs=(
            P(("serve", "store"), None),
            P(),
            P(),
            P(),
            P("store", None, "serve"),
            P("store", None, "serve"),
            P("store", None, "serve"),
            P(),
            P(("serve", "store"), None),
            P(("serve", "store"), None),
        ),
        out_specs=P(("serve", "store"), None),
        check_vma=False,
    )
```

```python
import jax
import jax.numpy as jnp
from jax import lax
from jax.experimental import pallas as pl
from jax.experimental.pallas import tpu as pltpu
from jax.sharding import PartitionSpec as P

HEADS = 32
KV_HEADS = 8
HEAD_DIM = 64
ADAPTER_RANK = 16
ADP_DEV = 32
LEN_MAX = 64


def rotary(heads_in, positions):
    half_dim = HEAD_DIM // 2
    frequency = 500000.0 ** (-(jnp.arange(half_dim).astype(jnp.float32) * 2.0 / HEAD_DIM))
    angles = positions.astype(jnp.float32)[:, None] * frequency[None, :]
    cosine_table = jnp.cos(angles)[:, None, :]
    sine_table = jnp.sin(angles)[:, None, :]
    first_half = heads_in[..., :half_dim]
    second_half = heads_in[..., half_dim:]
    return jnp.concatenate(
        [
            first_half * cosine_table - second_half * sine_table,
            second_half * cosine_table + first_half * sine_table,
        ],
        axis=-1,
    )


def table_lookup(table, wanted):
    entries = jnp.arange(table.shape[0], dtype=jnp.int32)
    return jnp.sum(jnp.where(wanted[..., None] == entries, table, 0), axis=-1)


def reduced_rank_products(block_list, down_panels, up_query, up_value):
    low = jnp.einsum(
        "jkd,jrd->jkr", block_list, down_panels, preferred_element_type=jnp.float32
    ).astype(jnp.bfloat16)
    query_update = jnp.einsum(
        "jkr,jrd->jkd", low[..., :ADAPTER_RANK], up_query, preferred_element_type=jnp.float32
    ).astype(jnp.bfloat16)
    value_update = jnp.einsum(
        "jkr,jrd->jkd", low[..., ADAPTER_RANK:], up_value, preferred_element_type=jnp.float32
    ).astype(jnp.bfloat16)
    return (query_update, value_update)


def local_choice(panel_set, lists, adapter_panel_slot, my_store):
    source_slots = table_lookup(adapter_panel_slot, lists)
    mine_mask = source_slots // ADP_DEV == my_store
    local_source = jnp.sum(jnp.where(mine_mask, source_slots % ADP_DEV, 0), axis=1)
    return tuple((jnp.take(panel, local_source, axis=0) for panel in panel_set))


def attention(query_rot, key_rot, value_rows, request_ids):
    tok_rows = query_rot.shape[0]
    per_group = HEADS // KV_HEADS
    block_rows = min(128, tok_rows)
    reach = LEN_MAX
    key_pad = jnp.concatenate(
        [jnp.zeros((reach,) + key_rot.shape[1:], key_rot.dtype), key_rot], axis=0
    )
    value_pad = jnp.concatenate(
        [jnp.zeros((reach,) + value_rows.shape[1:], value_rows.dtype), value_rows], axis=0
    )
    ids_pad = jnp.concatenate([jnp.full((reach,), -1, jnp.int32), request_ids], axis=0)
    token_order = jnp.arange(tok_rows, dtype=jnp.int32)
    order_pad = jnp.concatenate([jnp.full((reach,), -1, jnp.int32), token_order], axis=0)
    outputs = []
    for block_index in range(tok_rows // block_rows):
        first = block_index * block_rows
        query_block = query_rot[first : first + block_rows]
        query_ids = request_ids[first : first + block_rows]
        query_order = token_order[first : first + block_rows]
        key_block = key_pad[first : first + reach + block_rows]
        value_block = value_pad[first : first + reach + block_rows]
        key_ids = ids_pad[first : first + reach + block_rows]
        key_order = order_pad[first : first + reach + block_rows]
        allowed = (query_ids[:, None] == key_ids[None, :]) & (
            key_order[None, :] <= query_order[:, None]
        )
        pieces = []
        for group_index in range(KV_HEADS):
            query_part = query_block[:, group_index * per_group : (group_index + 1) * per_group, :]
            key_part = key_block[:, group_index, :]
            value_part = value_block[:, group_index, :]
            scores = jnp.einsum(
                "qhd,kd->hqk", query_part, key_part, preferred_element_type=jnp.float32
            ) * HEAD_DIM ** (-0.5)
            scores = jnp.where(allowed[None], scores, -jnp.inf)
            row_max = jnp.max(scores, axis=-1, keepdims=True)
            raised = jnp.exp(scores - row_max)
            row_total = jnp.sum(raised, axis=-1)
            weights = raised.astype(jnp.bfloat16)
            mixed_heads = (
                jnp.einsum("hqk,kd->qhd", weights, value_part, preferred_element_type=jnp.float32)
                / jnp.transpose(row_total)[:, :, None]
            )
            pieces.append(mixed_heads)
        outputs.append(
            jnp.concatenate(pieces, axis=1)
            .reshape(block_rows, HEADS * HEAD_DIM)
            .astype(jnp.bfloat16)
        )
    return jnp.concatenate(outputs, axis=0)


def local(
    normalized_hidden_states,
    query_weight_matrix,
    key_weight_matrix,
    value_weight_matrix,
    adapter_down_weight,
    adapter_up_query_weight,
    adapter_up_value_weight,
    adapter_panel_slot,
    adapter_per_request,
    request_token_length,
):
    axes = ("serve", "store")
    serve_count = lax.axis_size("serve")
    store_count = lax.axis_size("store")
    my_store = lax.axis_index("store")
    tok_rows, width = normalized_hidden_states.shape
    request_count = request_token_length.shape[1]
    adp_dev, rank2, cols = adapter_down_weight.shape
    vcols = adapter_up_value_weight.shape[2]
    device_total = serve_count * store_count
    panel_table = jnp.concatenate(
        [
            adapter_down_weight[:, :ADAPTER_RANK],
            adapter_down_weight[:, ADAPTER_RANK:],
            adapter_up_query_weight,
            adapter_up_value_weight,
        ],
        axis=2,
    )
    my_slots = table_lookup(adapter_panel_slot, adapter_per_request[0])
    slot_for_owner = jnp.sum(
        jnp.where(
            my_slots[None, :] // ADP_DEV == jnp.arange(store_count, dtype=jnp.int32)[:, None],
            my_slots[None, :] % ADP_DEV,
            0,
        ),
        axis=1,
    )
    local_pick = lax.all_to_all(
        jnp.tile(slot_for_owner, serve_count).reshape(device_total, 1), axes, 0, 0, tiled=True
    ).reshape(device_total)
    send = jnp.take(panel_table, local_pick, axis=0, mode="clip")
    got = lax.all_to_all(send, axes, 0, 0, tiled=True)

    lengths = request_token_length[0]
    adapters = adapter_per_request[0]
    request_ends = jnp.cumsum(lengths)
    starts = request_ends - lengths
    token_order = jnp.arange(tok_rows, dtype=jnp.int32)
    request_ids = jnp.sum((token_order[:, None] >= request_ends[None, :]).astype(jnp.int32), axis=1)
    member = request_ids[:, None] == jnp.arange(request_count, dtype=jnp.int32)[None, :]
    positions = token_order - jnp.sum(jnp.where(member, starts[None, :], 0), axis=1)
    owners = table_lookup(adapter_panel_slot, adapters) // ADP_DEV
    owner_token = jnp.sum(jnp.where(member, owners[None, :], 0), axis=1)

    q_base = jnp.dot(
        normalized_hidden_states, query_weight_matrix, preferred_element_type=jnp.float32
    )
    k_base = jnp.dot(
        normalized_hidden_states, key_weight_matrix, preferred_element_type=jnp.float32
    )
    v_base = jnp.dot(
        normalized_hidden_states, value_weight_matrix, preferred_element_type=jnp.float32
    )
    return fused_attention(
        q_base, k_base, v_base, normalized_hidden_states,
        got.reshape(-1, got.shape[-1]), owner_token, positions,
    )


def _swap_halves(x):
    return jnp.concatenate([x[:, 32:64], x[:, 0:32], x[:, 96:128], x[:, 64:96]], axis=1)


def _attend_kernel(qkv_ref, x_ref, got_ref, aux_ref, out_ref, q_s, kd_s, vd_s, dq_ref, dv_ref, dt_s):
    q_width = dq_ref.shape[1]
    kv_width = dv_ref.shape[1]
    qb_ref = qkv_ref.at[:, 0:q_width]
    kb_ref = qkv_ref.at[:, q_width:q_width + kv_width]
    vb_ref = qkv_ref.at[:, q_width + kv_width:q_width + 2 * kv_width]
    blk = qb_ref.shape[0]
    rows = kd_s.shape[2]
    b = pl.program_id(0)
    g0 = pl.multiple_of(b * blk, blk)
    cols = 256
    slices = x_ref.shape[1] // cols
    q_chunks = qb_ref.shape[1] // 128
    k_chunks = kb_ref.shape[1] // 128
    lane = lax.broadcasted_iota(jnp.int32, (1, 128), 1)
    owner_lane = lax.broadcasted_iota(jnp.int32, (1, cols), 1) // 16

    @pl.when(b == 0)
    def _():
        for sl in range(slices):
            panel = got_ref[sl * cols:(sl + 1) * cols, 0:2 * cols].astype(jnp.float32)
            dt_s[sl, :, 0:cols] = jnp.transpose(panel[:, 0:cols]).astype(jnp.bfloat16)
            dt_s[sl, :, cols:2 * cols] = jnp.transpose(panel[:, cols:2 * cols]).astype(jnp.bfloat16)
        kd_s[:, :, blk:2 * blk] = jnp.zeros((kd_s.shape[0], kd_s.shape[1], blk), kd_s.dtype)
        vd_s[:, blk:2 * blk, :] = jnp.zeros((vd_s.shape[0], blk, vd_s.shape[2]), vd_s.dtype)

    low = jnp.zeros((blk, 2 * cols), jnp.float32)
    nt = (((1,), (1,)), ((), ()))
    for sl in range(slices):
        low += jnp.dot(x_ref[:, sl * cols:(sl + 1) * cols], dt_s[sl], preferred_element_type=jnp.float32)
    low_q = low[:, 0:cols]
    low_v = low[:, cols:2 * cols]
    mine = owner_lane == aux_ref[:, 257:258].astype(jnp.int32)
    low_q = jnp.where(mine, low_q.astype(jnp.bfloat16), jnp.zeros((), jnp.bfloat16))
    low_v = jnp.where(mine, low_v.astype(jnp.bfloat16), jnp.zeros((), jnp.bfloat16))
    pieces = []
    for sl in range(slices):
        upq = got_ref[sl * cols:(sl + 1) * cols, 2 * cols:3 * cols]
        dq_ref[:, sl * cols:(sl + 1) * cols] = jnp.dot(
            low_q, upq, preferred_element_type=jnp.float32).astype(jnp.bfloat16)
        upv = got_ref[sl * cols:(sl + 1) * cols, 3 * cols:3 * cols + 64]
        pieces.append(jnp.dot(low_v, upv, preferred_element_type=jnp.float32))
    for c in range(slices // 2):
        dv_ref[:, c * 128:(c + 1) * 128] = jnp.concatenate(
            [pieces[2 * c], pieces[2 * c + 1]], axis=1).astype(jnp.bfloat16)

    cos = aux_ref[:, 0:128]
    sin = aux_ref[:, 128:256]

    def q_col(c, carry2):
        c0 = pl.multiple_of(c * 128, 128)
        x = qb_ref[:, pl.ds(c0, 128)] + dq_ref[:, pl.ds(c0, 128)].astype(jnp.float32)
        q_s[:, pl.ds(c0, 128)] = (x * cos + _swap_halves(x) * sin).astype(jnp.bfloat16)
        return carry2

    lax.fori_loop(0, q_chunks, q_col, 0, unroll=True)
    zeros = jnp.zeros((blk, 64), jnp.float32)
    for c in range(k_chunks):
        x = kb_ref[:, c * 128:(c + 1) * 128]
        k = (x * cos + _swap_halves(x) * sin).astype(jnp.bfloat16).astype(jnp.float32)
        v = vb_ref[:, c * 128:(c + 1) * 128] + dv_ref[:, c * 128:(c + 1) * 128].astype(jnp.float32)
        v = v.astype(jnp.bfloat16).astype(jnp.float32)
        for half in range(2):
            g = 2 * c + half
            kg = k[:, half * 64:(half + 1) * 64]
            vg = v[:, half * 64:(half + 1) * 64]
            kd_s[g, :, pl.ds(g0, blk)] = jnp.transpose(jnp.concatenate([kg, kg], axis=1)).astype(jnp.bfloat16)
            vd_s[g, pl.ds(g0, blk), 0:128] = jnp.concatenate([vg, zeros], axis=1).astype(jnp.bfloat16)
            vd_s[g, pl.ds(g0, blk), 128:256] = jnp.concatenate([zeros, vg], axis=1).astype(jnp.bfloat16)

    window = 2 * blk
    per_group = HEADS // KV_HEADS
    ws = pl.multiple_of(jnp.clip(g0 - blk, 0, rows - window), blk)
    qpos = aux_ref[:, 256:257].astype(jnp.int32)
    qidx = g0 + lax.broadcasted_iota(jnp.int32, (blk, 1), 0)
    kidx = ws + lax.broadcasted_iota(jnp.int32, (1, window), 1)
    allowed = (kidx >= qidx - qpos) & (kidx <= qidx)

    def head_pair(j, carry2):
        g = j // (per_group // 2)
        c0 = pl.multiple_of(j * 128, 128)
        qc = q_s[:, pl.ds(c0, 128)]
        kd = kd_s[g, :, pl.ds(ws, window)]
        vd = vd_s[g, pl.ds(ws, window), :]
        zero = jnp.zeros_like(qc)
        probs, totals = [], []
        for half in range(2):
            keep = (lane < 64) if half == 0 else (lane >= 64)
            qh = jnp.where(keep, qc, zero)
            s = jnp.dot(qh, kd, preferred_element_type=jnp.float32) * (HEAD_DIM ** -0.5)
            s = jnp.where(allowed, s, -jnp.inf)
            m = jnp.max(s, axis=1, keepdims=True)
            p = jnp.exp(s - m)
            totals.append(jnp.sum(p, axis=1, keepdims=True))
            probs.append(p.astype(jnp.bfloat16))
        o = (jnp.dot(probs[0], vd[:, 0:128], preferred_element_type=jnp.float32)
             + jnp.dot(probs[1], vd[:, 128:256], preferred_element_type=jnp.float32))
        o = o * jnp.where(lane < 64, 1.0 / totals[0], 1.0 / totals[1])
        out_ref[:, pl.ds(c0, 128)] = o.astype(out_ref.dtype)
        return carry2

    lax.fori_loop(0, HEADS // 2, head_pair, 0, unroll=True)


def rope_tables(positions):
    half_dim = HEAD_DIM // 2
    frequency = 500000.0 ** (-(jnp.arange(half_dim).astype(jnp.float32) * 2.0 / HEAD_DIM))
    angles = positions.astype(jnp.float32)[:, None] * frequency[None, :]
    cos = jnp.cos(angles)
    sin = jnp.sin(angles)
    cos_t = jnp.concatenate([cos, cos, cos, cos], axis=1)
    sin_t = jnp.concatenate([-sin, sin, -sin, sin], axis=1)
    return cos_t, sin_t


def fused_attention(q_base, k_base, v_base, states, got, owner_token, positions):
    rows = q_base.shape[0]
    cos_t, sin_t = rope_tables(positions)
    side = jnp.zeros((rows, 128), jnp.float32)
    side = side.at[:, 0].set(positions.astype(jnp.float32)).at[:, 1].set(owner_token.astype(jnp.float32))
    aux = jnp.concatenate([cos_t, sin_t, side], axis=1)
    qkv = jnp.concatenate([q_base, k_base, v_base], axis=1)
    flops = 2 * rows * 256 * 64 * 2 * HEADS * 2 + 2 * rows * 256 * (2 * 2048 + 2048 + 512)
    blk = 128
    row_block = lambda width: pl.BlockSpec((blk, width), lambda b: (b, 0))
    return pl.pallas_call(
        _attend_kernel,
        out_shape=jax.ShapeDtypeStruct((rows, HEADS * HEAD_DIM), jnp.bfloat16),
        grid=(rows // blk,),
        in_specs=[
            row_block(qkv.shape[1]),
            row_block(states.shape[1]),
            pl.BlockSpec(got.shape, lambda b: (0, 0)),
            row_block(aux.shape[1]),
        ],
        out_specs=row_block(HEADS * HEAD_DIM),
        scratch_shapes=[
            pltpu.VMEM((blk, HEADS * HEAD_DIM), jnp.bfloat16),
            pltpu.VMEM((KV_HEADS, 128, rows), jnp.bfloat16),
            pltpu.VMEM((KV_HEADS, rows, 256), jnp.bfloat16),
            pltpu.VMEM((blk, HEADS * HEAD_DIM), jnp.bfloat16),
            pltpu.VMEM((blk, KV_HEADS * HEAD_DIM), jnp.bfloat16),
            pltpu.VMEM((states.shape[1] // 256, 256, 512), jnp.bfloat16),
        ],
        compiler_params=pltpu.CompilerParams(
            dimension_semantics=("arbitrary",), vmem_limit_bytes=48 * 1024 * 1024
        ),
        cost_estimate=pl.CostEstimate(flops=flops, transcendentals=rows * 256 * HEADS,
                                      bytes_accessed=rows * (2048 * 8 + 512 * 8 + 256 * 4) + got.size * 2),
    )(qkv, states, got, aux)


def solution(mesh):
    return jax.shard_map(
        local,
        mesh=mesh,
        in_specs=(
            P(("serve", "store"), None),
            P(),
            P(),
            P(),
            P("store", None, "serve"),
            P("store", None, "serve"),
            P("store", None, "serve"),
            P(),
            P(("serve", "store"), None),
            P(("serve", "store"), None),
        ),
        out_specs=P(("serve", "store"), None),
        check_vma=False,
    )
```

```python
import jax
import jax.numpy as jnp
from jax import lax
from jax.experimental import pallas as pl
from jax.experimental.pallas import tpu as pltpu
from jax.sharding import PartitionSpec as P

HEADS = 32
KV_HEADS = 8
HEAD_DIM = 64
ADAPTER_RANK = 16
ADP_DEV = 32
LEN_MAX = 64


def rotary(heads_in, positions):
    half_dim = HEAD_DIM // 2
    frequency = 500000.0 ** (-(jnp.arange(half_dim).astype(jnp.float32) * 2.0 / HEAD_DIM))
    angles = positions.astype(jnp.float32)[:, None] * frequency[None, :]
    cosine_table = jnp.cos(angles)[:, None, :]
    sine_table = jnp.sin(angles)[:, None, :]
    first_half = heads_in[..., :half_dim]
    second_half = heads_in[..., half_dim:]
    return jnp.concatenate(
        [
            first_half * cosine_table - second_half * sine_table,
            second_half * cosine_table + first_half * sine_table,
        ],
        axis=-1,
    )


def table_lookup(table, wanted):
    entries = jnp.arange(table.shape[0], dtype=jnp.int32)
    return jnp.sum(jnp.where(wanted[..., None] == entries, table, 0), axis=-1)


def reduced_rank_products(block_list, down_panels, up_query, up_value):
    low = jnp.einsum(
        "jkd,jrd->jkr", block_list, down_panels, preferred_element_type=jnp.float32
    ).astype(jnp.bfloat16)
    query_update = jnp.einsum(
        "jkr,jrd->jkd", low[..., :ADAPTER_RANK], up_query, preferred_element_type=jnp.float32
    ).astype(jnp.bfloat16)
    value_update = jnp.einsum(
        "jkr,jrd->jkd", low[..., ADAPTER_RANK:], up_value, preferred_element_type=jnp.float32
    ).astype(jnp.bfloat16)
    return (query_update, value_update)


def local_choice(panel_set, lists, adapter_panel_slot, my_store):
    source_slots = table_lookup(adapter_panel_slot, lists)
    mine_mask = source_slots // ADP_DEV == my_store
    local_source = jnp.sum(jnp.where(mine_mask, source_slots % ADP_DEV, 0), axis=1)
    return tuple((jnp.take(panel, local_source, axis=0) for panel in panel_set))


def attention(query_rot, key_rot, value_rows, request_ids):
    tok_rows = query_rot.shape[0]
    per_group = HEADS // KV_HEADS
    block_rows = min(128, tok_rows)
    reach = LEN_MAX
    key_pad = jnp.concatenate(
        [jnp.zeros((reach,) + key_rot.shape[1:], key_rot.dtype), key_rot], axis=0
    )
    value_pad = jnp.concatenate(
        [jnp.zeros((reach,) + value_rows.shape[1:], value_rows.dtype), value_rows], axis=0
    )
    ids_pad = jnp.concatenate([jnp.full((reach,), -1, jnp.int32), request_ids], axis=0)
    token_order = jnp.arange(tok_rows, dtype=jnp.int32)
    order_pad = jnp.concatenate([jnp.full((reach,), -1, jnp.int32), token_order], axis=0)
    outputs = []
    for block_index in range(tok_rows // block_rows):
        first = block_index * block_rows
        query_block = query_rot[first : first + block_rows]
        query_ids = request_ids[first : first + block_rows]
        query_order = token_order[first : first + block_rows]
        key_block = key_pad[first : first + reach + block_rows]
        value_block = value_pad[first : first + reach + block_rows]
        key_ids = ids_pad[first : first + reach + block_rows]
        key_order = order_pad[first : first + reach + block_rows]
        allowed = (query_ids[:, None] == key_ids[None, :]) & (
            key_order[None, :] <= query_order[:, None]
        )
        pieces = []
        for group_index in range(KV_HEADS):
            query_part = query_block[:, group_index * per_group : (group_index + 1) * per_group, :]
            key_part = key_block[:, group_index, :]
            value_part = value_block[:, group_index, :]
            scores = jnp.einsum(
                "qhd,kd->hqk", query_part, key_part, preferred_element_type=jnp.float32
            ) * HEAD_DIM ** (-0.5)
            scores = jnp.where(allowed[None], scores, -jnp.inf)
            row_max = jnp.max(scores, axis=-1, keepdims=True)
            raised = jnp.exp(scores - row_max)
            row_total = jnp.sum(raised, axis=-1)
            weights = raised.astype(jnp.bfloat16)
            mixed_heads = (
                jnp.einsum("hqk,kd->qhd", weights, value_part, preferred_element_type=jnp.float32)
                / jnp.transpose(row_total)[:, :, None]
            )
            pieces.append(mixed_heads)
        outputs.append(
            jnp.concatenate(pieces, axis=1)
            .reshape(block_rows, HEADS * HEAD_DIM)
            .astype(jnp.bfloat16)
        )
    return jnp.concatenate(outputs, axis=0)


def local(
    normalized_hidden_states,
    query_weight_matrix,
    key_weight_matrix,
    value_weight_matrix,
    adapter_down_weight,
    adapter_up_query_weight,
    adapter_up_value_weight,
    adapter_panel_slot,
    adapter_per_request,
    request_token_length,
):
    axes = ("serve", "store")
    serve_count = lax.axis_size("serve")
    store_count = lax.axis_size("store")
    my_store = lax.axis_index("store")
    tok_rows, width = normalized_hidden_states.shape
    request_count = request_token_length.shape[1]
    adp_dev, rank2, cols = adapter_down_weight.shape
    vcols = adapter_up_value_weight.shape[2]
    device_total = serve_count * store_count
    panel_table = jnp.concatenate(
        [
            adapter_down_weight[:, :ADAPTER_RANK],
            adapter_down_weight[:, ADAPTER_RANK:],
            adapter_up_query_weight,
            adapter_up_value_weight,
        ],
        axis=2,
    )
    my_slots = table_lookup(adapter_panel_slot, adapter_per_request[0])
    slot_for_owner = jnp.sum(
        jnp.where(
            my_slots[None, :] // ADP_DEV == jnp.arange(store_count, dtype=jnp.int32)[:, None],
            my_slots[None, :] % ADP_DEV,
            0,
        ),
        axis=1,
    )
    local_pick = lax.all_to_all(
        jnp.tile(slot_for_owner, serve_count).reshape(device_total, 1), axes, 0, 0, tiled=True
    ).reshape(device_total)
    send = jnp.take(panel_table, local_pick, axis=0, mode="clip")
    got = lax.all_to_all(send, axes, 0, 0, tiled=True)

    lengths = request_token_length[0]
    adapters = adapter_per_request[0]
    request_ends = jnp.cumsum(lengths)
    starts = request_ends - lengths
    token_order = jnp.arange(tok_rows, dtype=jnp.int32)
    request_ids = jnp.sum((token_order[:, None] >= request_ends[None, :]).astype(jnp.int32), axis=1)
    member = request_ids[:, None] == jnp.arange(request_count, dtype=jnp.int32)[None, :]
    positions = token_order - jnp.sum(jnp.where(member, starts[None, :], 0), axis=1)
    owners = table_lookup(adapter_panel_slot, adapters) // ADP_DEV
    owner_token = jnp.sum(jnp.where(member, owners[None, :], 0), axis=1)

    q_base = jnp.dot(
        normalized_hidden_states, query_weight_matrix, preferred_element_type=jnp.float32
    )
    k_base = jnp.dot(
        normalized_hidden_states, key_weight_matrix, preferred_element_type=jnp.float32
    )
    v_base = jnp.dot(
        normalized_hidden_states, value_weight_matrix, preferred_element_type=jnp.float32
    )
    return fused_attention(
        q_base, k_base, v_base, normalized_hidden_states,
        got.reshape(-1, got.shape[-1]), owner_token, positions,
    )


def _swap_halves(x):
    return jnp.concatenate([x[:, 32:64], x[:, 0:32], x[:, 96:128], x[:, 64:96]], axis=1)


def _attend_kernel(qkv_ref, got_ref, aux_ref, out_ref, q_s, kd_s, vd_s, dq_ref, dv_ref, dt_s):
    q_width = dq_ref.shape[1]
    kv_width = dv_ref.shape[1]
    qb_ref = qkv_ref.at[:, 0:q_width]
    kb_ref = qkv_ref.at[:, q_width:q_width + kv_width]
    vb_ref = qkv_ref.at[:, q_width + kv_width:q_width + 2 * kv_width]
    x_ref = qkv_ref.at[:, q_width + 2 * kv_width:]
    blk = qb_ref.shape[0]
    rows = kd_s.shape[2]
    b = pl.program_id(0)
    g0 = pl.multiple_of(b * blk, blk)
    cols = 256
    slices = x_ref.shape[1] // cols
    q_chunks = qb_ref.shape[1] // 128
    k_chunks = kb_ref.shape[1] // 128
    lane = lax.broadcasted_iota(jnp.int32, (1, 128), 1)
    owner_lane = lax.broadcasted_iota(jnp.int32, (1, cols), 1) // 16

    @pl.when(b == 0)
    def _():
        for sl in range(slices):
            panel = got_ref[sl * cols:(sl + 1) * cols, 0:2 * cols].astype(jnp.float32)
            dt_s[sl, :, 0:cols] = jnp.transpose(panel[:, 0:cols]).astype(jnp.bfloat16)
            dt_s[sl, :, cols:2 * cols] = jnp.transpose(panel[:, cols:2 * cols]).astype(jnp.bfloat16)
        kd_s[:, :, blk:2 * blk] = jnp.zeros((kd_s.shape[0], kd_s.shape[1], blk), kd_s.dtype)
        vd_s[:, blk:2 * blk, :] = jnp.zeros((vd_s.shape[0], blk, vd_s.shape[2]), vd_s.dtype)

    low = jnp.zeros((blk, 2 * cols), jnp.float32)
    nt = (((1,), (1,)), ((), ()))
    for sl in range(slices):
        low += jnp.dot(x_ref[:, sl * cols:(sl + 1) * cols].astype(jnp.bfloat16), dt_s[sl],
                       preferred_element_type=jnp.float32)
    low_q = low[:, 0:cols]
    low_v = low[:, cols:2 * cols]
    mine = owner_lane == aux_ref[:, 257:258].astype(jnp.int32)
    low_q = jnp.where(mine, low_q.astype(jnp.bfloat16), jnp.zeros((), jnp.bfloat16))
    low_v = jnp.where(mine, low_v.astype(jnp.bfloat16), jnp.zeros((), jnp.bfloat16))
    pieces = []
    for sl in range(slices):
        upq = got_ref[sl * cols:(sl + 1) * cols, 2 * cols:3 * cols]
        dq_ref[:, sl * cols:(sl + 1) * cols] = jnp.dot(
            low_q, upq, preferred_element_type=jnp.float32).astype(jnp.bfloat16)
        upv = got_ref[sl * cols:(sl + 1) * cols, 3 * cols:3 * cols + 64]
        pieces.append(jnp.dot(low_v, upv, preferred_element_type=jnp.float32))
    for c in range(slices // 2):
        dv_ref[:, c * 128:(c + 1) * 128] = jnp.concatenate(
            [pieces[2 * c], pieces[2 * c + 1]], axis=1).astype(jnp.bfloat16)

    cos = aux_ref[:, 0:128]
    sin = aux_ref[:, 128:256]

    def q_col(c, carry2):
        c0 = pl.multiple_of(c * 128, 128)
        x = qb_ref[:, pl.ds(c0, 128)] + dq_ref[:, pl.ds(c0, 128)].astype(jnp.float32)
        q_s[:, pl.ds(c0, 128)] = (x * cos + _swap_halves(x) * sin).astype(jnp.bfloat16)
        return carry2

    lax.fori_loop(0, q_chunks, q_col, 0, unroll=True)
    zeros = jnp.zeros((blk, 64), jnp.float32)
    for c in range(k_chunks):
        x = kb_ref[:, c * 128:(c + 1) * 128]
        k = (x * cos + _swap_halves(x) * sin).astype(jnp.bfloat16).astype(jnp.float32)
        v = vb_ref[:, c * 128:(c + 1) * 128] + dv_ref[:, c * 128:(c + 1) * 128].astype(jnp.float32)
        v = v.astype(jnp.bfloat16).astype(jnp.float32)
        for half in range(2):
            g = 2 * c + half
            kg = k[:, half * 64:(half + 1) * 64]
            vg = v[:, half * 64:(half + 1) * 64]
            kd_s[g, :, pl.ds(g0, blk)] = jnp.transpose(jnp.concatenate([kg, kg], axis=1)).astype(jnp.bfloat16)
            vd_s[g, pl.ds(g0, blk), 0:128] = jnp.concatenate([vg, zeros], axis=1).astype(jnp.bfloat16)
            vd_s[g, pl.ds(g0, blk), 128:256] = jnp.concatenate([zeros, vg], axis=1).astype(jnp.bfloat16)

    window = 2 * blk
    per_group = HEADS // KV_HEADS
    ws = pl.multiple_of(jnp.clip(g0 - blk, 0, rows - window), blk)
    qpos = aux_ref[:, 256:257].astype(jnp.int32)
    qidx = g0 + lax.broadcasted_iota(jnp.int32, (blk, 1), 0)
    kidx = ws + lax.broadcasted_iota(jnp.int32, (1, window), 1)
    allowed = (kidx >= qidx - qpos) & (kidx <= qidx)

    def head_pair(j, carry2):
        g = j // (per_group // 2)
        c0 = pl.multiple_of(j * 128, 128)
        qc = q_s[:, pl.ds(c0, 128)]
        kd = kd_s[g, :, pl.ds(ws, window)]
        vd = vd_s[g, pl.ds(ws, window), :]
        zero = jnp.zeros_like(qc)
        probs, totals = [], []
        for half in range(2):
            keep = (lane < 64) if half == 0 else (lane >= 64)
            qh = jnp.where(keep, qc, zero)
            s = jnp.dot(qh, kd, preferred_element_type=jnp.float32) * (HEAD_DIM ** -0.5)
            s = jnp.where(allowed, s, -jnp.inf)
            m = jnp.max(s, axis=1, keepdims=True)
            p = jnp.exp(s - m)
            totals.append(jnp.sum(p, axis=1, keepdims=True))
            probs.append(p.astype(jnp.bfloat16))
        o = (jnp.dot(probs[0], vd[:, 0:128], preferred_element_type=jnp.float32)
             + jnp.dot(probs[1], vd[:, 128:256], preferred_element_type=jnp.float32))
        o = o * jnp.where(lane < 64, 1.0 / totals[0], 1.0 / totals[1])
        out_ref[:, pl.ds(c0, 128)] = o.astype(out_ref.dtype)
        return carry2

    lax.fori_loop(0, HEADS // 2, head_pair, 0, unroll=True)


def rope_tables(positions):
    half_dim = HEAD_DIM // 2
    frequency = 500000.0 ** (-(jnp.arange(half_dim).astype(jnp.float32) * 2.0 / HEAD_DIM))
    angles = positions.astype(jnp.float32)[:, None] * frequency[None, :]
    cos = jnp.cos(angles)
    sin = jnp.sin(angles)
    cos_t = jnp.concatenate([cos, cos, cos, cos], axis=1)
    sin_t = jnp.concatenate([-sin, sin, -sin, sin], axis=1)
    return cos_t, sin_t


def fused_attention(q_base, k_base, v_base, states, got, owner_token, positions):
    rows = q_base.shape[0]
    cos_t, sin_t = rope_tables(positions)
    side = jnp.zeros((rows, 128), jnp.float32)
    side = side.at[:, 0].set(positions.astype(jnp.float32)).at[:, 1].set(owner_token.astype(jnp.float32))
    aux = jnp.concatenate([cos_t, sin_t, side], axis=1)
    qkv = jnp.concatenate([q_base, k_base, v_base, states.astype(jnp.float32)], axis=1)
    flops = 2 * rows * 256 * 64 * 2 * HEADS * 2 + 2 * rows * 256 * (2 * 2048 + 2048 + 512)
    blk = 128
    row_block = lambda width: pl.BlockSpec((blk, width), lambda b: (b, 0))
    return pl.pallas_call(
        _attend_kernel,
        out_shape=jax.ShapeDtypeStruct((rows, HEADS * HEAD_DIM), jnp.bfloat16),
        grid=(rows // blk,),
        in_specs=[
            row_block(qkv.shape[1]),
            pl.BlockSpec(got.shape, lambda b: (0, 0)),
            row_block(aux.shape[1]),
        ],
        out_specs=row_block(HEADS * HEAD_DIM),
        scratch_shapes=[
            pltpu.VMEM((blk, HEADS * HEAD_DIM), jnp.bfloat16),
            pltpu.VMEM((KV_HEADS, 128, rows), jnp.bfloat16),
            pltpu.VMEM((KV_HEADS, rows, 256), jnp.bfloat16),
            pltpu.VMEM((blk, HEADS * HEAD_DIM), jnp.bfloat16),
            pltpu.VMEM((blk, KV_HEADS * HEAD_DIM), jnp.bfloat16),
            pltpu.VMEM((states.shape[1] // 256, 256, 512), jnp.bfloat16),
        ],
        compiler_params=pltpu.CompilerParams(
            dimension_semantics=("arbitrary",), vmem_limit_bytes=48 * 1024 * 1024
        ),
        cost_estimate=pl.CostEstimate(flops=flops, transcendentals=rows * 256 * HEADS,
                                      bytes_accessed=rows * (2048 * 8 + 512 * 8 + 256 * 4) + got.size * 2),
    )(qkv, got, aux)


def solution(mesh):
    return jax.shard_map(
        local,
        mesh=mesh,
        in_specs=(
            P(("serve", "store"), None),
            P(),
            P(),
            P(),
            P("store", None, "serve"),
            P("store", None, "serve"),
            P("store", None, "serve"),
            P(),
            P(("serve", "store"), None),
            P(("serve", "store"), None),
        ),
        out_specs=P(("serve", "store"), None),
        check_vma=False,
    )
```

```python
import jax
import jax.numpy as jnp
from jax import lax
from jax.experimental import pallas as pl
from jax.experimental.pallas import tpu as pltpu
from jax.sharding import PartitionSpec as P

HEADS = 32
KV_HEADS = 8
HEAD_DIM = 64
ADAPTER_RANK = 16
ADP_DEV = 32
LEN_MAX = 64


def rotary(heads_in, positions):
    half_dim = HEAD_DIM // 2
    frequency = 500000.0 ** (-(jnp.arange(half_dim).astype(jnp.float32) * 2.0 / HEAD_DIM))
    angles = positions.astype(jnp.float32)[:, None] * frequency[None, :]
    cosine_table = jnp.cos(angles)[:, None, :]
    sine_table = jnp.sin(angles)[:, None, :]
    first_half = heads_in[..., :half_dim]
    second_half = heads_in[..., half_dim:]
    return jnp.concatenate(
        [
            first_half * cosine_table - second_half * sine_table,
            second_half * cosine_table + first_half * sine_table,
        ],
        axis=-1,
    )


def table_lookup(table, wanted):
    entries = jnp.arange(table.shape[0], dtype=jnp.int32)
    return jnp.sum(jnp.where(wanted[..., None] == entries, table, 0), axis=-1)


def reduced_rank_products(block_list, down_panels, up_query, up_value):
    low = jnp.einsum(
        "jkd,jrd->jkr", block_list, down_panels, preferred_element_type=jnp.float32
    ).astype(jnp.bfloat16)
    query_update = jnp.einsum(
        "jkr,jrd->jkd", low[..., :ADAPTER_RANK], up_query, preferred_element_type=jnp.float32
    ).astype(jnp.bfloat16)
    value_update = jnp.einsum(
        "jkr,jrd->jkd", low[..., ADAPTER_RANK:], up_value, preferred_element_type=jnp.float32
    ).astype(jnp.bfloat16)
    return (query_update, value_update)


def local_choice(panel_set, lists, adapter_panel_slot, my_store):
    source_slots = table_lookup(adapter_panel_slot, lists)
    mine_mask = source_slots // ADP_DEV == my_store
    local_source = jnp.sum(jnp.where(mine_mask, source_slots % ADP_DEV, 0), axis=1)
    return tuple((jnp.take(panel, local_source, axis=0) for panel in panel_set))


def attention(query_rot, key_rot, value_rows, request_ids):
    tok_rows = query_rot.shape[0]
    per_group = HEADS // KV_HEADS
    block_rows = min(128, tok_rows)
    reach = LEN_MAX
    key_pad = jnp.concatenate(
        [jnp.zeros((reach,) + key_rot.shape[1:], key_rot.dtype), key_rot], axis=0
    )
    value_pad = jnp.concatenate(
        [jnp.zeros((reach,) + value_rows.shape[1:], value_rows.dtype), value_rows], axis=0
    )
    ids_pad = jnp.concatenate([jnp.full((reach,), -1, jnp.int32), request_ids], axis=0)
    token_order = jnp.arange(tok_rows, dtype=jnp.int32)
    order_pad = jnp.concatenate([jnp.full((reach,), -1, jnp.int32), token_order], axis=0)
    outputs = []
    for block_index in range(tok_rows // block_rows):
        first = block_index * block_rows
        query_block = query_rot[first : first + block_rows]
        query_ids = request_ids[first : first + block_rows]
        query_order = token_order[first : first + block_rows]
        key_block = key_pad[first : first + reach + block_rows]
        value_block = value_pad[first : first + reach + block_rows]
        key_ids = ids_pad[first : first + reach + block_rows]
        key_order = order_pad[first : first + reach + block_rows]
        allowed = (query_ids[:, None] == key_ids[None, :]) & (
            key_order[None, :] <= query_order[:, None]
        )
        pieces = []
        for group_index in range(KV_HEADS):
            query_part = query_block[:, group_index * per_group : (group_index + 1) * per_group, :]
            key_part = key_block[:, group_index, :]
            value_part = value_block[:, group_index, :]
            scores = jnp.einsum(
                "qhd,kd->hqk", query_part, key_part, preferred_element_type=jnp.float32
            ) * HEAD_DIM ** (-0.5)
            scores = jnp.where(allowed[None], scores, -jnp.inf)
            row_max = jnp.max(scores, axis=-1, keepdims=True)
            raised = jnp.exp(scores - row_max)
            row_total = jnp.sum(raised, axis=-1)
            weights = raised.astype(jnp.bfloat16)
            mixed_heads = (
                jnp.einsum("hqk,kd->qhd", weights, value_part, preferred_element_type=jnp.float32)
                / jnp.transpose(row_total)[:, :, None]
            )
            pieces.append(mixed_heads)
        outputs.append(
            jnp.concatenate(pieces, axis=1)
            .reshape(block_rows, HEADS * HEAD_DIM)
            .astype(jnp.bfloat16)
        )
    return jnp.concatenate(outputs, axis=0)


def local(
    normalized_hidden_states,
    query_weight_matrix,
    key_weight_matrix,
    value_weight_matrix,
    adapter_down_weight,
    adapter_up_query_weight,
    adapter_up_value_weight,
    adapter_panel_slot,
    adapter_per_request,
    request_token_length,
):
    axes = ("serve", "store")
    serve_count = lax.axis_size("serve")
    store_count = lax.axis_size("store")
    my_store = lax.axis_index("store")
    tok_rows, width = normalized_hidden_states.shape
    request_count = request_token_length.shape[1]
    adp_dev, rank2, cols = adapter_down_weight.shape
    vcols = adapter_up_value_weight.shape[2]
    device_total = serve_count * store_count
    panel_table = jnp.concatenate(
        [
            adapter_down_weight[:, :ADAPTER_RANK],
            adapter_down_weight[:, ADAPTER_RANK:],
            adapter_up_query_weight,
            adapter_up_value_weight,
        ],
        axis=2,
    )
    my_slots = table_lookup(adapter_panel_slot, adapter_per_request[0])
    slot_for_owner = jnp.sum(
        jnp.where(
            my_slots[None, :] // ADP_DEV == jnp.arange(store_count, dtype=jnp.int32)[:, None],
            my_slots[None, :] % ADP_DEV,
            0,
        ),
        axis=1,
    )
    local_pick = lax.all_to_all(
        jnp.tile(slot_for_owner, serve_count).reshape(device_total, 1), axes, 0, 0, tiled=True
    ).reshape(device_total)
    send = jnp.take(panel_table, local_pick, axis=0, mode="clip")
    got = lax.all_to_all(send, axes, 0, 0, tiled=True)

    lengths = request_token_length[0]
    adapters = adapter_per_request[0]
    request_ends = jnp.cumsum(lengths)
    starts = request_ends - lengths
    token_order = jnp.arange(tok_rows, dtype=jnp.int32)
    request_ids = jnp.sum((token_order[:, None] >= request_ends[None, :]).astype(jnp.int32), axis=1)
    member = request_ids[:, None] == jnp.arange(request_count, dtype=jnp.int32)[None, :]
    positions = token_order - jnp.sum(jnp.where(member, starts[None, :], 0), axis=1)
    owners = table_lookup(adapter_panel_slot, adapters) // ADP_DEV
    owner_token = jnp.sum(jnp.where(member, owners[None, :], 0), axis=1)

    q_base = jnp.dot(
        normalized_hidden_states, query_weight_matrix, preferred_element_type=jnp.float32
    )
    k_base = jnp.dot(
        normalized_hidden_states, key_weight_matrix, preferred_element_type=jnp.float32
    )
    v_base = jnp.dot(
        normalized_hidden_states, value_weight_matrix, preferred_element_type=jnp.float32
    )
    return fused_attention(
        q_base, k_base, v_base, normalized_hidden_states,
        got.reshape(-1, got.shape[-1]), owner_token, positions,
    )


def _swap_halves(x, use_first):
    return jnp.where(use_first, pltpu.roll(x, 32, 1), pltpu.roll(x, 96, 1))


def _attend_kernel(qkv_ref, x_ref, got_ref, aux_ref, out_ref, q_s, kd_s, vd_s, dq_ref, dv_ref, dt_s):
    q_width = dq_ref.shape[1]
    kv_width = dv_ref.shape[1]
    qb_ref = qkv_ref.at[:, 0:q_width]
    kb_ref = qkv_ref.at[:, q_width:q_width + kv_width]
    vb_ref = qkv_ref.at[:, q_width + kv_width:q_width + 2 * kv_width]
    blk = qb_ref.shape[0]
    rows = kd_s.shape[2]
    b = pl.program_id(0)
    g0 = pl.multiple_of(b * blk, blk)
    cols = 256
    slices = x_ref.shape[1] // cols
    q_chunks = qb_ref.shape[1] // 128
    k_chunks = kb_ref.shape[1] // 128
    lane = lax.broadcasted_iota(jnp.int32, (1, 128), 1)
    owner_lane = lax.broadcasted_iota(jnp.int32, (1, cols), 1) // 16

    @pl.when(b == 0)
    def _():
        for sl in range(slices):
            panel = got_ref[sl * cols:(sl + 1) * cols, 0:2 * cols].astype(jnp.float32)
            dt_s[sl, :, 0:cols] = jnp.transpose(panel[:, 0:cols]).astype(jnp.bfloat16)
            dt_s[sl, :, cols:2 * cols] = jnp.transpose(panel[:, cols:2 * cols]).astype(jnp.bfloat16)
        kd_s[:, :, blk:2 * blk] = jnp.zeros((kd_s.shape[0], kd_s.shape[1], blk), kd_s.dtype)
        vd_s[:, blk:2 * blk, :] = jnp.zeros((vd_s.shape[0], blk, vd_s.shape[2]), vd_s.dtype)

    low = jnp.zeros((blk, 2 * cols), jnp.float32)
    nt = (((1,), (1,)), ((), ()))
    for sl in range(slices):
        low += jnp.dot(x_ref[:, sl * cols:(sl + 1) * cols], dt_s[sl], preferred_element_type=jnp.float32)
    low_q = low[:, 0:cols]
    low_v = low[:, cols:2 * cols]
    mine = owner_lane == aux_ref[:, 257:258].astype(jnp.int32)
    low_q = jnp.where(mine, low_q.astype(jnp.bfloat16), jnp.zeros((), jnp.bfloat16))
    low_v = jnp.where(mine, low_v.astype(jnp.bfloat16), jnp.zeros((), jnp.bfloat16))
    pieces = []
    for sl in range(slices):
        upq = got_ref[sl * cols:(sl + 1) * cols, 2 * cols:3 * cols]
        dq_ref[:, sl * cols:(sl + 1) * cols] = jnp.dot(
            low_q, upq, preferred_element_type=jnp.float32).astype(jnp.bfloat16)
        upv = got_ref[sl * cols:(sl + 1) * cols, 3 * cols:3 * cols + 64]
        pieces.append(jnp.dot(low_v, upv, preferred_element_type=jnp.float32))
    for c in range(slices // 2):
        dv_ref[:, c * 128:(c + 1) * 128] = jnp.concatenate(
            [pieces[2 * c], pieces[2 * c + 1]], axis=1).astype(jnp.bfloat16)

    lane_of = lax.broadcasted_iota(jnp.int32, (blk, 128), 1)
    partner = jnp.where(lane_of % 64 < 32, lane_of + 32, lane_of - 32)
    use_first = pltpu.roll(lane_of, 32, 1) == partner
    cos = aux_ref[:, 0:128]
    sin = aux_ref[:, 128:256]

    def q_col(c, carry2):
        c0 = pl.multiple_of(c * 128, 128)
        x = qb_ref[:, pl.ds(c0, 128)] + dq_ref[:, pl.ds(c0, 128)].astype(jnp.float32)
        q_s[:, pl.ds(c0, 128)] = (x * cos + _swap_halves(x, use_first) * sin).astype(jnp.bfloat16)
        return carry2

    lax.fori_loop(0, q_chunks, q_col, 0, unroll=True)
    zeros = jnp.zeros((blk, 64), jnp.float32)
    for c in range(k_chunks):
        x = kb_ref[:, c * 128:(c + 1) * 128]
        k = (x * cos + _swap_halves(x, use_first) * sin).astype(jnp.bfloat16).astype(jnp.float32)
        v = vb_ref[:, c * 128:(c + 1) * 128] + dv_ref[:, c * 128:(c + 1) * 128].astype(jnp.float32)
        v = v.astype(jnp.bfloat16).astype(jnp.float32)
        for half in range(2):
            g = 2 * c + half
            kg = k[:, half * 64:(half + 1) * 64]
            vg = v[:, half * 64:(half + 1) * 64]
            kd_s[g, :, pl.ds(g0, blk)] = jnp.transpose(jnp.concatenate([kg, kg], axis=1)).astype(jnp.bfloat16)
            vd_s[g, pl.ds(g0, blk), 0:128] = jnp.concatenate([vg, zeros], axis=1).astype(jnp.bfloat16)
            vd_s[g, pl.ds(g0, blk), 128:256] = jnp.concatenate([zeros, vg], axis=1).astype(jnp.bfloat16)

    window = 2 * blk
    per_group = HEADS // KV_HEADS
    ws = pl.multiple_of(jnp.clip(g0 - blk, 0, rows - window), blk)
    qpos = aux_ref[:, 256:257].astype(jnp.int32)
    qidx = g0 + lax.broadcasted_iota(jnp.int32, (blk, 1), 0)
    kidx = ws + lax.broadcasted_iota(jnp.int32, (1, window), 1)
    allowed = (kidx >= qidx - qpos) & (kidx <= qidx)

    def head_pair(j, carry2):
        g = j // (per_group // 2)
        c0 = pl.multiple_of(j * 128, 128)
        qc = q_s[:, pl.ds(c0, 128)]
        kd = kd_s[g, :, pl.ds(ws, window)]
        vd = vd_s[g, pl.ds(ws, window), :]
        zero = jnp.zeros_like(qc)
        probs, totals = [], []
        for half in range(2):
            keep = (lane < 64) if half == 0 else (lane >= 64)
            qh = jnp.where(keep, qc, zero)
            s = jnp.dot(qh, kd, preferred_element_type=jnp.float32) * (HEAD_DIM ** -0.5)
            s = jnp.where(allowed, s, -jnp.inf)
            m = jnp.max(s, axis=1, keepdims=True)
            p = jnp.exp(s - m)
            totals.append(jnp.sum(p, axis=1, keepdims=True))
            probs.append(p.astype(jnp.bfloat16))
        o = (jnp.dot(probs[0], vd[:, 0:128], preferred_element_type=jnp.float32)
             + jnp.dot(probs[1], vd[:, 128:256], preferred_element_type=jnp.float32))
        o = o * jnp.where(lane < 64, 1.0 / totals[0], 1.0 / totals[1])
        out_ref[:, pl.ds(c0, 128)] = o.astype(out_ref.dtype)
        return carry2

    lax.fori_loop(0, HEADS // 2, head_pair, 0, unroll=True)


def rope_tables(positions):
    half_dim = HEAD_DIM // 2
    frequency = 500000.0 ** (-(jnp.arange(half_dim).astype(jnp.float32) * 2.0 / HEAD_DIM))
    angles = positions.astype(jnp.float32)[:, None] * frequency[None, :]
    cos = jnp.cos(angles)
    sin = jnp.sin(angles)
    cos_t = jnp.concatenate([cos, cos, cos, cos], axis=1)
    sin_t = jnp.concatenate([-sin, sin, -sin, sin], axis=1)
    return cos_t, sin_t


def fused_attention(q_base, k_base, v_base, states, got, owner_token, positions):
    rows = q_base.shape[0]
    cos_t, sin_t = rope_tables(positions)
    side = jnp.zeros((rows, 128), jnp.float32)
    side = side.at[:, 0].set(positions.astype(jnp.float32)).at[:, 1].set(owner_token.astype(jnp.float32))
    aux = jnp.concatenate([cos_t, sin_t, side], axis=1)
    qkv = jnp.concatenate([q_base, k_base, v_base], axis=1)
    flops = 2 * rows * 256 * 64 * 2 * HEADS * 2 + 2 * rows * 256 * (2 * 2048 + 2048 + 512)
    blk = 128
    row_block = lambda width: pl.BlockSpec((blk, width), lambda b: (b, 0))
    return pl.pallas_call(
        _attend_kernel,
        out_shape=jax.ShapeDtypeStruct((rows, HEADS * HEAD_DIM), jnp.bfloat16),
        grid=(rows // blk,),
        in_specs=[
            row_block(qkv.shape[1]),
            row_block(states.shape[1]),
            pl.BlockSpec(got.shape, lambda b: (0, 0)),
            row_block(aux.shape[1]),
        ],
        out_specs=row_block(HEADS * HEAD_DIM),
        scratch_shapes=[
            pltpu.VMEM((blk, HEADS * HEAD_DIM), jnp.bfloat16),
            pltpu.VMEM((KV_HEADS, 128, rows), jnp.bfloat16),
            pltpu.VMEM((KV_HEADS, rows, 256), jnp.bfloat16),
            pltpu.VMEM((blk, HEADS * HEAD_DIM), jnp.bfloat16),
            pltpu.VMEM((blk, KV_HEADS * HEAD_DIM), jnp.bfloat16),
            pltpu.VMEM((states.shape[1] // 256, 256, 512), jnp.bfloat16),
        ],
        compiler_params=pltpu.CompilerParams(
            dimension_semantics=("arbitrary",), vmem_limit_bytes=48 * 1024 * 1024
        ),
        cost_estimate=pl.CostEstimate(flops=flops, transcendentals=rows * 256 * HEADS,
                                      bytes_accessed=rows * (2048 * 8 + 512 * 8 + 256 * 4) + got.size * 2),
    )(qkv, states, got, aux)


def solution(mesh):
    return jax.shard_map(
        local,
        mesh=mesh,
        in_specs=(
            P(("serve", "store"), None),
            P(),
            P(),
            P(),
            P("store", None, "serve"),
            P("store", None, "serve"),
            P("store", None, "serve"),
            P(),
            P(("serve", "store"), None),
            P(("serve", "store"), None),
        ),
        out_specs=P(("serve", "store"), None),
        check_vma=False,
    )
```

```python
import jax
import jax.numpy as jnp
from jax import lax
from jax.experimental import pallas as pl
from jax.experimental.pallas import tpu as pltpu
from jax.sharding import PartitionSpec as P

HEADS = 32
KV_HEADS = 8
HEAD_DIM = 64
ADAPTER_RANK = 16
ADP_DEV = 32
LEN_MAX = 64


def rotary(heads_in, positions):
    half_dim = HEAD_DIM // 2
    frequency = 500000.0 ** (-(jnp.arange(half_dim).astype(jnp.float32) * 2.0 / HEAD_DIM))
    angles = positions.astype(jnp.float32)[:, None] * frequency[None, :]
    cosine_table = jnp.cos(angles)[:, None, :]
    sine_table = jnp.sin(angles)[:, None, :]
    first_half = heads_in[..., :half_dim]
    second_half = heads_in[..., half_dim:]
    return jnp.concatenate(
        [
            first_half * cosine_table - second_half * sine_table,
            second_half * cosine_table + first_half * sine_table,
        ],
        axis=-1,
    )


def table_lookup(table, wanted):
    entries = jnp.arange(table.shape[0], dtype=jnp.int32)
    return jnp.sum(jnp.where(wanted[..., None] == entries, table, 0), axis=-1)


def reduced_rank_products(block_list, down_panels, up_query, up_value):
    low = jnp.einsum(
        "jkd,jrd->jkr", block_list, down_panels, preferred_element_type=jnp.float32
    ).astype(jnp.bfloat16)
    query_update = jnp.einsum(
        "jkr,jrd->jkd", low[..., :ADAPTER_RANK], up_query, preferred_element_type=jnp.float32
    ).astype(jnp.bfloat16)
    value_update = jnp.einsum(
        "jkr,jrd->jkd", low[..., ADAPTER_RANK:], up_value, preferred_element_type=jnp.float32
    ).astype(jnp.bfloat16)
    return (query_update, value_update)


def local_choice(panel_set, lists, adapter_panel_slot, my_store):
    source_slots = table_lookup(adapter_panel_slot, lists)
    mine_mask = source_slots // ADP_DEV == my_store
    local_source = jnp.sum(jnp.where(mine_mask, source_slots % ADP_DEV, 0), axis=1)
    return tuple((jnp.take(panel, local_source, axis=0) for panel in panel_set))


def attention(query_rot, key_rot, value_rows, request_ids):
    tok_rows = query_rot.shape[0]
    per_group = HEADS // KV_HEADS
    block_rows = min(128, tok_rows)
    reach = LEN_MAX
    key_pad = jnp.concatenate(
        [jnp.zeros((reach,) + key_rot.shape[1:], key_rot.dtype), key_rot], axis=0
    )
    value_pad = jnp.concatenate(
        [jnp.zeros((reach,) + value_rows.shape[1:], value_rows.dtype), value_rows], axis=0
    )
    ids_pad = jnp.concatenate([jnp.full((reach,), -1, jnp.int32), request_ids], axis=0)
    token_order = jnp.arange(tok_rows, dtype=jnp.int32)
    order_pad = jnp.concatenate([jnp.full((reach,), -1, jnp.int32), token_order], axis=0)
    outputs = []
    for block_index in range(tok_rows // block_rows):
        first = block_index * block_rows
        query_block = query_rot[first : first + block_rows]
        query_ids = request_ids[first : first + block_rows]
        query_order = token_order[first : first + block_rows]
        key_block = key_pad[first : first + reach + block_rows]
        value_block = value_pad[first : first + reach + block_rows]
        key_ids = ids_pad[first : first + reach + block_rows]
        key_order = order_pad[first : first + reach + block_rows]
        allowed = (query_ids[:, None] == key_ids[None, :]) & (
            key_order[None, :] <= query_order[:, None]
        )
        pieces = []
        for group_index in range(KV_HEADS):
            query_part = query_block[:, group_index * per_group : (group_index + 1) * per_group, :]
            key_part = key_block[:, group_index, :]
            value_part = value_block[:, group_index, :]
            scores = jnp.einsum(
                "qhd,kd->hqk", query_part, key_part, preferred_element_type=jnp.float32
            ) * HEAD_DIM ** (-0.5)
            scores = jnp.where(allowed[None], scores, -jnp.inf)
            row_max = jnp.max(scores, axis=-1, keepdims=True)
            raised = jnp.exp(scores - row_max)
            row_total = jnp.sum(raised, axis=-1)
            weights = raised.astype(jnp.bfloat16)
            mixed_heads = (
                jnp.einsum("hqk,kd->qhd", weights, value_part, preferred_element_type=jnp.float32)
                / jnp.transpose(row_total)[:, :, None]
            )
            pieces.append(mixed_heads)
        outputs.append(
            jnp.concatenate(pieces, axis=1)
            .reshape(block_rows, HEADS * HEAD_DIM)
            .astype(jnp.bfloat16)
        )
    return jnp.concatenate(outputs, axis=0)


def local(
    normalized_hidden_states,
    query_weight_matrix,
    key_weight_matrix,
    value_weight_matrix,
    adapter_down_weight,
    adapter_up_query_weight,
    adapter_up_value_weight,
    adapter_panel_slot,
    adapter_per_request,
    request_token_length,
):
    axes = ("serve", "store")
    serve_count = lax.axis_size("serve")
    store_count = lax.axis_size("store")
    my_store = lax.axis_index("store")
    tok_rows, width = normalized_hidden_states.shape
    request_count = request_token_length.shape[1]
    adp_dev, rank2, cols = adapter_down_weight.shape
    vcols = adapter_up_value_weight.shape[2]
    device_total = serve_count * store_count
    panel_table = jnp.concatenate(
        [
            adapter_down_weight[:, :ADAPTER_RANK],
            adapter_down_weight[:, ADAPTER_RANK:],
            adapter_up_query_weight,
            adapter_up_value_weight,
        ],
        axis=2,
    )
    my_slots = table_lookup(adapter_panel_slot, adapter_per_request[0])
    slot_for_owner = jnp.sum(
        jnp.where(
            my_slots[None, :] // ADP_DEV == jnp.arange(store_count, dtype=jnp.int32)[:, None],
            my_slots[None, :] % ADP_DEV,
            0,
        ),
        axis=1,
    )
    local_pick = lax.all_to_all(
        jnp.tile(slot_for_owner, serve_count).reshape(device_total, 1), axes, 0, 0, tiled=True
    ).reshape(device_total)
    send = jnp.take(panel_table, local_pick, axis=0, mode="clip")
    got = lax.all_to_all(send, axes, 0, 0, tiled=True)

    lengths = request_token_length[0]
    adapters = adapter_per_request[0]
    request_ends = jnp.cumsum(lengths)
    starts = request_ends - lengths
    token_order = jnp.arange(tok_rows, dtype=jnp.int32)
    request_ids = jnp.sum((token_order[:, None] >= request_ends[None, :]).astype(jnp.int32), axis=1)
    member = request_ids[:, None] == jnp.arange(request_count, dtype=jnp.int32)[None, :]
    positions = token_order - jnp.sum(jnp.where(member, starts[None, :], 0), axis=1)
    owners = table_lookup(adapter_panel_slot, adapters) // ADP_DEV
    owner_token = jnp.sum(jnp.where(member, owners[None, :], 0), axis=1)

    q_base = jnp.dot(
        normalized_hidden_states, query_weight_matrix, preferred_element_type=jnp.float32
    )
    k_base = jnp.dot(
        normalized_hidden_states, key_weight_matrix, preferred_element_type=jnp.float32
    )
    v_base = jnp.dot(
        normalized_hidden_states, value_weight_matrix, preferred_element_type=jnp.float32
    )
    return fused_attention(
        q_base, k_base, v_base, normalized_hidden_states,
        got.reshape(-1, got.shape[-1]), owner_token, positions,
    )


def _swap_halves(x):
    return jnp.concatenate([x[:, 32:64], x[:, 0:32], x[:, 96:128], x[:, 64:96]], axis=1)


def _attend_kernel(qkv_ref, x_ref, got_ref, aux_ref, out_ref, q_s, kd_s, vd_s, dq_ref, dv_ref, dt_s):
    q_width = dq_ref.shape[1]
    kv_width = dv_ref.shape[1]
    qb_ref = qkv_ref.at[:, 0:q_width]
    kb_ref = qkv_ref.at[:, q_width:q_width + kv_width]
    vb_ref = qkv_ref.at[:, q_width + kv_width:q_width + 2 * kv_width]
    blk = qb_ref.shape[0]
    rows = kd_s.shape[2]
    b = pl.program_id(0)
    g0 = pl.multiple_of(b * blk, blk)
    cols = 256
    slices = x_ref.shape[1] // cols
    q_chunks = qb_ref.shape[1] // 128
    k_chunks = kb_ref.shape[1] // 128
    lane = lax.broadcasted_iota(jnp.int32, (1, 128), 1)
    owner_lane = lax.broadcasted_iota(jnp.int32, (1, cols), 1) // 16

    @pl.when(b == 0)
    def _():
        for sl in range(slices):
            panel = got_ref[sl * cols:(sl + 1) * cols, 0:2 * cols].astype(jnp.float32)
            dt_s[sl, :, 0:cols] = jnp.transpose(panel[:, 0:cols]).astype(jnp.bfloat16)
            dt_s[sl, :, cols:2 * cols] = jnp.transpose(panel[:, cols:2 * cols]).astype(jnp.bfloat16)
        kd_s[:, :, blk:2 * blk] = jnp.zeros((kd_s.shape[0], kd_s.shape[1], blk), kd_s.dtype)
        vd_s[:, blk:2 * blk, :] = jnp.zeros((vd_s.shape[0], blk, vd_s.shape[2]), vd_s.dtype)

    low = jnp.zeros((blk, 2 * cols), jnp.float32)
    nt = (((1,), (1,)), ((), ()))
    for sl in range(slices):
        low += jnp.dot(x_ref[:, sl * cols:(sl + 1) * cols], dt_s[sl], preferred_element_type=jnp.float32)
    low_q = low[:, 0:cols]
    low_v = low[:, cols:2 * cols]
    mine = owner_lane == aux_ref[:, 257:258].astype(jnp.int32)
    low_q = jnp.where(mine, low_q.astype(jnp.bfloat16), jnp.zeros((), jnp.bfloat16))
    low_v = jnp.where(mine, low_v.astype(jnp.bfloat16), jnp.zeros((), jnp.bfloat16))
    pieces = []
    for sl in range(slices):
        upq = got_ref[sl * cols:(sl + 1) * cols, 2 * cols:3 * cols]
        dq_ref[:, sl * cols:(sl + 1) * cols] = jnp.dot(
            low_q, upq, preferred_element_type=jnp.float32).astype(jnp.bfloat16)
        upv = got_ref[sl * cols:(sl + 1) * cols, 3 * cols:3 * cols + 64]
        pieces.append(jnp.dot(low_v, upv, preferred_element_type=jnp.float32))
    for c in range(slices // 2):
        dv_ref[:, c * 128:(c + 1) * 128] = jnp.concatenate(
            [pieces[2 * c], pieces[2 * c + 1]], axis=1).astype(jnp.bfloat16)

    cos = aux_ref[:, 0:128]
    sin = aux_ref[:, 128:256]

    def q_col(c, carry2):
        c0 = pl.multiple_of(c * 128, 128)
        x = qb_ref[:, pl.ds(c0, 128)] + dq_ref[:, pl.ds(c0, 128)].astype(jnp.float32)
        q_s[:, pl.ds(c0, 128)] = (x * cos + _swap_halves(x) * sin).astype(jnp.bfloat16)
        return carry2

    lax.fori_loop(0, q_chunks, q_col, 0, unroll=True)
    zeros = jnp.zeros((blk, 64), jnp.float32)
    for c in range(k_chunks):
        x = kb_ref[:, c * 128:(c + 1) * 128]
        k = (x * cos + _swap_halves(x) * sin).astype(jnp.bfloat16).astype(jnp.float32)
        v = vb_ref[:, c * 128:(c + 1) * 128] + dv_ref[:, c * 128:(c + 1) * 128].astype(jnp.float32)
        v = v.astype(jnp.bfloat16).astype(jnp.float32)
        for half in range(2):
            g = 2 * c + half
            kg = k[:, half * 64:(half + 1) * 64]
            vg = v[:, half * 64:(half + 1) * 64]
            kd_s[g, :, pl.ds(g0, blk)] = jnp.transpose(jnp.concatenate([kg, kg], axis=1)).astype(jnp.bfloat16)
            vd_s[g, pl.ds(g0, blk), 0:128] = jnp.concatenate([vg, zeros], axis=1).astype(jnp.bfloat16)
            vd_s[g, pl.ds(g0, blk), 128:256] = jnp.concatenate([zeros, vg], axis=1).astype(jnp.bfloat16)

    per_group = HEADS // KV_HEADS
    qpos = aux_ref[:, 256:257].astype(jnp.int32)
    qidx = g0 + lax.broadcasted_iota(jnp.int32, (blk, 1), 0)

    def attend(window, ws):
        kidx = ws + lax.broadcasted_iota(jnp.int32, (1, window), 1)
        allowed = (kidx >= qidx - qpos) & (kidx <= qidx)

        def head_pair(j, carry2):
            g = j // (per_group // 2)
            c0 = pl.multiple_of(j * 128, 128)
            qc = q_s[:, pl.ds(c0, 128)]
            kd = kd_s[g, :, pl.ds(ws, window)]
            vd = vd_s[g, pl.ds(ws, window), :]
            zero = jnp.zeros_like(qc)
            probs, totals = [], []
            for half in range(2):
                keep = (lane < 64) if half == 0 else (lane >= 64)
                qh = jnp.where(keep, qc, zero)
                s = jnp.dot(qh, kd, preferred_element_type=jnp.float32) * (HEAD_DIM ** -0.5)
                s = jnp.where(allowed, s, -jnp.inf)
                m = jnp.max(s, axis=1, keepdims=True)
                p = jnp.exp(s - m)
                totals.append(jnp.sum(p, axis=1, keepdims=True))
                probs.append(p.astype(jnp.bfloat16))
            o = (jnp.dot(probs[0], vd[:, 0:128], preferred_element_type=jnp.float32)
                 + jnp.dot(probs[1], vd[:, 128:256], preferred_element_type=jnp.float32))
            o = o * jnp.where(lane < 64, 1.0 / totals[0], 1.0 / totals[1])
            out_ref[:, pl.ds(c0, 128)] = o.astype(out_ref.dtype)
            return carry2

        lax.fori_loop(0, HEADS // 2, head_pair, 0, unroll=True)

    @pl.when(b == 0)
    def _():
        attend(blk, 0)

    @pl.when(b > 0)
    def _():
        attend(2 * blk, pl.multiple_of(jnp.clip(g0 - blk, 0, rows - 2 * blk), blk))


def rope_tables(positions):
    half_dim = HEAD_DIM // 2
    frequency = 500000.0 ** (-(jnp.arange(half_dim).astype(jnp.float32) * 2.0 / HEAD_DIM))
    angles = positions.astype(jnp.float32)[:, None] * frequency[None, :]
    cos = jnp.cos(angles)
    sin = jnp.sin(angles)
    cos_t = jnp.concatenate([cos, cos, cos, cos], axis=1)
    sin_t = jnp.concatenate([-sin, sin, -sin, sin], axis=1)
    return cos_t, sin_t


def fused_attention(q_base, k_base, v_base, states, got, owner_token, positions):
    rows = q_base.shape[0]
    cos_t, sin_t = rope_tables(positions)
    side = jnp.zeros((rows, 128), jnp.float32)
    side = side.at[:, 0].set(positions.astype(jnp.float32)).at[:, 1].set(owner_token.astype(jnp.float32))
    aux = jnp.concatenate([cos_t, sin_t, side], axis=1)
    qkv = jnp.concatenate([q_base, k_base, v_base], axis=1)
    flops = 2 * rows * 256 * 64 * 2 * HEADS * 2 + 2 * rows * 256 * (2 * 2048 + 2048 + 512)
    blk = 128
    row_block = lambda width: pl.BlockSpec((blk, width), lambda b: (b, 0))
    return pl.pallas_call(
        _attend_kernel,
        out_shape=jax.ShapeDtypeStruct((rows, HEADS * HEAD_DIM), jnp.bfloat16),
        grid=(rows // blk,),
        in_specs=[
            row_block(qkv.shape[1]),
            row_block(states.shape[1]),
            pl.BlockSpec(got.shape, lambda b: (0, 0)),
            row_block(aux.shape[1]),
        ],
        out_specs=row_block(HEADS * HEAD_DIM),
        scratch_shapes=[
            pltpu.VMEM((blk, HEADS * HEAD_DIM), jnp.bfloat16),
            pltpu.VMEM((KV_HEADS, 128, rows), jnp.bfloat16),
            pltpu.VMEM((KV_HEADS, rows, 256), jnp.bfloat16),
            pltpu.VMEM((blk, HEADS * HEAD_DIM), jnp.bfloat16),
            pltpu.VMEM((blk, KV_HEADS * HEAD_DIM), jnp.bfloat16),
            pltpu.VMEM((states.shape[1] // 256, 256, 512), jnp.bfloat16),
        ],
        compiler_params=pltpu.CompilerParams(
            dimension_semantics=("arbitrary",), vmem_limit_bytes=48 * 1024 * 1024,
        ),
        cost_estimate=pl.CostEstimate(flops=flops, transcendentals=rows * 256 * HEADS,
                                      bytes_accessed=rows * (2048 * 8 + 512 * 8 + 256 * 4) + got.size * 2),
    )(qkv, states, got, aux)


def solution(mesh):
    return jax.shard_map(
        local,
        mesh=mesh,
        in_specs=(
            P(("serve", "store"), None),
            P(),
            P(),
            P(),
            P("store", None, "serve"),
            P("store", None, "serve"),
            P("store", None, "serve"),
            P(),
            P(("serve", "store"), None),
            P(("serve", "store"), None),
        ),
        out_specs=P(("serve", "store"), None),
        check_vma=False,
    )
```

```python
import jax
import jax.numpy as jnp
from jax import lax
from jax.experimental import pallas as pl
from jax.experimental.pallas import tpu as pltpu
from jax.sharding import PartitionSpec as P

HEADS = 32
KV_HEADS = 8
HEAD_DIM = 64
ADAPTER_RANK = 16
ADP_DEV = 32
LEN_MAX = 64


def rotary(heads_in, positions):
    half_dim = HEAD_DIM // 2
    frequency = 500000.0 ** (-(jnp.arange(half_dim).astype(jnp.float32) * 2.0 / HEAD_DIM))
    angles = positions.astype(jnp.float32)[:, None] * frequency[None, :]
    cosine_table = jnp.cos(angles)[:, None, :]
    sine_table = jnp.sin(angles)[:, None, :]
    first_half = heads_in[..., :half_dim]
    second_half = heads_in[..., half_dim:]
    return jnp.concatenate(
        [
            first_half * cosine_table - second_half * sine_table,
            second_half * cosine_table + first_half * sine_table,
        ],
        axis=-1,
    )


def table_lookup(table, wanted):
    entries = jnp.arange(table.shape[0], dtype=jnp.int32)
    return jnp.sum(jnp.where(wanted[..., None] == entries, table, 0), axis=-1)


def reduced_rank_products(block_list, down_panels, up_query, up_value):
    low = jnp.einsum(
        "jkd,jrd->jkr", block_list, down_panels, preferred_element_type=jnp.float32
    ).astype(jnp.bfloat16)
    query_update = jnp.einsum(
        "jkr,jrd->jkd", low[..., :ADAPTER_RANK], up_query, preferred_element_type=jnp.float32
    ).astype(jnp.bfloat16)
    value_update = jnp.einsum(
        "jkr,jrd->jkd", low[..., ADAPTER_RANK:], up_value, preferred_element_type=jnp.float32
    ).astype(jnp.bfloat16)
    return (query_update, value_update)


def local_choice(panel_set, lists, adapter_panel_slot, my_store):
    source_slots = table_lookup(adapter_panel_slot, lists)
    mine_mask = source_slots // ADP_DEV == my_store
    local_source = jnp.sum(jnp.where(mine_mask, source_slots % ADP_DEV, 0), axis=1)
    return tuple((jnp.take(panel, local_source, axis=0) for panel in panel_set))


def attention(query_rot, key_rot, value_rows, request_ids):
    tok_rows = query_rot.shape[0]
    per_group = HEADS // KV_HEADS
    block_rows = min(128, tok_rows)
    reach = LEN_MAX
    key_pad = jnp.concatenate(
        [jnp.zeros((reach,) + key_rot.shape[1:], key_rot.dtype), key_rot], axis=0
    )
    value_pad = jnp.concatenate(
        [jnp.zeros((reach,) + value_rows.shape[1:], value_rows.dtype), value_rows], axis=0
    )
    ids_pad = jnp.concatenate([jnp.full((reach,), -1, jnp.int32), request_ids], axis=0)
    token_order = jnp.arange(tok_rows, dtype=jnp.int32)
    order_pad = jnp.concatenate([jnp.full((reach,), -1, jnp.int32), token_order], axis=0)
    outputs = []
    for block_index in range(tok_rows // block_rows):
        first = block_index * block_rows
        query_block = query_rot[first : first + block_rows]
        query_ids = request_ids[first : first + block_rows]
        query_order = token_order[first : first + block_rows]
        key_block = key_pad[first : first + reach + block_rows]
        value_block = value_pad[first : first + reach + block_rows]
        key_ids = ids_pad[first : first + reach + block_rows]
        key_order = order_pad[first : first + reach + block_rows]
        allowed = (query_ids[:, None] == key_ids[None, :]) & (
            key_order[None, :] <= query_order[:, None]
        )
        pieces = []
        for group_index in range(KV_HEADS):
            query_part = query_block[:, group_index * per_group : (group_index + 1) * per_group, :]
            key_part = key_block[:, group_index, :]
            value_part = value_block[:, group_index, :]
            scores = jnp.einsum(
                "qhd,kd->hqk", query_part, key_part, preferred_element_type=jnp.float32
            ) * HEAD_DIM ** (-0.5)
            scores = jnp.where(allowed[None], scores, -jnp.inf)
            row_max = jnp.max(scores, axis=-1, keepdims=True)
            raised = jnp.exp(scores - row_max)
            row_total = jnp.sum(raised, axis=-1)
            weights = raised.astype(jnp.bfloat16)
            mixed_heads = (
                jnp.einsum("hqk,kd->qhd", weights, value_part, preferred_element_type=jnp.float32)
                / jnp.transpose(row_total)[:, :, None]
            )
            pieces.append(mixed_heads)
        outputs.append(
            jnp.concatenate(pieces, axis=1)
            .reshape(block_rows, HEADS * HEAD_DIM)
            .astype(jnp.bfloat16)
        )
    return jnp.concatenate(outputs, axis=0)


def local(
    normalized_hidden_states,
    query_weight_matrix,
    key_weight_matrix,
    value_weight_matrix,
    adapter_down_weight,
    adapter_up_query_weight,
    adapter_up_value_weight,
    adapter_panel_slot,
    adapter_per_request,
    request_token_length,
):
    axes = ("serve", "store")
    serve_count = lax.axis_size("serve")
    store_count = lax.axis_size("store")
    my_store = lax.axis_index("store")
    tok_rows, width = normalized_hidden_states.shape
    request_count = request_token_length.shape[1]
    adp_dev, rank2, cols = adapter_down_weight.shape
    vcols = adapter_up_value_weight.shape[2]
    device_total = serve_count * store_count
    panel_table = jnp.concatenate(
        [
            adapter_down_weight[:, :ADAPTER_RANK],
            adapter_down_weight[:, ADAPTER_RANK:],
            adapter_up_query_weight,
            adapter_up_value_weight,
        ],
        axis=2,
    )
    my_slots = table_lookup(adapter_panel_slot, adapter_per_request[0])
    slot_for_owner = jnp.sum(
        jnp.where(
            my_slots[None, :] // ADP_DEV == jnp.arange(store_count, dtype=jnp.int32)[:, None],
            my_slots[None, :] % ADP_DEV,
            0,
        ),
        axis=1,
    )
    local_pick = lax.all_to_all(
        jnp.tile(slot_for_owner, serve_count).reshape(device_total, 1), axes, 0, 0, tiled=True
    ).reshape(device_total)
    send = jnp.take(panel_table, local_pick, axis=0, mode="clip")
    got = lax.all_to_all(send, axes, 0, 0, tiled=True)

    lengths = request_token_length[0]
    adapters = adapter_per_request[0]
    request_ends = jnp.cumsum(lengths)
    starts = request_ends - lengths
    token_order = jnp.arange(tok_rows, dtype=jnp.int32)
    request_ids = jnp.sum((token_order[:, None] >= request_ends[None, :]).astype(jnp.int32), axis=1)
    member = request_ids[:, None] == jnp.arange(request_count, dtype=jnp.int32)[None, :]
    positions = token_order - jnp.sum(jnp.where(member, starts[None, :], 0), axis=1)
    owners = table_lookup(adapter_panel_slot, adapters) // ADP_DEV
    owner_token = jnp.sum(jnp.where(member, owners[None, :], 0), axis=1)

    q_base = jnp.dot(
        normalized_hidden_states, query_weight_matrix, preferred_element_type=jnp.float32
    )
    k_base = jnp.dot(
        normalized_hidden_states, key_weight_matrix, preferred_element_type=jnp.float32
    )
    v_base = jnp.dot(
        normalized_hidden_states, value_weight_matrix, preferred_element_type=jnp.float32
    )
    return fused_attention(
        q_base, k_base, v_base, normalized_hidden_states,
        got.reshape(-1, got.shape[-1]), owner_token, positions,
    )


def _swap_halves(x):
    return jnp.concatenate([x[:, 32:64], x[:, 0:32], x[:, 96:128], x[:, 64:96]], axis=1)


def _attend_kernel(qkv_ref, x_ref, got_ref, aux_ref, out_ref, q_s, kd_s, vd_s, dq_ref, dv_ref, dt_s):
    q_width = dq_ref.shape[1]
    kv_width = dv_ref.shape[1]
    qb_ref = qkv_ref.at[:, 0:q_width]
    kb_ref = qkv_ref.at[:, q_width:q_width + kv_width]
    vb_ref = qkv_ref.at[:, q_width + kv_width:q_width + 2 * kv_width]
    blk = qb_ref.shape[0]
    rows = kd_s.shape[3]
    b = pl.program_id(0)
    g0 = pl.multiple_of(b * blk, blk)
    cols = 256
    slices = x_ref.shape[1] // cols
    q_chunks = qb_ref.shape[1] // 128
    k_chunks = kb_ref.shape[1] // 128
    lane = lax.broadcasted_iota(jnp.int32, (1, 128), 1)
    owner_lane = lax.broadcasted_iota(jnp.int32, (1, cols), 1) // 16

    @pl.when(b == 0)
    def _():
        for sl in range(slices):
            panel = got_ref[sl * cols:(sl + 1) * cols, 0:2 * cols].astype(jnp.float32)
            dt_s[sl, :, 0:cols] = jnp.transpose(panel[:, 0:cols]).astype(jnp.bfloat16)
            dt_s[sl, :, cols:2 * cols] = jnp.transpose(panel[:, cols:2 * cols]).astype(jnp.bfloat16)
        kd_s[:, :, :, blk:2 * blk] = jnp.zeros(kd_s.shape[:3] + (blk,), kd_s.dtype)
        vd_s[:, blk:2 * blk, :] = jnp.zeros((vd_s.shape[0], blk, vd_s.shape[2]), vd_s.dtype)

    low = jnp.zeros((blk, 2 * cols), jnp.float32)
    nt = (((1,), (1,)), ((), ()))
    for sl in range(slices):
        low += jnp.dot(x_ref[:, sl * cols:(sl + 1) * cols], dt_s[sl], preferred_element_type=jnp.float32)
    low_q = low[:, 0:cols]
    low_v = low[:, cols:2 * cols]
    mine = owner_lane == aux_ref[:, 257:258].astype(jnp.int32)
    low_q = jnp.where(mine, low_q.astype(jnp.bfloat16), jnp.zeros((), jnp.bfloat16))
    low_v = jnp.where(mine, low_v.astype(jnp.bfloat16), jnp.zeros((), jnp.bfloat16))
    pieces = []
    for sl in range(slices):
        upq = got_ref[sl * cols:(sl + 1) * cols, 2 * cols:3 * cols]
        dq_ref[:, sl * cols:(sl + 1) * cols] = jnp.dot(
            low_q, upq, preferred_element_type=jnp.float32).astype(jnp.bfloat16)
        upv = got_ref[sl * cols:(sl + 1) * cols, 3 * cols:3 * cols + 64]
        pieces.append(jnp.dot(low_v, upv, preferred_element_type=jnp.float32))
    for c in range(slices // 2):
        dv_ref[:, c * 128:(c + 1) * 128] = jnp.concatenate(
            [pieces[2 * c], pieces[2 * c + 1]], axis=1).astype(jnp.bfloat16)

    cos = aux_ref[:, 0:128]
    sin = aux_ref[:, 128:256]

    def q_col(c, carry2):
        c0 = pl.multiple_of(c * 128, 128)
        x = qb_ref[:, pl.ds(c0, 128)] + dq_ref[:, pl.ds(c0, 128)].astype(jnp.float32)
        q_s[:, pl.ds(c0, 128)] = (x * cos + _swap_halves(x) * sin).astype(jnp.bfloat16)
        return carry2

    lax.fori_loop(0, q_chunks, q_col, 0, unroll=True)
    zeros = jnp.zeros((blk, 64), jnp.float32)
    for c in range(k_chunks):
        x = kb_ref[:, c * 128:(c + 1) * 128]
        k = (x * cos + _swap_halves(x) * sin).astype(jnp.bfloat16).astype(jnp.float32)
        v = vb_ref[:, c * 128:(c + 1) * 128] + dv_ref[:, c * 128:(c + 1) * 128].astype(jnp.float32)
        v = v.astype(jnp.bfloat16).astype(jnp.float32)
        for half in range(2):
            g = 2 * c + half
            kg = k[:, half * 64:(half + 1) * 64]
            vg = v[:, half * 64:(half + 1) * 64]
            kd_s[g, 0, :, pl.ds(g0, blk)] = jnp.transpose(jnp.concatenate([kg, zeros], axis=1)).astype(jnp.bfloat16)
            kd_s[g, 1, :, pl.ds(g0, blk)] = jnp.transpose(jnp.concatenate([zeros, kg], axis=1)).astype(jnp.bfloat16)
            vd_s[g, pl.ds(g0, blk), 0:128] = jnp.concatenate([vg, zeros], axis=1).astype(jnp.bfloat16)
            vd_s[g, pl.ds(g0, blk), 128:256] = jnp.concatenate([zeros, vg], axis=1).astype(jnp.bfloat16)

    window = 2 * blk
    per_group = HEADS // KV_HEADS
    ws = pl.multiple_of(jnp.clip(g0 - blk, 0, rows - window), blk)
    qpos = aux_ref[:, 256:257].astype(jnp.int32)
    qidx = g0 + lax.broadcasted_iota(jnp.int32, (blk, 1), 0)
    kidx = ws + lax.broadcasted_iota(jnp.int32, (1, window), 1)
    allowed = (kidx >= qidx - qpos) & (kidx <= qidx)

    def head_pair(j, carry2):
        g = j // (per_group // 2)
        c0 = pl.multiple_of(j * 128, 128)
        qc = q_s[:, pl.ds(c0, 128)]
        vd = vd_s[g, pl.ds(ws, window), :]
        probs, totals = [], []
        for half in range(2):
            kd = kd_s[g, half, :, pl.ds(ws, window)]
            s = jnp.dot(qc, kd, preferred_element_type=jnp.float32) * (HEAD_DIM ** -0.5)
            s = jnp.where(allowed, s, -jnp.inf)
            m = jnp.max(s, axis=1, keepdims=True)
            p = jnp.exp(s - m)
            totals.append(jnp.sum(p, axis=1, keepdims=True))
            probs.append(p.astype(jnp.bfloat16))
        o = (jnp.dot(probs[0], vd[:, 0:128], preferred_element_type=jnp.float32)
             + jnp.dot(probs[1], vd[:, 128:256], preferred_element_type=jnp.float32))
        o = o * jnp.where(lane < 64, 1.0 / totals[0], 1.0 / totals[1])
        out_ref[:, pl.ds(c0, 128)] = o.astype(out_ref.dtype)
        return carry2

    lax.fori_loop(0, HEADS // 2, head_pair, 0, unroll=True)


def rope_tables(positions):
    half_dim = HEAD_DIM // 2
    frequency = 500000.0 ** (-(jnp.arange(half_dim).astype(jnp.float32) * 2.0 / HEAD_DIM))
    angles = positions.astype(jnp.float32)[:, None] * frequency[None, :]
    cos = jnp.cos(angles)
    sin = jnp.sin(angles)
    cos_t = jnp.concatenate([cos, cos, cos, cos], axis=1)
    sin_t = jnp.concatenate([-sin, sin, -sin, sin], axis=1)
    return cos_t, sin_t


def fused_attention(q_base, k_base, v_base, states, got, owner_token, positions):
    rows = q_base.shape[0]
    cos_t, sin_t = rope_tables(positions)
    side = jnp.zeros((rows, 128), jnp.float32)
    side = side.at[:, 0].set(positions.astype(jnp.float32)).at[:, 1].set(owner_token.astype(jnp.float32))
    aux = jnp.concatenate([cos_t, sin_t, side], axis=1)
    qkv = jnp.concatenate([q_base, k_base, v_base], axis=1)
    flops = 2 * rows * 256 * 64 * 2 * HEADS * 2 + 2 * rows * 256 * (2 * 2048 + 2048 + 512)
    blk = 128
    row_block = lambda width: pl.BlockSpec((blk, width), lambda b: (b, 0))
    return pl.pallas_call(
        _attend_kernel,
        out_shape=jax.ShapeDtypeStruct((rows, HEADS * HEAD_DIM), jnp.bfloat16),
        grid=(rows // blk,),
        in_specs=[
            row_block(qkv.shape[1]),
            row_block(states.shape[1]),
            pl.BlockSpec(got.shape, lambda b: (0, 0)),
            row_block(aux.shape[1]),
        ],
        out_specs=row_block(HEADS * HEAD_DIM),
        scratch_shapes=[
            pltpu.VMEM((blk, HEADS * HEAD_DIM), jnp.bfloat16),
            pltpu.VMEM((KV_HEADS, 2, 128, rows), jnp.bfloat16),
            pltpu.VMEM((KV_HEADS, rows, 256), jnp.bfloat16),
            pltpu.VMEM((blk, HEADS * HEAD_DIM), jnp.bfloat16),
            pltpu.VMEM((blk, KV_HEADS * HEAD_DIM), jnp.bfloat16),
            pltpu.VMEM((states.shape[1] // 256, 256, 512), jnp.bfloat16),
        ],
        compiler_params=pltpu.CompilerParams(
            dimension_semantics=("arbitrary",), vmem_limit_bytes=48 * 1024 * 1024,
        ),
        cost_estimate=pl.CostEstimate(flops=flops, transcendentals=rows * 256 * HEADS,
                                      bytes_accessed=rows * (2048 * 8 + 512 * 8 + 256 * 4) + got.size * 2),
    )(qkv, states, got, aux)


def solution(mesh):
    return jax.shard_map(
        local,
        mesh=mesh,
        in_specs=(
            P(("serve", "store"), None),
            P(),
            P(),
            P(),
            P("store", None, "serve"),
            P("store", None, "serve"),
            P("store", None, "serve"),
            P(),
            P(("serve", "store"), None),
            P(("serve", "store"), None),
        ),
        out_specs=P(("serve", "store"), None),
        check_vma=False,
    )
```
